256 devices in a mesh: sec: 2 (over y_hi), gx: 16 (over y_lo, z), gy: 8 (over x, core).
Axes of the slice: x: 4, y: 4 (y_hi: 2, y_lo: 2; y = y_hi * 2 + y_lo), z: 8, core: 2. Of those that a mesh axis runs over, the one named last changes fastest.
Arguments:
- ocean_velocity: float32 [2, 8, 1024, 2048], P(None, None, 'gx', ('sec', 'gy')), may hold values from -6 to 6
- wind_stress: float32 [2, 1024, 2048], P(None, 'gx', ('sec', 'gy')), may hold values from -6 to 6
- level_counts: int32 [1024, 2048], P('gx', ('sec', 'gy')), may hold values from 1 to 8
- floe_position: float32 [16, 16, 2, 2048], P('gx', ('sec', 'gy')), may hold values from 0 to 4
- floe_velocity: float32 [16, 16, 2, 2048], P('gx', ('sec', 'gy')), may hold values from -3 to 3
- floe_radius: float32 [16, 16, 2048], P('gx', ('sec', 'gy')), may hold values from 0.5 to 1.5
- floe_mass: float32 [16, 16, 2048], P('gx', ('sec', 'gy')), may hold values from 0.5 to 5
- floe_polygon: float32 [16, 16, 32, 2048], P('gx', ('sec', 'gy')), may hold values from -2 to 2
- remap_cells: int32 [16, 16, 2048], P('gx', ('sec', 'gy')), may hold values from 0 to 131071, as said below
- contact_count: int32 [16, 16], P('gx', ('sec', 'gy')), may hold values from 8 to 64, as said below
- contact_list: int32 [16, 16, 3, 64], P('gx', ('sec', 'gy')), may hold values from 0 to 15, as said below
- move_index: int32 [16, 16, 8, 128], P('gx', ('sec', 'gy')), may hold values from 0 to 2047, as said below
- move_count: int32 [16, 16, 8], P('gx', ('sec', 'gy')), may hold values from 42 to 128, as said below
Outputs:
- ocean_next: float32 [2, 8, 1024, 2048], P(None, None, 'gx', ('sec', 'gy'))
- floe_next: float32 [16, 16, 4, 2048], P('gx', ('sec', 'gy'))
- arrivals: float32 [16, 16, 8, 38, 128], P('gx', ('sec', 'gy'))
The draws below stay inside these ranges and needn't reach their ends.
Inputs may be any that keep to these rules, and one draw needn't show every extreme that they name: `contact_list`: row 0 of each slot names a block of the tile, 0 to 15; row 1 a source 0 to 8, 4 meaning the tile itself; row 2 a block of the source: 0 to 15 for source 4, else 0 to 3. Only the first contact_count slots count. `contact_count`: some tile uses all 64 slots in every draw. `move_index`: the floes named by one tile over all directions and slots are distinct. `move_count`: every tile fills all 128 slots towards at least one neighbour. `remap_cells`: Row-major index over the 1024 rows and the tile's 128 columns. The floes of tile row i lie in grid rows i * 64 - 64 // 2 to i * 64 + 64 + 64 // 2 - 1 (within the grid), and every tile has floes in the first and the last row of that band.
All inputs are finite; a program needn't handle non-finite values.
Results may differ from the reference program's by a relative error of at most 0.0003.
Values sent between devices are 32-bit elements; how exact they have to be, the bound alone decides.
No kernel may reach another device: no remote copies, remote signals or barrier semaphores. Data moves between devices by JAX's collectives and lax.ppermute only.
A program may use at most 64 MiB of HBM per device.

```python
import math
import jax
import jax.numpy as jnp
from jax import lax

CX = 64
CY = 128
LEV = 8
OSTEPS = 4
NB = 16
GHOST = 4
CMAX = 64
MIG = 128
NV = 16
FLOE_DEV = 2048
TILE_ROWS = 16
TILE_COLS = 16
NX = 1024
NY = 2048


def draw_remap_cells(key, part):
    row_key, col_key = jax.random.split(jax.random.fold_in(key, 11))
    shape = (TILE_ROWS, TILE_COLS, FLOE_DEV)
    offsets = jax.random.randint(row_key, shape, 0, 2 * CX)
    base = jnp.arange(TILE_ROWS, dtype=jnp.int32)[:, None, None] * CX - CX // 2
    lowest = jnp.clip(base, 0, NX - 1)
    highest = jnp.clip(base + 2 * CX - 1, 0, NX - 1)
    rows_drawn = jnp.clip(base + offsets, 0, NX - 1)
    cols_drawn = jax.random.randint(col_key, shape, 0, CY)
    which = jnp.arange(FLOE_DEV, dtype=jnp.int32)[None, None, :]
    rows_drawn = jnp.where(which == 0, lowest, jnp.where(which == 1, highest, rows_drawn))
    cols_drawn = jnp.where(which == 0, 0, jnp.where(which == 1, CY - 1, cols_drawn))
    return (rows_drawn * CY + cols_drawn).astype(jnp.int32)


def draw_contact_count(key, part):
    first_key, second_key = jax.random.split(key)
    tiles = TILE_ROWS * TILE_COLS
    halvings = jax.random.randint(first_key, (tiles,), 0, 4)
    counts = jnp.right_shift(jnp.full((tiles,), CMAX, jnp.int32), halvings.astype(jnp.int32))
    busiest = jax.random.randint(second_key, (), 0, tiles)
    counts = jnp.where(jnp.arange(tiles) == busiest, CMAX, counts)
    return counts.reshape(TILE_ROWS, TILE_COLS).astype(jnp.int32)


def draw_contact_list(key, part):
    block_key, source_key, other_key = jax.random.split(key, 3)
    shape = (TILE_ROWS, TILE_COLS, CMAX)
    own_block = jax.random.randint(block_key, shape, 0, NB)
    picked = jax.random.randint(source_key, shape, 0, 16)
    shifted = picked - 8
    source = jnp.where(picked < 8, 4, shifted + (shifted >= 4).astype(jnp.int32))
    other = jax.random.randint(other_key, shape, 0, NB)
    other = jnp.where(source == 4, other, other % GHOST)
    return jnp.stack([own_block, source, other], axis=2).astype(jnp.int32)


def draw_move_index(key, part):
    keys = jax.random.split(key, TILE_ROWS * TILE_COLS)
    chosen = jax.vmap(lambda single: jax.random.permutation(single, FLOE_DEV)[:8 * MIG])(keys)
    return chosen.reshape(TILE_ROWS, TILE_COLS, 8, MIG).astype(jnp.int32)


def draw_move_count(key, part):
    first_key, second_key = jax.random.split(key)
    counts = jax.random.randint(first_key, (TILE_ROWS, TILE_COLS, 8), MIG // 3, MIG + 1)
    fullest = jax.random.randint(second_key, (TILE_ROWS, TILE_COLS, 1), 0, 8)
    counts = jnp.where(jnp.arange(8)[None, None, :] == fullest, MIG, counts)
    return counts.astype(jnp.int32)


def plant(drawn, rng, low, top_value):
    dims = drawn.shape
    place = [jax.random.randint(jax.random.fold_in(rng, axis), (), 0, dims[axis]) for axis in range(len(dims))]
    drawn = drawn.at[tuple(place)].set(low)
    longest = dims.index(max(dims))
    place[longest] = (place[longest] + 1) % dims[longest]
    return drawn.at[tuple(place)].set(top_value)


def steps_of(stream_key, shape, shards, smallest, high):
    def one(dim, parts):
        heights = jax.random.uniform(jax.random.fold_in(jax.random.fold_in(stream_key, 6), dim), (parts,), jnp.float32, smallest / len(shards), high / len(shards))
        return jnp.repeat(jnp.exp(heights), shape[dim] // parts).reshape((-1,) + (1,) * (len(shape) - dim - 1))

    level = one(*shards[0])
    for cut in shards[1:]:
        level = level * one(*cut)
    return level


def scatter_about(rng, extent, spread, most, cuts=(), kind=jnp.bfloat16):
    values = spread * jax.random.normal(rng, extent, jnp.float32)
    if cuts:
        values = values * steps_of(rng, extent, cuts, -0.22, 0.18)
    return jnp.clip(values, -most, most).astype(kind)


def setup_inputs(seed: int = 0) -> dict:
    arg_keys = jax.random.split(jax.random.key(seed), 14)
    ocean_velocity = scatter_about(arg_keys[0], (2, LEV, NX, NY), 1.0, 6.0, ((2, 16), (3, 16)), jnp.float32)
    wind_stress = scatter_about(arg_keys[1], (2, NX, NY), 1.0, 6.0, ((1, 16), (2, 16)), jnp.float32)
    level_counts = plant(jax.random.randint(arg_keys[2], (NX, NY), 1, LEV + 1), jax.random.fold_in(arg_keys[2], 1), 1, LEV).astype(jnp.int32)
    floe_position = jnp.clip(4.0 * jax.random.uniform(arg_keys[3], (TILE_ROWS, TILE_COLS, 2, FLOE_DEV), jnp.float32) ** steps_of(arg_keys[3], (TILE_ROWS, TILE_COLS, 2, FLOE_DEV), ((0, 16), (1, 16)), -0.2, 0.2), 0.0, 4.0)
    floe_velocity = scatter_about(arg_keys[4], (TILE_ROWS, TILE_COLS, 2, FLOE_DEV), 0.5, 3.0, ((0, 16), (1, 16)), jnp.float32)
    floe_radius = jnp.clip(0.5 + 1.0 * jax.random.uniform(arg_keys[5], (TILE_ROWS, TILE_COLS, FLOE_DEV), jnp.float32) ** steps_of(arg_keys[5], (TILE_ROWS, TILE_COLS, FLOE_DEV), ((0, 16), (1, 16)), -0.2, 0.2), 0.5, 1.5)
    floe_mass = jnp.clip(jnp.exp(math.log(5.0) - 2.3025851 * jax.random.uniform(arg_keys[6], (TILE_ROWS, TILE_COLS, FLOE_DEV), jnp.float32) ** steps_of(arg_keys[6], (TILE_ROWS, TILE_COLS, FLOE_DEV), ((0, 16), (1, 16)), -0.2, 0.2)), 0.5, 5.0)
    floe_polygon = scatter_about(arg_keys[7], (TILE_ROWS, TILE_COLS, 2 * NV, FLOE_DEV), 0.3, 2.0, ((0, 16), (1, 16)), jnp.float32)
    remap_cells = draw_remap_cells(jax.random.fold_in(arg_keys[13], 71), 0)
    contact_count = draw_contact_count(jax.random.fold_in(arg_keys[13], 71), 0)
    contact_list = draw_contact_list(jax.random.fold_in(arg_keys[13], 71), 0)
    move_index = draw_move_index(jax.random.fold_in(arg_keys[13], 71), 0)
    move_count = draw_move_count(jax.random.fold_in(arg_keys[13], 71), 0)
    return {"ocean_velocity": ocean_velocity, "wind_stress": wind_stress, "level_counts": level_counts, "floe_position": floe_position, "floe_velocity": floe_velocity, "floe_radius": floe_radius, "floe_mass": floe_mass, "floe_polygon": floe_polygon, "remap_cells": remap_cells, "contact_count": contact_count, "contact_list": contact_list, "move_index": move_index, "move_count": move_count}


SOFTEN = 0.1
STIFFNESS = 0.1
DAMPING = 0.05
VERT_MIX = 0.15
CORIOLIS = 0.1
SURFACE_GAIN = 0.25
WATER_DRAG = 0.1
AIR_GAIN = 0.2
ICE_STEP = 0.5
PLACES = (0, 1, 2, 3, 5, 6, 7, 8)

def ocean_substep(flow, padded, wet, wind):
    levels_here = flow.shape[1]
    lap = padded[:, :, :-2, 1:-1] + padded[:, :, 2:, 1:-1] + padded[:, :, 1:-1, :-2] + padded[:, :, 1:-1, 2:] - 4.0 * flow
    depth = jnp.arange(levels_here, dtype=jnp.float32)
    horizontal = (0.15 - 0.05 * depth / levels_here)[None, :, None, None]
    flux = VERT_MIX * (flow[:, 1:] - flow[:, :-1]) * wet[None, 1:]
    empty = jnp.zeros_like(flow[:, :1])
    vert = jnp.concatenate([flux, empty], axis=1) - jnp.concatenate([empty, flux], axis=1)
    turning = jnp.stack([CORIOLIS * flow[1], -CORIOLIS * flow[0]])
    surface = jnp.concatenate([SURFACE_GAIN * wind[:, None], jnp.zeros_like(flow[:, 1:])], axis=1)
    return (flow + horizontal * lap + vert + turning + surface) * wet[None]

def pair_forces(first, second):
    delta_x = first[:, 0, :, None] - second[:, 0, None, :]
    delta_y = first[:, 1, :, None] - second[:, 1, None, :]
    distance = jnp.sqrt(delta_x * delta_x + delta_y * delta_y + SOFTEN * SOFTEN)
    reach = first[:, 4, :, None] + second[:, 4, None, :]
    intersection = jnp.maximum(reach - distance, 0.0)
    reduced = first[:, 4, :, None] * second[:, 4, None, :] / reach
    normal_x = delta_x / distance
    normal_y = delta_y / distance
    closing = (first[:, 2, :, None] - second[:, 2, None, :]) * normal_x + (first[:, 3, :, None] - second[:, 3, None, :]) * normal_y
    magnitude = intersection * reduced * (STIFFNESS - DAMPING * closing)
    return jnp.stack([lax.optimization_barrier(jnp.sum(magnitude * normal_x, axis=2)), lax.optimization_barrier(jnp.sum(magnitude * normal_y, axis=2))], axis=1)

def block_table(own, ghosts):
    blocks = own.shape[1] // 128
    edge_blocks = ghosts.shape[2] // 128
    mine = own.reshape(5, blocks, 128).transpose(1, 0, 2)
    theirs = ghosts.reshape(8, 5, edge_blocks, 128).transpose(0, 2, 1, 3).reshape(8 * edge_blocks, 5, 128)
    return jnp.concatenate([mine, theirs], axis=0)

def contact_batch(table, lists, valid, blocks, edge_blocks):
    source = lists[1]
    neighbour = source - (source > 4).astype(jnp.int32)
    partner = jnp.where(source == 4, lists[2], blocks + neighbour * edge_blocks + lists[2])
    forces = pair_forces(table[lists[0]], table[partner])
    forces = jnp.where(valid[:, None, None], forces, 0.0)
    onehot = (lists[0][:, None] == jnp.arange(blocks, dtype=jnp.int32)[None, :]).astype(jnp.float32)
    return jnp.einsum('pn,pcf->ncf', onehot, forces, precision=lax.Precision.HIGHEST)

def tile_contacts(own, ghosts, lists, count):
    blocks = own.shape[1] // 128
    edge_blocks = ghosts.shape[2] // 128
    table = block_table(own, ghosts)
    slots = lists.shape[1]
    batch = math.gcd(slots, 32)
    grouped = lists.reshape(3, slots // batch, batch).transpose(1, 0, 2)
    starts = jnp.arange(slots // batch, dtype=jnp.int32) * batch

    def accumulate(total, item):
        group, start = item
        valid = start + jnp.arange(batch, dtype=jnp.int32) < count
        return (total + contact_batch(table, group, valid, blocks, edge_blocks), None)
    total, unused = lax.scan(accumulate, jnp.zeros((blocks, 2, 128), jnp.float32), (grouped, starts))
    return total.transpose(1, 0, 2).reshape(2, blocks * 128)

def reference(ocean_velocity, wind_stress, level_counts, floe_position, floe_velocity, floe_radius, floe_mass, floe_polygon, remap_cells, contact_count, contact_list, move_index, move_count):
    levels_here = ocean_velocity.shape[1]
    wet = (jnp.arange(levels_here, dtype=jnp.int32)[:, None, None] < level_counts[None]).astype(jnp.float32)
    flow = ocean_velocity * wet[None]
    for substep in range(OSTEPS):
        padded = jnp.pad(flow, ((0, 0), (0, 0), (1, 1), (1, 1)))
        flow = ocean_substep(flow, padded, wet, wind_stress)
    ocean_next = flow
    surface = jnp.stack([flow[0, 0], flow[1, 0], wind_stress[0], wind_stress[1]])
    tile_rows, tile_cols, floes = remap_cells.shape
    strip_rows = remap_cells // CY
    strip_cols = jnp.arange(tile_cols, dtype=jnp.int32)[None, :, None] * CY + remap_cells % CY
    sampled = jnp.moveaxis(surface[:, strip_rows, strip_cols], 0, 2)
    record = jnp.concatenate([floe_position, floe_velocity, floe_radius[:, :, None]], axis=2)
    edge = record[:, :, :, :GHOST * 128]
    padded_edge = jnp.pad(edge, ((1, 1), (1, 1), (0, 0), (0, 0)))
    ghosts = jnp.stack([padded_edge[p // 3:p // 3 + tile_rows, p % 3:p % 3 + tile_cols] for p in PLACES], axis=2)
    devices = tile_rows * tile_cols
    contact = lax.map(lambda item: tile_contacts(*item), (record.reshape(devices, 5, floes), ghosts.reshape(devices, 8, 5, GHOST * 128), contact_list.reshape(devices, 3, -1), contact_count.reshape(devices)))
    contact = contact.reshape(tile_rows, tile_cols, 2, floes)
    area = math.pi * floe_radius * floe_radius
    relative = sampled[:, :, 0:2] - floe_velocity
    speed = jnp.sqrt(lax.optimization_barrier(jnp.sum(relative * relative, axis=2, keepdims=True)))
    total = contact + area[:, :, None] * (WATER_DRAG * speed * relative + AIR_GAIN * sampled[:, :, 2:4])
    new_velocity = floe_velocity + ICE_STEP * total / floe_mass[:, :, None]
    new_position = floe_position + ICE_STEP * new_velocity
    floe_next = jnp.concatenate([new_position, new_velocity], axis=2)
    rows_all = jnp.concatenate([floe_next, floe_radius[:, :, None], floe_mass[:, :, None], floe_polygon], axis=2)
    width = rows_all.shape[2]
    slots = move_index.shape[3]
    chosen = move_index.reshape(tile_rows, tile_cols, 1, 8 * slots)
    taken = jnp.take_along_axis(rows_all, jnp.broadcast_to(chosen, (tile_rows, tile_cols, width, 8 * slots)), axis=3)
    taken = taken.reshape(tile_rows, tile_cols, width, 8, slots).transpose(0, 1, 3, 2, 4)
    valid = jnp.arange(slots, dtype=jnp.int32)[None, None, None, :] < move_count[:, :, :, None]
    outgoing = jnp.where(valid[:, :, :, None, :], taken, 0.0)
    padded_out = jnp.pad(outgoing, ((1, 1), (1, 1), (0, 0), (0, 0), (0, 0)))
    pieces = []
    for way in range(8):
        row_step = PLACES[way] // 3 - 1
        col_step = PLACES[way] % 3 - 1
        pieces.append(padded_out[1 - row_step:1 - row_step + tile_rows, 1 - col_step:1 - col_step + tile_cols, way])
    arrivals = jnp.stack(pieces, axis=2)
    return (ocean_next, floe_next, arrivals)
```

```python
import math

import jax
import jax.numpy as jnp
from jax import lax
from jax.sharding import PartitionSpec as P

OSTEPS = 4
GHOST = 4


SOFTEN = 0.1
STIFFNESS = 0.1
DAMPING = 0.05
VERT_MIX = 0.15
CORIOLIS = 0.1
SURFACE_GAIN = 0.25
WATER_DRAG = 0.1
AIR_GAIN = 0.2
ICE_STEP = 0.5
PLACES = (0, 1, 2, 3, 5, 6, 7, 8)


def with_halo(array, sides, width):
    for axis, dim in sides:
        size, length = (lax.axis_size(axis), array.shape[dim])
        up = [(i, (i + 1) % size) for i in range(size - 1)]
        down = [(j, i) for i, j in up]
        last = lax.slice_in_dim(array, length - width, length, axis=dim)
        leading = lax.slice_in_dim(array, 0, width, axis=dim)
        before = lax.ppermute(last, axis, up)
        after = lax.ppermute(leading, axis, down)
        array = jnp.concatenate([before, array, after], axis=dim)
    return array


def ocean_substep(flow, padded, wet, wind):
    levels_here = flow.shape[1]
    lap = (
        padded[:, :, :-2, 1:-1]
        + padded[:, :, 2:, 1:-1]
        + padded[:, :, 1:-1, :-2]
        + padded[:, :, 1:-1, 2:]
        - 4.0 * flow
    )
    depth = jnp.arange(levels_here, dtype=jnp.float32)
    horizontal = (0.15 - 0.05 * depth / levels_here)[None, :, None, None]
    flux = VERT_MIX * (flow[:, 1:] - flow[:, :-1]) * wet[None, 1:]
    empty = jnp.zeros_like(flow[:, :1])
    vert = jnp.concatenate([flux, empty], axis=1) - jnp.concatenate([empty, flux], axis=1)
    turning = jnp.stack([CORIOLIS * flow[1], -CORIOLIS * flow[0]])
    surface = jnp.concatenate([SURFACE_GAIN * wind[:, None], jnp.zeros_like(flow[:, 1:])], axis=1)
    return (flow + horizontal * lap + vert + turning + surface) * wet[None]


def pair_forces(first, second):
    delta_x = first[:, 0, :, None] - second[:, 0, None, :]
    delta_y = first[:, 1, :, None] - second[:, 1, None, :]
    distance = jnp.sqrt(delta_x * delta_x + delta_y * delta_y + SOFTEN * SOFTEN)
    reach = first[:, 4, :, None] + second[:, 4, None, :]
    intersection = jnp.maximum(reach - distance, 0.0)
    reduced = first[:, 4, :, None] * second[:, 4, None, :] / reach
    normal_x = delta_x / distance
    normal_y = delta_y / distance
    closing = (first[:, 2, :, None] - second[:, 2, None, :]) * normal_x + (
        first[:, 3, :, None] - second[:, 3, None, :]
    ) * normal_y
    magnitude = intersection * reduced * (STIFFNESS - DAMPING * closing)
    return jnp.stack(
        [jnp.sum(magnitude * normal_x, axis=2), jnp.sum(magnitude * normal_y, axis=2)], axis=1
    )


def block_table(own, ghosts):
    blocks = own.shape[1] // 128
    edge_blocks = ghosts.shape[2] // 128
    mine = own.reshape(5, blocks, 128).transpose(1, 0, 2)
    theirs = (
        ghosts.reshape(8, 5, edge_blocks, 128)
        .transpose(0, 2, 1, 3)
        .reshape(8 * edge_blocks, 5, 128)
    )
    return jnp.concatenate([mine, theirs], axis=0)


def contact_batch(table, lists, valid, blocks, edge_blocks):
    source = lists[1]
    neighbour = source - (source > 4).astype(jnp.int32)
    partner = jnp.where(source == 4, lists[2], blocks + neighbour * edge_blocks + lists[2])
    forces = pair_forces(table[lists[0]], table[partner])
    forces = jnp.where(valid[:, None, None], forces, 0.0)
    onehot = (lists[0][:, None] == jnp.arange(blocks, dtype=jnp.int32)[None, :]).astype(jnp.float32)
    return jnp.einsum("pn,pcf->ncf", onehot, forces, precision=lax.Precision.HIGHEST)


def exchange(low, high, axis):
    size = lax.axis_size(axis)
    up = [(i, i + 1) for i in range(size - 1)]
    down = [(i + 1, i) for i in range(size - 1)]
    from_previous = lax.ppermute(high, axis, up)
    from_next = lax.ppermute(low, axis, down)
    return from_previous, from_next


def shards(
    ocean_velocity,
    wind_stress,
    level_counts,
    floe_position,
    floe_velocity,
    floe_radius,
    floe_mass,
    floe_polygon,
    remap_cells,
    contact_count,
    contact_list,
    move_index,
    move_count,
):
    columns = ("sec", "gy")
    comps, levels_here, rows_here, cols_here = ocean_velocity.shape
    halo = OSTEPS
    position = floe_position[0, 0]
    velocity = floe_velocity[0, 0]
    radius = floe_radius[0, 0]
    mass = floe_mass[0, 0]
    cells = remap_cells[0, 0]
    floes = position.shape[1]
    blocks = floes // 128
    record = jnp.concatenate([position, velocity, radius[None]], axis=0)
    edge = record[:, : GHOST * 128]
    edge_size = edge.size

    fields = jnp.concatenate(
        [
            ocean_velocity.reshape(comps * levels_here, rows_here, cols_here),
            wind_stress,
            level_counts.astype(jnp.float32)[None],
        ],
        axis=0,
    )
    channels = fields.shape[0]
    row_strip = channels * halo * cols_here
    low = jnp.concatenate([fields[:, :halo].reshape(-1), edge.reshape(-1)])
    high = jnp.concatenate([fields[:, -halo:].reshape(-1), edge.reshape(-1)])
    above, below = exchange(low, high, "gx")
    extended = jnp.concatenate(
        [
            above[:row_strip].reshape(channels, halo, cols_here),
            fields,
            below[:row_strip].reshape(channels, halo, cols_here),
        ],
        axis=1,
    )
    ghost_column = jnp.stack(
        [above[row_strip:].reshape(edge.shape), edge, below[row_strip:].reshape(edge.shape)]
    )
    ext_rows = rows_here + 2 * halo
    col_strip = channels * ext_rows * halo
    low = jnp.concatenate([extended[:, :, :halo].reshape(-1), ghost_column.reshape(-1)])
    high = jnp.concatenate([extended[:, :, -halo:].reshape(-1), ghost_column.reshape(-1)])
    left, right = exchange(low, high, columns)
    extended = jnp.concatenate(
        [
            left[:col_strip].reshape(channels, ext_rows, halo),
            extended,
            right[:col_strip].reshape(channels, ext_rows, halo),
        ],
        axis=2,
    )
    ghost_left = left[col_strip:].reshape(3, *edge.shape)
    ghost_right = right[col_strip:].reshape(3, *edge.shape)
    beside = [ghost_left, ghost_column, ghost_right]
    ghosts = jnp.stack([beside[p % 3][p // 3] for p in PLACES])

    ext_cols = cols_here + 2 * halo
    counts_ext = extended[-1]
    wet = (jnp.arange(levels_here, dtype=jnp.float32)[:, None, None] < counts_ext[None]).astype(
        jnp.float32
    )
    wind_ext = extended[comps * levels_here : comps * levels_here + 2]
    flow = extended[: comps * levels_here].reshape(comps, levels_here, ext_rows, ext_cols) * wet[None]
    for substep in range(OSTEPS):
        padded = jnp.pad(flow, ((0, 0), (0, 0), (1, 1), (1, 1)))
        flow = ocean_substep(flow, padded, wet, wind_ext)
    flow = flow[:, :, halo : halo + rows_here, halo : halo + cols_here]

    table = block_table(record, ghosts)
    surface = jnp.stack([flow[0, 0], flow[1, 0], wind_stress[0], wind_stress[1]])
    margin = rows_here // 2
    from_above, from_below = exchange(surface[:, :margin], surface[:, -margin:], "gx")
    near = jnp.concatenate([from_above, surface, from_below], axis=1)
    first_row = lax.axis_index("gx") * rows_here - margin
    sampled = jnp.take(near.reshape(4, -1), cells - first_row * cols_here, axis=1)
    lists = contact_list[0, 0]
    count = contact_count[0, 0]
    slots = lists.shape[1]
    batch = math.gcd(slots, 32)
    rounds = (count + batch - 1) // batch

    def accumulate(turn, total):
        start = turn * batch
        group = lax.dynamic_slice_in_dim(lists, start, batch, 1)
        valid = start + jnp.arange(batch, dtype=jnp.int32) < count
        return total + contact_batch(table, group, valid, blocks, GHOST)

    contact = lax.fori_loop(0, rounds, accumulate, jnp.zeros((blocks, 2, 128), jnp.float32))
    contact = contact.transpose(1, 0, 2).reshape(2, floes)
    area = math.pi * radius * radius
    relative = sampled[0:2] - velocity
    speed = jnp.sqrt(jnp.sum(relative * relative, axis=0, keepdims=True))
    total = contact + area[None] * (WATER_DRAG * speed * relative + AIR_GAIN * sampled[2:4])
    new_velocity = velocity + ICE_STEP * total / mass[None]
    new_position = position + ICE_STEP * new_velocity
    floe_next = jnp.concatenate([new_position, new_velocity], axis=0)
    rows_all = jnp.concatenate([floe_next, radius[None], mass[None], floe_polygon[0, 0]], axis=0)
    width = rows_all.shape[0]
    leaving = move_index[0, 0]
    capacity = leaving.shape[1]
    taken = (
        jnp.take(rows_all, leaving.reshape(-1), axis=1)
        .reshape(width, 8, capacity)
        .transpose(1, 0, 2)
    )
    valid_slots = jnp.arange(capacity, dtype=jnp.int32)[None, :] < move_count[0, 0][:, None]
    outgoing = jnp.where(valid_slots[:, None, :], taken, 0.0)
    from_above, from_below = exchange(outgoing[0:3], outgoing[5:8], "gx")
    heading_left = jnp.stack([from_below[0], outgoing[3], from_above[0]])
    heading_right = jnp.stack([from_below[2], outgoing[4], from_above[2]])
    from_left, from_right = exchange(heading_left, heading_right, columns)
    arrivals = jnp.stack(
        [
            from_right[0],
            from_below[1],
            from_left[0],
            from_right[1],
            from_left[1],
            from_right[2],
            from_above[1],
            from_left[2],
        ]
    )
    return (flow, floe_next[None, None], arrivals[None, None])


def solution(mesh):
    return jax.shard_map(
        shards,
        mesh=mesh,
        in_specs=(
            P(None, None, "gx", ("sec", "gy")),
            P(None, "gx", ("sec", "gy")),
            P("gx", ("sec", "gy")),
            P("gx", ("sec", "gy"), None, None),
            P("gx", ("sec", "gy"), None, None),
            P("gx", ("sec", "gy"), None),
            P("gx", ("sec", "gy"), None),
            P("gx", ("sec", "gy"), None, None),
            P("gx", ("sec", "gy"), None),
            P("gx", ("sec", "gy")),
            P("gx", ("sec", "gy"), None, None),
            P("gx", ("sec", "gy"), None, None),
            P("gx", ("sec", "gy"), None),
        ),
        out_specs=(
            P(None, None, "gx", ("sec", "gy")),
            P("gx", ("sec", "gy"), None, None),
            P("gx", ("sec", "gy"), None, None, None),
        ),
        check_vma=False,
    )
```

```python
import math

import jax
import jax.numpy as jnp
from jax import lax
from jax.experimental import pallas as pl
from jax.experimental.pallas import tpu as pltpu
from jax.sharding import PartitionSpec as P

OSTEPS = 4
GHOST = 4


SOFTEN = 0.1
STIFFNESS = 0.1
DAMPING = 0.05
VERT_MIX = 0.15
CORIOLIS = 0.1
SURFACE_GAIN = 0.25
WATER_DRAG = 0.1
AIR_GAIN = 0.2
ICE_STEP = 0.5
PLACES = (0, 1, 2, 3, 5, 6, 7, 8)


def with_halo(array, sides, width):
    for axis, dim in sides:
        size, length = (lax.axis_size(axis), array.shape[dim])
        up = [(i, (i + 1) % size) for i in range(size - 1)]
        down = [(j, i) for i, j in up]
        last = lax.slice_in_dim(array, length - width, length, axis=dim)
        leading = lax.slice_in_dim(array, 0, width, axis=dim)
        before = lax.ppermute(last, axis, up)
        after = lax.ppermute(leading, axis, down)
        array = jnp.concatenate([before, array, after], axis=dim)
    return array


def ocean_substep(flow, padded, wet, wind):
    levels_here = flow.shape[1]
    lap = (
        padded[:, :, :-2, 1:-1]
        + padded[:, :, 2:, 1:-1]
        + padded[:, :, 1:-1, :-2]
        + padded[:, :, 1:-1, 2:]
        - 4.0 * flow
    )
    depth = jnp.arange(levels_here, dtype=jnp.float32)
    horizontal = (0.15 - 0.05 * depth / levels_here)[None, :, None, None]
    flux = VERT_MIX * (flow[:, 1:] - flow[:, :-1]) * wet[None, 1:]
    empty = jnp.zeros_like(flow[:, :1])
    vert = jnp.concatenate([flux, empty], axis=1) - jnp.concatenate([empty, flux], axis=1)
    turning = jnp.stack([CORIOLIS * flow[1], -CORIOLIS * flow[0]])
    surface = jnp.concatenate([SURFACE_GAIN * wind[:, None], jnp.zeros_like(flow[:, 1:])], axis=1)
    return (flow + horizontal * lap + vert + turning + surface) * wet[None]


def pair_forces(first, second):
    delta_x = first[:, 0, :, None] - second[:, 0, None, :]
    delta_y = first[:, 1, :, None] - second[:, 1, None, :]
    distance = jnp.sqrt(delta_x * delta_x + delta_y * delta_y + SOFTEN * SOFTEN)
    reach = first[:, 4, :, None] + second[:, 4, None, :]
    intersection = jnp.maximum(reach - distance, 0.0)
    reduced = first[:, 4, :, None] * second[:, 4, None, :] / reach
    normal_x = delta_x / distance
    normal_y = delta_y / distance
    closing = (first[:, 2, :, None] - second[:, 2, None, :]) * normal_x + (
        first[:, 3, :, None] - second[:, 3, None, :]
    ) * normal_y
    magnitude = intersection * reduced * (STIFFNESS - DAMPING * closing)
    return jnp.stack(
        [jnp.sum(magnitude * normal_x, axis=2), jnp.sum(magnitude * normal_y, axis=2)], axis=1
    )


def block_table(own, ghosts):
    blocks = own.shape[1] // 128
    edge_blocks = ghosts.shape[2] // 128
    mine = own.reshape(5, blocks, 128).transpose(1, 0, 2)
    theirs = (
        ghosts.reshape(8, 5, edge_blocks, 128)
        .transpose(0, 2, 1, 3)
        .reshape(8 * edge_blocks, 5, 128)
    )
    return jnp.concatenate([mine, theirs], axis=0)


def contact_batch(table, lists, valid, blocks, edge_blocks):
    source = lists[1]
    neighbour = source - (source > 4).astype(jnp.int32)
    partner = jnp.where(source == 4, lists[2], blocks + neighbour * edge_blocks + lists[2])
    forces = pair_forces(table[lists[0]], table[partner])
    forces = jnp.where(valid[:, None, None], forces, 0.0)
    onehot = (lists[0][:, None] == jnp.arange(blocks, dtype=jnp.int32)[None, :]).astype(jnp.float32)
    return jnp.einsum("pn,pcf->ncf", onehot, forces, precision=lax.Precision.HIGHEST)


def split_three(x):
    high = x.astype(jnp.bfloat16)
    rest = x - high.astype(jnp.float32)
    middle = rest.astype(jnp.bfloat16)
    low = (rest - middle.astype(jnp.float32)).astype(jnp.bfloat16)
    return high, middle, low


def exact_select(parts, onehot):
    high, middle, low = (jnp.dot(p, onehot, preferred_element_type=jnp.float32) for p in parts)
    return (high + middle) + low


def sample_kernel(window_ref, rows_ref, cols_ref, out_ref):
    window_rows, window_cols = window_ref.shape[1:]
    floes = rows_ref.shape[1]
    onehot = (
        lax.broadcasted_iota(jnp.int32, (window_rows, floes), 0) == rows_ref[...]
    ).astype(jnp.bfloat16)
    pick = lax.broadcasted_iota(jnp.int32, (window_cols, floes), 0) == cols_ref[...]
    for channel in range(window_ref.shape[0]):
        picked = exact_select(split_three(window_ref[channel].T), onehot)
        out_ref[channel : channel + 1, :] = jnp.sum(
            jnp.where(pick, picked, 0.0), axis=0, keepdims=True
        )


def sample_surface(window, rows, cols):
    return pl.pallas_call(
        sample_kernel,
        out_shape=jax.ShapeDtypeStruct((window.shape[0], rows.shape[1]), jnp.float32),
    )(window, rows, cols)


def gather_kernel(state_ref, radius_ref, mass_ref, polygon_ref, index_ref, out_ref, head_ref):
    floes = state_ref.shape[1]
    slots = index_ref.shape[1]
    head_ref[...] = jnp.zeros_like(head_ref)
    head_ref[0:4, :] = state_ref[...]
    head_ref[4:5, :] = radius_ref[...]
    head_ref[5:6, :] = mass_ref[...]
    head = split_three(head_ref[...])
    polygon = split_three(polygon_ref[...])
    rows = head_ref.shape[0]
    for way in range(index_ref.shape[0]):
        onehot = (
            lax.broadcasted_iota(jnp.int32, (floes, slots), 0) == index_ref[way : way + 1, :]
        ).astype(jnp.bfloat16)
        out_ref[way, 0:rows, :] = exact_select(head, onehot)
        out_ref[way, rows:, :] = exact_select(polygon, onehot)


def gather_records(state, radius, mass, polygon, index):
    rows = 8 + polygon.shape[0]
    return pl.pallas_call(
        gather_kernel,
        out_shape=jax.ShapeDtypeStruct((index.shape[0], rows, index.shape[1]), jnp.float32),
        scratch_shapes=[pltpu.VMEM((8, state.shape[1]), jnp.float32)],
    )(state, radius, mass, polygon, index)


def exchange(low, high, axis):
    size = lax.axis_size(axis)
    up = [(i, i + 1) for i in range(size - 1)]
    down = [(i + 1, i) for i in range(size - 1)]
    from_previous = lax.ppermute(high, axis, up)
    from_next = lax.ppermute(low, axis, down)
    return from_previous, from_next


def shards(
    ocean_velocity,
    wind_stress,
    level_counts,
    floe_position,
    floe_velocity,
    floe_radius,
    floe_mass,
    floe_polygon,
    remap_cells,
    contact_count,
    contact_list,
    move_index,
    move_count,
):
    columns = ("sec", "gy")
    comps, levels_here, rows_here, cols_here = ocean_velocity.shape
    halo = OSTEPS
    position = floe_position[0, 0]
    velocity = floe_velocity[0, 0]
    radius = floe_radius[0, 0]
    mass = floe_mass[0, 0]
    cells = remap_cells[0, 0]
    floes = position.shape[1]
    blocks = floes // 128
    record = jnp.concatenate([position, velocity, radius[None]], axis=0)
    edge = record[:, : GHOST * 128]
    edge_size = edge.size

    fields = jnp.concatenate(
        [
            ocean_velocity.reshape(comps * levels_here, rows_here, cols_here),
            wind_stress,
            level_counts.astype(jnp.float32)[None],
        ],
        axis=0,
    )
    channels = fields.shape[0]
    row_strip = channels * halo * cols_here
    low = jnp.concatenate([fields[:, :halo].reshape(-1), edge.reshape(-1)])
    high = jnp.concatenate([fields[:, -halo:].reshape(-1), edge.reshape(-1)])
    above, below = exchange(low, high, "gx")
    extended = jnp.concatenate(
        [
            above[:row_strip].reshape(channels, halo, cols_here),
            fields,
            below[:row_strip].reshape(channels, halo, cols_here),
        ],
        axis=1,
    )
    ghost_column = jnp.stack(
        [above[row_strip:].reshape(edge.shape), edge, below[row_strip:].reshape(edge.shape)]
    )
    ext_rows = rows_here + 2 * halo
    col_strip = channels * ext_rows * halo
    low = jnp.concatenate([extended[:, :, :halo].reshape(-1), ghost_column.reshape(-1)])
    high = jnp.concatenate([extended[:, :, -halo:].reshape(-1), ghost_column.reshape(-1)])
    left, right = exchange(low, high, columns)
    extended = jnp.concatenate(
        [
            left[:col_strip].reshape(channels, ext_rows, halo),
            extended,
            right[:col_strip].reshape(channels, ext_rows, halo),
        ],
        axis=2,
    )
    ghost_left = left[col_strip:].reshape(3, *edge.shape)
    ghost_right = right[col_strip:].reshape(3, *edge.shape)
    beside = [ghost_left, ghost_column, ghost_right]
    ghosts = jnp.stack([beside[p % 3][p // 3] for p in PLACES])

    ext_cols = cols_here + 2 * halo
    counts_ext = extended[-1]
    wet = (jnp.arange(levels_here, dtype=jnp.float32)[:, None, None] < counts_ext[None]).astype(
        jnp.float32
    )
    wind_ext = extended[comps * levels_here : comps * levels_here + 2]
    flow = extended[: comps * levels_here].reshape(comps, levels_here, ext_rows, ext_cols) * wet[None]
    for substep in range(OSTEPS):
        padded = jnp.pad(flow, ((0, 0), (0, 0), (1, 1), (1, 1)))
        flow = ocean_substep(flow, padded, wet, wind_ext)
    flow = flow[:, :, halo : halo + rows_here, halo : halo + cols_here]

    table = block_table(record, ghosts)
    surface = jnp.stack([flow[0, 0], flow[1, 0], wind_stress[0], wind_stress[1]])
    margin = rows_here // 2
    from_above, from_below = exchange(surface[:, :margin], surface[:, -margin:], "gx")
    near = jnp.concatenate([from_above, surface, from_below], axis=1)
    first_row = lax.axis_index("gx") * rows_here - margin
    sampled = sample_surface(
        near,
        (cells // cols_here - first_row)[None],
        (cells % cols_here)[None],
    )
    lists = contact_list[0, 0]
    count = contact_count[0, 0]
    slots = lists.shape[1]
    batch = math.gcd(slots, 32)
    rounds = (count + batch - 1) // batch

    def accumulate(turn, total):
        start = turn * batch
        group = lax.dynamic_slice_in_dim(lists, start, batch, 1)
        valid = start + jnp.arange(batch, dtype=jnp.int32) < count
        return total + contact_batch(table, group, valid, blocks, GHOST)

    contact = lax.fori_loop(0, rounds, accumulate, jnp.zeros((blocks, 2, 128), jnp.float32))
    contact = contact.transpose(1, 0, 2).reshape(2, floes)
    area = math.pi * radius * radius
    relative = sampled[0:2] - velocity
    speed = jnp.sqrt(jnp.sum(relative * relative, axis=0, keepdims=True))
    total = contact + area[None] * (WATER_DRAG * speed * relative + AIR_GAIN * sampled[2:4])
    new_velocity = velocity + ICE_STEP * total / mass[None]
    new_position = position + ICE_STEP * new_velocity
    floe_next = jnp.concatenate([new_position, new_velocity], axis=0)
    leaving = move_index[0, 0]
    capacity = leaving.shape[1]
    valid_slots = jnp.arange(capacity, dtype=jnp.int32)[None, :] < move_count[0, 0][:, None]
    outgoing = gather_records(
        floe_next, radius[None], mass[None], floe_polygon[0, 0], jnp.where(valid_slots, leaving, -1)
    )
    from_above, from_below = exchange(outgoing[0:3], outgoing[5:8], "gx")
    heading_left = jnp.stack([from_below[0], outgoing[3], from_above[0]])
    heading_right = jnp.stack([from_below[2], outgoing[4], from_above[2]])
    from_left, from_right = exchange(heading_left, heading_right, columns)
    arrivals = jnp.stack(
        [
            from_right[0],
            from_below[1],
            from_left[0],
            from_right[1],
            from_left[1],
            from_right[2],
            from_above[1],
            from_left[2],
        ]
    )
    arrivals = jnp.concatenate([arrivals[:, 0:6], arrivals[:, 8:]], axis=1)
    return (flow, floe_next[None, None], arrivals[None, None])


def solution(mesh):
    return jax.shard_map(
        shards,
        mesh=mesh,
        in_specs=(
            P(None, None, "gx", ("sec", "gy")),
            P(None, "gx", ("sec", "gy")),
            P("gx", ("sec", "gy")),
            P("gx", ("sec", "gy"), None, None),
            P("gx", ("sec", "gy"), None, None),
            P("gx", ("sec", "gy"), None),
            P("gx", ("sec", "gy"), None),
            P("gx", ("sec", "gy"), None, None),
            P("gx", ("sec", "gy"), None),
            P("gx", ("sec", "gy")),
            P("gx", ("sec", "gy"), None, None),
            P("gx", ("sec", "gy"), None, None),
            P("gx", ("sec", "gy"), None),
        ),
        out_specs=(
            P(None, None, "gx", ("sec", "gy")),
            P("gx", ("sec", "gy"), None, None),
            P("gx", ("sec", "gy"), None, None, None),
        ),
        check_vma=False,
    )
```

```python
import math

import jax
import jax.numpy as jnp
from jax import lax
from jax.experimental import pallas as pl
from jax.experimental.pallas import tpu as pltpu
from jax.sharding import PartitionSpec as P

OSTEPS = 4
GHOST = 4


SOFTEN = 0.1
STIFFNESS = 0.1
DAMPING = 0.05
VERT_MIX = 0.15
CORIOLIS = 0.1
SURFACE_GAIN = 0.25
WATER_DRAG = 0.1
AIR_GAIN = 0.2
ICE_STEP = 0.5
PLACES = (0, 1, 2, 3, 5, 6, 7, 8)


def with_halo(array, sides, width):
    for axis, dim in sides:
        size, length = (lax.axis_size(axis), array.shape[dim])
        up = [(i, (i + 1) % size) for i in range(size - 1)]
        down = [(j, i) for i, j in up]
        last = lax.slice_in_dim(array, length - width, length, axis=dim)
        leading = lax.slice_in_dim(array, 0, width, axis=dim)
        before = lax.ppermute(last, axis, up)
        after = lax.ppermute(leading, axis, down)
        array = jnp.concatenate([before, array, after], axis=dim)
    return array


def ocean_substep(flow, padded, wet, wind):
    levels_here = flow.shape[1]
    lap = (
        padded[:, :, :-2, 1:-1]
        + padded[:, :, 2:, 1:-1]
        + padded[:, :, 1:-1, :-2]
        + padded[:, :, 1:-1, 2:]
        - 4.0 * flow
    )
    depth = jnp.arange(levels_here, dtype=jnp.float32)
    horizontal = (0.15 - 0.05 * depth / levels_here)[None, :, None, None]
    flux = VERT_MIX * (flow[:, 1:] - flow[:, :-1]) * wet[None, 1:]
    empty = jnp.zeros_like(flow[:, :1])
    vert = jnp.concatenate([flux, empty], axis=1) - jnp.concatenate([empty, flux], axis=1)
    turning = jnp.stack([CORIOLIS * flow[1], -CORIOLIS * flow[0]])
    surface = jnp.concatenate([SURFACE_GAIN * wind[:, None], jnp.zeros_like(flow[:, 1:])], axis=1)
    return (flow + horizontal * lap + vert + turning + surface) * wet[None]


def pair_forces(first, second):
    own = first[:, :, None, :]
    other = second[:, :, :, None]
    delta_x = own[:, 0] - other[:, 0]
    delta_y = own[:, 1] - other[:, 1]
    inverse = lax.rsqrt(delta_x * delta_x + delta_y * delta_y + SOFTEN * SOFTEN)
    distance = (delta_x * delta_x + delta_y * delta_y + SOFTEN * SOFTEN) * inverse
    reach = own[:, 4] + other[:, 4]
    intersection = jnp.maximum(reach - distance, 0.0)
    reduced = own[:, 4] * other[:, 4] / reach
    normal_x = delta_x * inverse
    normal_y = delta_y * inverse
    closing = (own[:, 2] - other[:, 2]) * normal_x + (own[:, 3] - other[:, 3]) * normal_y
    magnitude = intersection * reduced * (STIFFNESS - DAMPING * closing)
    return jnp.stack(
        [jnp.sum(magnitude * normal_x, axis=1), jnp.sum(magnitude * normal_y, axis=1)], axis=1
    )


def block_table(own, ghosts):
    blocks = own.shape[1] // 128
    edge_blocks = ghosts.shape[2] // 128
    mine = own.reshape(5, blocks, 128).transpose(1, 0, 2)
    theirs = (
        ghosts.reshape(8, 5, edge_blocks, 128)
        .transpose(0, 2, 1, 3)
        .reshape(8 * edge_blocks, 5, 128)
    )
    return jnp.concatenate([mine, theirs], axis=0)


def contact_batch(table, lists, valid, blocks, edge_blocks):
    source = lists[1]
    neighbour = source - (source > 4).astype(jnp.int32)
    partner = jnp.where(source == 4, lists[2], blocks + neighbour * edge_blocks + lists[2])
    forces = pair_forces(table[lists[0]], table[partner])
    forces = jnp.where(valid[:, None, None], forces, 0.0)
    onehot = (lists[0][:, None] == jnp.arange(blocks, dtype=jnp.int32)[None, :]).astype(jnp.float32)
    return jnp.einsum("pn,pcf->ncf", onehot, forces, precision=lax.Precision.HIGHEST)


def split_three(x):
    high = x.astype(jnp.bfloat16)
    rest = x - high.astype(jnp.float32)
    middle = rest.astype(jnp.bfloat16)
    low = (rest - middle.astype(jnp.float32)).astype(jnp.bfloat16)
    return high, middle, low


def exact_select(parts, onehot):
    high, middle, low = (jnp.dot(p, onehot, preferred_element_type=jnp.float32) for p in parts)
    return (high + middle) + low


def sample_kernel(window_ref, rows_ref, cols_ref, out_ref):
    window_rows, window_cols = window_ref.shape[1:]
    floes = rows_ref.shape[1]
    onehot = (
        lax.broadcasted_iota(jnp.int32, (window_rows, floes), 0) == rows_ref[...]
    ).astype(jnp.bfloat16)
    pick = lax.broadcasted_iota(jnp.int32, (window_cols, floes), 0) == cols_ref[...]
    for channel in range(window_ref.shape[0]):
        picked = exact_select(split_three(window_ref[channel].T), onehot)
        out_ref[channel : channel + 1, :] = jnp.sum(
            jnp.where(pick, picked, 0.0), axis=0, keepdims=True
        )


def sample_surface(window, rows, cols):
    return pl.pallas_call(
        sample_kernel,
        out_shape=jax.ShapeDtypeStruct((window.shape[0], rows.shape[1]), jnp.float32),
    )(window, rows, cols)


def gather_kernel(state_ref, radius_ref, mass_ref, polygon_ref, index_ref, out_ref, head_ref):
    floes = state_ref.shape[1]
    slots = index_ref.shape[1]
    head_ref[...] = jnp.zeros_like(head_ref)
    head_ref[0:4, :] = state_ref[...]
    head_ref[4:5, :] = radius_ref[...]
    head_ref[5:6, :] = mass_ref[...]
    head = split_three(head_ref[...])
    polygon = split_three(polygon_ref[...])
    rows = head_ref.shape[0]
    for way in range(index_ref.shape[0]):
        onehot = (
            lax.broadcasted_iota(jnp.int32, (floes, slots), 0) == index_ref[way : way + 1, :]
        ).astype(jnp.bfloat16)
        out_ref[way, 0:rows, :] = exact_select(head, onehot)
        out_ref[way, rows:, :] = exact_select(polygon, onehot)


def gather_records(state, radius, mass, polygon, index):
    rows = 8 + polygon.shape[0]
    return pl.pallas_call(
        gather_kernel,
        out_shape=jax.ShapeDtypeStruct((index.shape[0], rows, index.shape[1]), jnp.float32),
        scratch_shapes=[pltpu.VMEM((8, state.shape[1]), jnp.float32)],
    )(state, radius, mass, polygon, index)


def exchange(low, high, axis):
    size = lax.axis_size(axis)
    up = [(i, i + 1) for i in range(size - 1)]
    down = [(i + 1, i) for i in range(size - 1)]
    from_previous = lax.ppermute(high, axis, up)
    from_next = lax.ppermute(low, axis, down)
    return from_previous, from_next


def shards(
    ocean_velocity,
    wind_stress,
    level_counts,
    floe_position,
    floe_velocity,
    floe_radius,
    floe_mass,
    floe_polygon,
    remap_cells,
    contact_count,
    contact_list,
    move_index,
    move_count,
):
    columns = ("sec", "gy")
    comps, levels_here, rows_here, cols_here = ocean_velocity.shape
    halo = OSTEPS
    position = floe_position[0, 0]
    velocity = floe_velocity[0, 0]
    radius = floe_radius[0, 0]
    mass = floe_mass[0, 0]
    cells = remap_cells[0, 0]
    floes = position.shape[1]
    blocks = floes // 128
    record = jnp.concatenate([position, velocity, radius[None]], axis=0)
    edge = record[:, : GHOST * 128]
    edge_size = edge.size

    fields = jnp.concatenate(
        [
            ocean_velocity.reshape(comps * levels_here, rows_here, cols_here),
            wind_stress,
            level_counts.astype(jnp.float32)[None],
        ],
        axis=0,
    )
    channels = fields.shape[0]
    row_strip = channels * halo * cols_here
    low = jnp.concatenate([fields[:, :halo].reshape(-1), edge.reshape(-1)])
    high = jnp.concatenate([fields[:, -halo:].reshape(-1), edge.reshape(-1)])
    above, below = exchange(low, high, "gx")
    extended = jnp.concatenate(
        [
            above[:row_strip].reshape(channels, halo, cols_here),
            fields,
            below[:row_strip].reshape(channels, halo, cols_here),
        ],
        axis=1,
    )
    ghost_column = jnp.stack(
        [above[row_strip:].reshape(edge.shape), edge, below[row_strip:].reshape(edge.shape)]
    )
    ext_rows = rows_here + 2 * halo
    col_strip = channels * ext_rows * halo
    low = jnp.concatenate([extended[:, :, :halo].reshape(-1), ghost_column.reshape(-1)])
    high = jnp.concatenate([extended[:, :, -halo:].reshape(-1), ghost_column.reshape(-1)])
    left, right = exchange(low, high, columns)
    extended = jnp.concatenate(
        [
            left[:col_strip].reshape(channels, ext_rows, halo),
            extended,
            right[:col_strip].reshape(channels, ext_rows, halo),
        ],
        axis=2,
    )
    ghost_left = left[col_strip:].reshape(3, *edge.shape)
    ghost_right = right[col_strip:].reshape(3, *edge.shape)
    beside = [ghost_left, ghost_column, ghost_right]
    ghosts = jnp.stack([beside[p % 3][p // 3] for p in PLACES])

    ext_cols = cols_here + 2 * halo
    counts_ext = extended[-1]
    wet = (jnp.arange(levels_here, dtype=jnp.float32)[:, None, None] < counts_ext[None]).astype(
        jnp.float32
    )
    wind_ext = extended[comps * levels_here : comps * levels_here + 2]
    flow = extended[: comps * levels_here].reshape(comps, levels_here, ext_rows, ext_cols) * wet[None]
    for substep in range(OSTEPS):
        padded = jnp.pad(flow, ((0, 0), (0, 0), (1, 1), (1, 1)))
        flow = ocean_substep(flow, padded, wet, wind_ext)
    flow = flow[:, :, halo : halo + rows_here, halo : halo + cols_here]

    table = block_table(record, ghosts)
    surface = jnp.stack([flow[0, 0], flow[1, 0], wind_stress[0], wind_stress[1]])
    margin = rows_here // 2
    from_above, from_below = exchange(surface[:, :margin], surface[:, -margin:], "gx")
    near = jnp.concatenate([from_above, surface, from_below], axis=1)
    first_row = lax.axis_index("gx") * rows_here - margin
    sampled = sample_surface(
        near,
        (cells // cols_here - first_row)[None],
        (cells % cols_here)[None],
    )
    lists = contact_list[0, 0]
    count = contact_count[0, 0]
    valid = jnp.arange(lists.shape[1], dtype=jnp.int32) < count
    contact = contact_batch(table, lists, valid, blocks, GHOST)
    contact = contact.transpose(1, 0, 2).reshape(2, floes)
    area = math.pi * radius * radius
    relative = sampled[0:2] - velocity
    speed = jnp.sqrt(jnp.sum(relative * relative, axis=0, keepdims=True))
    total = contact + area[None] * (WATER_DRAG * speed * relative + AIR_GAIN * sampled[2:4])
    new_velocity = velocity + ICE_STEP * total / mass[None]
    new_position = position + ICE_STEP * new_velocity
    floe_next = jnp.concatenate([new_position, new_velocity], axis=0)
    leaving = move_index[0, 0]
    capacity = leaving.shape[1]
    valid_slots = jnp.arange(capacity, dtype=jnp.int32)[None, :] < move_count[0, 0][:, None]
    outgoing = gather_records(
        floe_next, radius[None], mass[None], floe_polygon[0, 0], jnp.where(valid_slots, leaving, -1)
    )
    from_above, from_below = exchange(outgoing[0:3], outgoing[5:8], "gx")
    heading_left = jnp.stack([from_below[0], outgoing[3], from_above[0]])
    heading_right = jnp.stack([from_below[2], outgoing[4], from_above[2]])
    from_left, from_right = exchange(heading_left, heading_right, columns)
    arrivals = jnp.stack(
        [
            from_right[0],
            from_below[1],
            from_left[0],
            from_right[1],
            from_left[1],
            from_right[2],
            from_above[1],
            from_left[2],
        ]
    )
    arrivals = jnp.concatenate([arrivals[:, 0:6], arrivals[:, 8:]], axis=1)
    return (flow, floe_next[None, None], arrivals[None, None])


def solution(mesh):
    return jax.shard_map(
        shards,
        mesh=mesh,
        in_specs=(
            P(None, None, "gx", ("sec", "gy")),
            P(None, "gx", ("sec", "gy")),
            P("gx", ("sec", "gy")),
            P("gx", ("sec", "gy"), None, None),
            P("gx", ("sec", "gy"), None, None),
            P("gx", ("sec", "gy"), None),
            P("gx", ("sec", "gy"), None),
            P("gx", ("sec", "gy"), None, None),
            P("gx", ("sec", "gy"), None),
            P("gx", ("sec", "gy")),
            P("gx", ("sec", "gy"), None, None),
            P("gx", ("sec", "gy"), None, None),
            P("gx", ("sec", "gy"), None),
        ),
        out_specs=(
            P(None, None, "gx", ("sec", "gy")),
            P("gx", ("sec", "gy"), None, None),
            P("gx", ("sec", "gy"), None, None, None),
        ),
        check_vma=False,
    )
```

```python
import math

import jax
import jax.numpy as jnp
from jax import lax
from jax.experimental import pallas as pl
from jax.experimental.pallas import tpu as pltpu
from jax.sharding import PartitionSpec as P

OSTEPS = 4
GHOST = 4


SOFTEN = 0.1
STIFFNESS = 0.1
DAMPING = 0.05
VERT_MIX = 0.15
CORIOLIS = 0.1
SURFACE_GAIN = 0.25
WATER_DRAG = 0.1
AIR_GAIN = 0.2
ICE_STEP = 0.5
PLACES = (0, 1, 2, 3, 5, 6, 7, 8)


def with_halo(array, sides, width):
    for axis, dim in sides:
        size, length = (lax.axis_size(axis), array.shape[dim])
        up = [(i, (i + 1) % size) for i in range(size - 1)]
        down = [(j, i) for i, j in up]
        last = lax.slice_in_dim(array, length - width, length, axis=dim)
        leading = lax.slice_in_dim(array, 0, width, axis=dim)
        before = lax.ppermute(last, axis, up)
        after = lax.ppermute(leading, axis, down)
        array = jnp.concatenate([before, array, after], axis=dim)
    return array


def ocean_substep(flow, padded, wet, wind):
    levels_here = flow.shape[1]
    lap = (
        padded[:, :, :-2, 1:-1]
        + padded[:, :, 2:, 1:-1]
        + padded[:, :, 1:-1, :-2]
        + padded[:, :, 1:-1, 2:]
        - 4.0 * flow
    )
    depth = jnp.arange(levels_here, dtype=jnp.float32)
    horizontal = (0.15 - 0.05 * depth / levels_here)[None, :, None, None]
    flux = VERT_MIX * (flow[:, 1:] - flow[:, :-1]) * wet[None, 1:]
    empty = jnp.zeros_like(flow[:, :1])
    vert = jnp.concatenate([flux, empty], axis=1) - jnp.concatenate([empty, flux], axis=1)
    turning = jnp.stack([CORIOLIS * flow[1], -CORIOLIS * flow[0]])
    surface = jnp.concatenate([SURFACE_GAIN * wind[:, None], jnp.zeros_like(flow[:, 1:])], axis=1)
    return (flow + horizontal * lap + vert + turning + surface) * wet[None]


def pair_forces(first, second):
    own = first[:, :, None, :]
    other = second[:, :, :, None]
    delta_x = own[:, 0] - other[:, 0]
    delta_y = own[:, 1] - other[:, 1]
    inverse = lax.rsqrt(delta_x * delta_x + delta_y * delta_y + SOFTEN * SOFTEN)
    distance = (delta_x * delta_x + delta_y * delta_y + SOFTEN * SOFTEN) * inverse
    reach = own[:, 4] + other[:, 4]
    intersection = jnp.maximum(reach - distance, 0.0)
    reduced = own[:, 4] * other[:, 4] / reach
    normal_x = delta_x * inverse
    normal_y = delta_y * inverse
    closing = (own[:, 2] - other[:, 2]) * normal_x + (own[:, 3] - other[:, 3]) * normal_y
    magnitude = intersection * reduced * (STIFFNESS - DAMPING * closing)
    return jnp.stack(
        [jnp.sum(magnitude * normal_x, axis=1), jnp.sum(magnitude * normal_y, axis=1)], axis=1
    )


def block_table(own, ghosts):
    blocks = own.shape[1] // 128
    edge_blocks = ghosts.shape[2] // 128
    mine = own.reshape(5, blocks, 128).transpose(1, 0, 2)
    theirs = (
        ghosts.reshape(8, 5, edge_blocks, 128)
        .transpose(0, 2, 1, 3)
        .reshape(8 * edge_blocks, 5, 128)
    )
    return jnp.concatenate([mine, theirs], axis=0)


def contact_batch(table, lists, valid, blocks, edge_blocks):
    source = lists[1]
    neighbour = source - (source > 4).astype(jnp.int32)
    partner = jnp.where(source == 4, lists[2], blocks + neighbour * edge_blocks + lists[2])
    forces = pair_forces(table[lists[0]], table[partner])
    forces = jnp.where(valid[:, None, None], forces, 0.0)
    onehot = (lists[0][:, None] == jnp.arange(blocks, dtype=jnp.int32)[None, :]).astype(jnp.float32)
    return jnp.einsum("pn,pcf->ncf", onehot, forces, precision=lax.Precision.HIGHEST)


def split_three(x):
    high = x.astype(jnp.bfloat16)
    rest = x - high.astype(jnp.float32)
    middle = rest.astype(jnp.bfloat16)
    low = (rest - middle.astype(jnp.float32)).astype(jnp.bfloat16)
    return high, middle, low


def exact_select(parts, onehot):
    high, middle, low = (jnp.dot(p, onehot, preferred_element_type=jnp.float32) for p in parts)
    return (high + middle) + low


def sample_kernel(window_ref, rows_ref, cols_ref, out_ref):
    window_rows, window_cols = window_ref.shape[1:]
    floes = rows_ref.shape[1]
    onehot = (
        lax.broadcasted_iota(jnp.int32, (window_rows, floes), 0) == rows_ref[...]
    ).astype(jnp.bfloat16)
    pick = lax.broadcasted_iota(jnp.int32, (window_cols, floes), 0) == cols_ref[...]
    for channel in range(window_ref.shape[0]):
        picked = exact_select(split_three(window_ref[channel].T), onehot)
        out_ref[channel : channel + 1, :] = jnp.sum(
            jnp.where(pick, picked, 0.0), axis=0, keepdims=True
        )


def sample_surface(window, rows, cols):
    return pl.pallas_call(
        sample_kernel,
        out_shape=jax.ShapeDtypeStruct((window.shape[0], rows.shape[1]), jnp.float32),
    )(window, rows, cols)


def gather_kernel(state_ref, radius_ref, mass_ref, polygon_ref, index_ref, out_ref, head_ref):
    floes = state_ref.shape[1]
    slots = index_ref.shape[1]
    head_ref[...] = jnp.zeros_like(head_ref)
    head_ref[0:4, :] = state_ref[...]
    head_ref[4:5, :] = radius_ref[...]
    head_ref[5:6, :] = mass_ref[...]
    head = split_three(head_ref[...])
    polygon = split_three(polygon_ref[...])
    rows = head_ref.shape[0]
    for way in range(index_ref.shape[0]):
        onehot = (
            lax.broadcasted_iota(jnp.int32, (floes, slots), 0) == index_ref[way : way + 1, :]
        ).astype(jnp.bfloat16)
        out_ref[way, 0:rows, :] = exact_select(head, onehot)
        out_ref[way, rows:, :] = exact_select(polygon, onehot)


def gather_records(state, radius, mass, polygon, index):
    rows = 8 + polygon.shape[0]
    return pl.pallas_call(
        gather_kernel,
        out_shape=jax.ShapeDtypeStruct((index.shape[0], rows, index.shape[1]), jnp.float32),
        scratch_shapes=[pltpu.VMEM((8, state.shape[1]), jnp.float32)],
    )(state, radius, mass, polygon, index)


def exchange(low, high, axis):
    size = lax.axis_size(axis)
    up = [(i, i + 1) for i in range(size - 1)]
    down = [(i + 1, i) for i in range(size - 1)]
    from_previous = lax.ppermute(high, axis, up)
    from_next = lax.ppermute(low, axis, down)
    return from_previous, from_next


def shards(
    ocean_velocity,
    wind_stress,
    level_counts,
    floe_position,
    floe_velocity,
    floe_radius,
    floe_mass,
    floe_polygon,
    remap_cells,
    contact_count,
    contact_list,
    move_index,
    move_count,
):
    columns = ("sec", "gy")
    comps, levels_here, rows_here, cols_here = ocean_velocity.shape
    halo = OSTEPS
    position = floe_position[0, 0]
    velocity = floe_velocity[0, 0]
    radius = floe_radius[0, 0]
    mass = floe_mass[0, 0]
    cells = remap_cells[0, 0]
    floes = position.shape[1]
    blocks = floes // 128
    record = jnp.concatenate([position, velocity, radius[None]], axis=0)
    edge = record[:, : GHOST * 128]
    edge_size = edge.size

    fields = jnp.concatenate(
        [
            ocean_velocity.reshape(comps * levels_here, rows_here, cols_here),
            wind_stress,
            level_counts.astype(jnp.float32)[None],
        ],
        axis=0,
    )
    channels = fields.shape[0]
    row_strip = channels * halo * cols_here
    low = jnp.concatenate([fields[:, :halo].reshape(-1), edge.reshape(-1)])
    high = jnp.concatenate([fields[:, -halo:].reshape(-1), edge.reshape(-1)])
    above, below = exchange(low, high, "gx")
    extended = jnp.concatenate(
        [
            above[:row_strip].reshape(channels, halo, cols_here),
            fields,
            below[:row_strip].reshape(channels, halo, cols_here),
        ],
        axis=1,
    )
    ghost_column = jnp.stack(
        [above[row_strip:].reshape(edge.shape), edge, below[row_strip:].reshape(edge.shape)]
    )
    ext_rows = rows_here + 2 * halo
    col_strip = channels * ext_rows * halo
    low = jnp.concatenate([extended[:, :, :halo].reshape(-1), ghost_column.reshape(-1)])
    high = jnp.concatenate([extended[:, :, -halo:].reshape(-1), ghost_column.reshape(-1)])
    left, right = exchange(low, high, columns)
    extended = jnp.concatenate(
        [
            left[:col_strip].reshape(channels, ext_rows, halo),
            extended,
            right[:col_strip].reshape(channels, ext_rows, halo),
        ],
        axis=2,
    )
    ghost_left = left[col_strip:].reshape(3, *edge.shape)
    ghost_right = right[col_strip:].reshape(3, *edge.shape)
    beside = [ghost_left, ghost_column, ghost_right]
    ghosts = jnp.stack([beside[p % 3][p // 3] for p in PLACES])

    ext_cols = cols_here + 2 * halo
    counts_ext = extended[-1]
    wet = (jnp.arange(levels_here, dtype=jnp.float32)[:, None, None] < counts_ext[None]).astype(
        jnp.float32
    )
    wind_ext = extended[comps * levels_here : comps * levels_here + 2]
    flow = extended[: comps * levels_here].reshape(comps, levels_here, ext_rows, ext_cols) * wet[None]
    for substep in range(OSTEPS):
        padded = jnp.pad(flow, ((0, 0), (0, 0), (1, 1), (1, 1)))
        flow = ocean_substep(flow, padded, wet, wind_ext)
    flow = flow[:, :, halo : halo + rows_here, halo : halo + cols_here]

    table = block_table(record, ghosts)
    surface = jnp.stack([flow[0, 0], flow[1, 0], wind_stress[0], wind_stress[1]])
    margin = rows_here // 2
    from_above, from_below = exchange(surface[:, :margin], surface[:, -margin:], "gx")
    near = jnp.concatenate([from_above, surface, from_below], axis=1)
    first_row = lax.axis_index("gx") * rows_here - margin
    sampled = sample_surface(
        near,
        (cells // cols_here - first_row)[None],
        (cells % cols_here)[None],
    )
    lists = contact_list[0, 0]
    count = contact_count[0, 0]
    slots = lists.shape[1]
    batch = math.gcd(slots, 32)
    rounds = (count + batch - 1) // batch

    def accumulate(turn, total):
        start = turn * batch
        group = lax.dynamic_slice_in_dim(lists, start, batch, 1)
        valid = start + jnp.arange(batch, dtype=jnp.int32) < count
        return total + contact_batch(table, group, valid, blocks, GHOST)

    contact = lax.fori_loop(0, rounds, accumulate, jnp.zeros((blocks, 2, 128), jnp.float32))
    contact = contact.transpose(1, 0, 2).reshape(2, floes)
    area = math.pi * radius * radius
    relative = sampled[0:2] - velocity
    speed = jnp.sqrt(jnp.sum(relative * relative, axis=0, keepdims=True))
    total = contact + area[None] * (WATER_DRAG * speed * relative + AIR_GAIN * sampled[2:4])
    new_velocity = velocity + ICE_STEP * total / mass[None]
    new_position = position + ICE_STEP * new_velocity
    floe_next = jnp.concatenate([new_position, new_velocity], axis=0)
    leaving = move_index[0, 0]
    capacity = leaving.shape[1]
    valid_slots = jnp.arange(capacity, dtype=jnp.int32)[None, :] < move_count[0, 0][:, None]
    outgoing = gather_records(
        floe_next, radius[None], mass[None], floe_polygon[0, 0], jnp.where(valid_slots, leaving, -1)
    )
    from_above, from_below = exchange(outgoing[0:3], outgoing[5:8], "gx")
    heading_left = jnp.stack([from_below[0], outgoing[3], from_above[0]])
    heading_right = jnp.stack([from_below[2], outgoing[4], from_above[2]])
    from_left, from_right = exchange(heading_left, heading_right, columns)
    arrivals = jnp.stack(
        [
            from_right[0],
            from_below[1],
            from_left[0],
            from_right[1],
            from_left[1],
            from_right[2],
            from_above[1],
            from_left[2],
        ]
    )
    arrivals = jnp.concatenate([arrivals[:, 0:6], arrivals[:, 8:]], axis=1)
    return (flow, floe_next[None, None], arrivals[None, None])


def solution(mesh):
    return jax.shard_map(
        shards,
        mesh=mesh,
        in_specs=(
            P(None, None, "gx", ("sec", "gy")),
            P(None, "gx", ("sec", "gy")),
            P("gx", ("sec", "gy")),
            P("gx", ("sec", "gy"), None, None),
            P("gx", ("sec", "gy"), None, None),
            P("gx", ("sec", "gy"), None),
            P("gx", ("sec", "gy"), None),
            P("gx", ("sec", "gy"), None, None),
            P("gx", ("sec", "gy"), None),
            P("gx", ("sec", "gy")),
            P("gx", ("sec", "gy"), None, None),
            P("gx", ("sec", "gy"), None, None),
            P("gx", ("sec", "gy"), None),
        ),
        out_specs=(
            P(None, None, "gx", ("sec", "gy")),
            P("gx", ("sec", "gy"), None, None),
            P("gx", ("sec", "gy"), None, None, None),
        ),
        check_vma=False,
    )
```

```python
import math

import jax
import jax.numpy as jnp
from jax import lax
from jax.experimental import pallas as pl
from jax.experimental.pallas import tpu as pltpu
from jax.sharding import PartitionSpec as P

OSTEPS = 4
GHOST = 4


SOFTEN = 0.1
STIFFNESS = 0.1
DAMPING = 0.05
VERT_MIX = 0.15
CORIOLIS = 0.1
SURFACE_GAIN = 0.25
WATER_DRAG = 0.1
AIR_GAIN = 0.2
ICE_STEP = 0.5
PLACES = (0, 1, 2, 3, 5, 6, 7, 8)


def with_halo(array, sides, width):
    for axis, dim in sides:
        size, length = (lax.axis_size(axis), array.shape[dim])
        up = [(i, (i + 1) % size) for i in range(size - 1)]
        down = [(j, i) for i, j in up]
        last = lax.slice_in_dim(array, length - width, length, axis=dim)
        leading = lax.slice_in_dim(array, 0, width, axis=dim)
        before = lax.ppermute(last, axis, up)
        after = lax.ppermute(leading, axis, down)
        array = jnp.concatenate([before, array, after], axis=dim)
    return array


def ocean_substep(flow, padded, wet, wind):
    levels_here = flow.shape[1]
    lap = (
        padded[:, :, :-2, 1:-1]
        + padded[:, :, 2:, 1:-1]
        + padded[:, :, 1:-1, :-2]
        + padded[:, :, 1:-1, 2:]
        - 4.0 * flow
    )
    depth = jnp.arange(levels_here, dtype=jnp.float32)
    horizontal = (0.15 - 0.05 * depth / levels_here)[None, :, None, None]
    flux = VERT_MIX * (flow[:, 1:] - flow[:, :-1]) * wet[None, 1:]
    empty = jnp.zeros_like(flow[:, :1])
    vert = jnp.concatenate([flux, empty], axis=1) - jnp.concatenate([empty, flux], axis=1)
    turning = jnp.stack([CORIOLIS * flow[1], -CORIOLIS * flow[0]])
    surface = jnp.concatenate([SURFACE_GAIN * wind[:, None], jnp.zeros_like(flow[:, 1:])], axis=1)
    return (flow + horizontal * lap + vert + turning + surface) * wet[None]


def pair_forces(first, second):
    own = first[:, :, None, :]
    other = second[:, :, :, None]
    delta_x = own[:, 0] - other[:, 0]
    delta_y = own[:, 1] - other[:, 1]
    inverse = lax.rsqrt(delta_x * delta_x + delta_y * delta_y + SOFTEN * SOFTEN)
    distance = (delta_x * delta_x + delta_y * delta_y + SOFTEN * SOFTEN) * inverse
    reach = own[:, 4] + other[:, 4]
    intersection = jnp.maximum(reach - distance, 0.0)
    reduced = own[:, 4] * other[:, 4] / reach
    normal_x = delta_x * inverse
    normal_y = delta_y * inverse
    closing = (own[:, 2] - other[:, 2]) * normal_x + (own[:, 3] - other[:, 3]) * normal_y
    magnitude = intersection * reduced * (STIFFNESS - DAMPING * closing)
    return jnp.stack(
        [jnp.sum(magnitude * normal_x, axis=1), jnp.sum(magnitude * normal_y, axis=1)], axis=1
    )


def block_table(own, ghosts):
    blocks = own.shape[1] // 128
    edge_blocks = ghosts.shape[2] // 128
    mine = own.reshape(5, blocks, 128).transpose(1, 0, 2)
    theirs = (
        ghosts.reshape(8, 5, edge_blocks, 128)
        .transpose(0, 2, 1, 3)
        .reshape(8 * edge_blocks, 5, 128)
    )
    return jnp.concatenate([mine, theirs], axis=0)


def contact_batch(table, lists, valid, blocks, edge_blocks):
    source = lists[1]
    neighbour = source - (source > 4).astype(jnp.int32)
    partner = jnp.where(source == 4, lists[2], blocks + neighbour * edge_blocks + lists[2])
    forces = pair_forces(table[lists[0]], table[partner])
    forces = jnp.where(valid[:, None, None], forces, 0.0)
    onehot = (lists[0][:, None] == jnp.arange(blocks, dtype=jnp.int32)[None, :]).astype(jnp.float32)
    return jnp.einsum("pn,pcf->ncf", onehot, forces, precision=lax.Precision.HIGHEST)


def split_three(x):
    high = x.astype(jnp.bfloat16)
    rest = x - high.astype(jnp.float32)
    middle = rest.astype(jnp.bfloat16)
    low = (rest - middle.astype(jnp.float32)).astype(jnp.bfloat16)
    return high, middle, low


def exact_select(parts, onehot):
    high, middle, low = (jnp.dot(p, onehot, preferred_element_type=jnp.float32) for p in parts)
    return (high + middle) + low


def sample_kernel(window_ref, rows_ref, cols_ref, out_ref):
    window_rows, window_cols = window_ref.shape[1:]
    floes = rows_ref.shape[1]
    onehot = (
        lax.broadcasted_iota(jnp.int32, (window_rows, floes), 0) == rows_ref[...]
    ).astype(jnp.bfloat16)
    pick = lax.broadcasted_iota(jnp.int32, (window_cols, floes), 0) == cols_ref[...]
    for channel in range(window_ref.shape[0]):
        picked = exact_select(split_three(window_ref[channel].T), onehot)
        out_ref[channel : channel + 1, :] = jnp.sum(
            jnp.where(pick, picked, 0.0), axis=0, keepdims=True
        )


def sample_surface(window, rows, cols):
    return pl.pallas_call(
        sample_kernel,
        out_shape=jax.ShapeDtypeStruct((window.shape[0], rows.shape[1]), jnp.float32),
    )(window, rows, cols)


def gather_kernel(state_ref, radius_ref, mass_ref, polygon_ref, index_ref, out_ref, head_ref):
    floes = state_ref.shape[1]
    slots = index_ref.shape[1]
    head_ref[...] = jnp.zeros_like(head_ref)
    head_ref[0:4, :] = state_ref[...]
    head_ref[4:5, :] = radius_ref[...]
    head_ref[5:6, :] = mass_ref[...]
    head = split_three(head_ref[...])
    polygon = split_three(polygon_ref[...])
    rows = head_ref.shape[0]
    for way in range(index_ref.shape[0]):
        onehot = (
            lax.broadcasted_iota(jnp.int32, (floes, slots), 0) == index_ref[way : way + 1, :]
        ).astype(jnp.bfloat16)
        out_ref[way, 0:rows, :] = exact_select(head, onehot)
        out_ref[way, rows:, :] = exact_select(polygon, onehot)


def gather_records(state, radius, mass, polygon, index):
    rows = 8 + polygon.shape[0]
    return pl.pallas_call(
        gather_kernel,
        out_shape=jax.ShapeDtypeStruct((index.shape[0], rows, index.shape[1]), jnp.float32),
        scratch_shapes=[pltpu.VMEM((8, state.shape[1]), jnp.float32)],
    )(state, radius, mass, polygon, index)


def exchange(low, high, axis):
    size = lax.axis_size(axis)
    up = [(i, i + 1) for i in range(size - 1)]
    down = [(i + 1, i) for i in range(size - 1)]
    from_previous = lax.ppermute(high, axis, up)
    from_next = lax.ppermute(low, axis, down)
    return from_previous, from_next


def send_to(array, row_step, col_step):
    sections, rows, cols = lax.axis_size("sec"), lax.axis_size("gx"), lax.axis_size("gy")

    def flat(row, col):
        return (col // cols) * rows * cols + row * cols + col % cols

    width = sections * cols
    pairs = [
        (flat(r, c), flat(r + row_step, c + col_step))
        for r in range(rows)
        for c in range(width)
        if 0 <= r + row_step < rows and 0 <= c + col_step < width
    ]
    return lax.ppermute(array, ("sec", "gx", "gy"), pairs)


def shards(
    ocean_velocity,
    wind_stress,
    level_counts,
    floe_position,
    floe_velocity,
    floe_radius,
    floe_mass,
    floe_polygon,
    remap_cells,
    contact_count,
    contact_list,
    move_index,
    move_count,
):
    columns = ("sec", "gy")
    comps, levels_here, rows_here, cols_here = ocean_velocity.shape
    halo = OSTEPS
    position = floe_position[0, 0]
    velocity = floe_velocity[0, 0]
    radius = floe_radius[0, 0]
    mass = floe_mass[0, 0]
    cells = remap_cells[0, 0]
    floes = position.shape[1]
    blocks = floes // 128
    record = jnp.concatenate([position, velocity, radius[None]], axis=0)
    edge = record[:, : GHOST * 128]
    edge_size = edge.size

    fields = jnp.concatenate(
        [
            ocean_velocity.reshape(comps * levels_here, rows_here, cols_here),
            wind_stress,
            level_counts.astype(jnp.float32)[None],
        ],
        axis=0,
    )
    channels = fields.shape[0]
    row_strip = channels * halo * cols_here
    low = jnp.concatenate([fields[:, :halo].reshape(-1), edge.reshape(-1)])
    high = jnp.concatenate([fields[:, -halo:].reshape(-1), edge.reshape(-1)])
    above, below = exchange(low, high, "gx")
    extended = jnp.concatenate(
        [
            above[:row_strip].reshape(channels, halo, cols_here),
            fields,
            below[:row_strip].reshape(channels, halo, cols_here),
        ],
        axis=1,
    )
    ghost_column = jnp.stack(
        [above[row_strip:].reshape(edge.shape), edge, below[row_strip:].reshape(edge.shape)]
    )
    ext_rows = rows_here + 2 * halo
    col_strip = channels * ext_rows * halo
    low = jnp.concatenate([extended[:, :, :halo].reshape(-1), ghost_column.reshape(-1)])
    high = jnp.concatenate([extended[:, :, -halo:].reshape(-1), ghost_column.reshape(-1)])
    left, right = exchange(low, high, columns)
    extended = jnp.concatenate(
        [
            left[:col_strip].reshape(channels, ext_rows, halo),
            extended,
            right[:col_strip].reshape(channels, ext_rows, halo),
        ],
        axis=2,
    )
    ghost_left = left[col_strip:].reshape(3, *edge.shape)
    ghost_right = right[col_strip:].reshape(3, *edge.shape)
    beside = [ghost_left, ghost_column, ghost_right]
    ghosts = jnp.stack([beside[p % 3][p // 3] for p in PLACES])

    ext_cols = cols_here + 2 * halo
    counts_ext = extended[-1]
    wet = (jnp.arange(levels_here, dtype=jnp.float32)[:, None, None] < counts_ext[None]).astype(
        jnp.float32
    )
    wind_ext = extended[comps * levels_here : comps * levels_here + 2]
    flow = extended[: comps * levels_here].reshape(comps, levels_here, ext_rows, ext_cols) * wet[None]
    for substep in range(OSTEPS):
        padded = jnp.pad(flow, ((0, 0), (0, 0), (1, 1), (1, 1)))
        flow = ocean_substep(flow, padded, wet, wind_ext)
    flow = flow[:, :, halo : halo + rows_here, halo : halo + cols_here]

    table = block_table(record, ghosts)
    surface = jnp.stack([flow[0, 0], flow[1, 0], wind_stress[0], wind_stress[1]])
    margin = rows_here // 2
    from_above, from_below = exchange(surface[:, :margin], surface[:, -margin:], "gx")
    near = jnp.concatenate([from_above, surface, from_below], axis=1)
    first_row = lax.axis_index("gx") * rows_here - margin
    sampled = sample_surface(
        near,
        (cells // cols_here - first_row)[None],
        (cells % cols_here)[None],
    )
    lists = contact_list[0, 0]
    count = contact_count[0, 0]
    slots = lists.shape[1]
    batch = math.gcd(slots, 32)
    rounds = (count + batch - 1) // batch

    def accumulate(turn, total):
        start = turn * batch
        group = lax.dynamic_slice_in_dim(lists, start, batch, 1)
        valid = start + jnp.arange(batch, dtype=jnp.int32) < count
        return total + contact_batch(table, group, valid, blocks, GHOST)

    contact = lax.fori_loop(0, rounds, accumulate, jnp.zeros((blocks, 2, 128), jnp.float32))
    contact = contact.transpose(1, 0, 2).reshape(2, floes)
    area = math.pi * radius * radius
    relative = sampled[0:2] - velocity
    speed = jnp.sqrt(jnp.sum(relative * relative, axis=0, keepdims=True))
    total = contact + area[None] * (WATER_DRAG * speed * relative + AIR_GAIN * sampled[2:4])
    new_velocity = velocity + ICE_STEP * total / mass[None]
    new_position = position + ICE_STEP * new_velocity
    floe_next = jnp.concatenate([new_position, new_velocity], axis=0)
    leaving = move_index[0, 0]
    capacity = leaving.shape[1]
    valid_slots = jnp.arange(capacity, dtype=jnp.int32)[None, :] < move_count[0, 0][:, None]
    outgoing = gather_records(
        floe_next, radius[None], mass[None], floe_polygon[0, 0], jnp.where(valid_slots, leaving, -1)
    )
    arrivals = jnp.stack(
        [send_to(outgoing[way], PLACES[way] // 3 - 1, PLACES[way] % 3 - 1) for way in range(8)]
    )
    arrivals = jnp.concatenate([arrivals[:, 0:6], arrivals[:, 8:]], axis=1)
    return (flow, floe_next[None, None], arrivals[None, None])


def solution(mesh):
    return jax.shard_map(
        shards,
        mesh=mesh,
        in_specs=(
            P(None, None, "gx", ("sec", "gy")),
            P(None, "gx", ("sec", "gy")),
            P("gx", ("sec", "gy")),
            P("gx", ("sec", "gy"), None, None),
            P("gx", ("sec", "gy"), None, None),
            P("gx", ("sec", "gy"), None),
            P("gx", ("sec", "gy"), None),
            P("gx", ("sec", "gy"), None, None),
            P("gx", ("sec", "gy"), None),
            P("gx", ("sec", "gy")),
            P("gx", ("sec", "gy"), None, None),
            P("gx", ("sec", "gy"), None, None),
            P("gx", ("sec", "gy"), None),
        ),
        out_specs=(
            P(None, None, "gx", ("sec", "gy")),
            P("gx", ("sec", "gy"), None, None),
            P("gx", ("sec", "gy"), None, None, None),
        ),
        check_vma=False,
    )
```

```python
import math

import jax
import jax.numpy as jnp
from jax import lax
from jax.experimental import pallas as pl
from jax.experimental.pallas import tpu as pltpu
from jax.sharding import PartitionSpec as P

OSTEPS = 4
GHOST = 4


SOFTEN = 0.1
STIFFNESS = 0.1
DAMPING = 0.05
VERT_MIX = 0.15
CORIOLIS = 0.1
SURFACE_GAIN = 0.25
WATER_DRAG = 0.1
AIR_GAIN = 0.2
ICE_STEP = 0.5
PLACES = (0, 1, 2, 3, 5, 6, 7, 8)


def with_halo(array, sides, width):
    for axis, dim in sides:
        size, length = (lax.axis_size(axis), array.shape[dim])
        up = [(i, (i + 1) % size) for i in range(size - 1)]
        down = [(j, i) for i, j in up]
        last = lax.slice_in_dim(array, length - width, length, axis=dim)
        leading = lax.slice_in_dim(array, 0, width, axis=dim)
        before = lax.ppermute(last, axis, up)
        after = lax.ppermute(leading, axis, down)
        array = jnp.concatenate([before, array, after], axis=dim)
    return array


def ocean_substep(flow, padded, wet, wind):
    levels_here = flow.shape[1]
    lap = (
        padded[:, :, :-2, 1:-1]
        + padded[:, :, 2:, 1:-1]
        + padded[:, :, 1:-1, :-2]
        + padded[:, :, 1:-1, 2:]
        - 4.0 * flow
    )
    depth = jnp.arange(levels_here, dtype=jnp.float32)
    horizontal = (0.15 - 0.05 * depth / levels_here)[None, :, None, None]
    flux = VERT_MIX * (flow[:, 1:] - flow[:, :-1]) * wet[None, 1:]
    empty = jnp.zeros_like(flow[:, :1])
    vert = jnp.concatenate([flux, empty], axis=1) - jnp.concatenate([empty, flux], axis=1)
    turning = jnp.stack([CORIOLIS * flow[1], -CORIOLIS * flow[0]])
    surface = jnp.concatenate([SURFACE_GAIN * wind[:, None], jnp.zeros_like(flow[:, 1:])], axis=1)
    return (flow + horizontal * lap + vert + turning + surface) * wet[None]


def pair_forces(first, second):
    own = first[:, :, None, :]
    other = second[:, :, :, None]
    delta_x = own[:, 0] - other[:, 0]
    delta_y = own[:, 1] - other[:, 1]
    inverse = lax.rsqrt(delta_x * delta_x + delta_y * delta_y + SOFTEN * SOFTEN)
    distance = (delta_x * delta_x + delta_y * delta_y + SOFTEN * SOFTEN) * inverse
    reach = own[:, 4] + other[:, 4]
    intersection = jnp.maximum(reach - distance, 0.0)
    reduced = own[:, 4] * other[:, 4] / reach
    normal_x = delta_x * inverse
    normal_y = delta_y * inverse
    closing = (own[:, 2] - other[:, 2]) * normal_x + (own[:, 3] - other[:, 3]) * normal_y
    magnitude = intersection * reduced * (STIFFNESS - DAMPING * closing)
    return jnp.stack(
        [jnp.sum(magnitude * normal_x, axis=1), jnp.sum(magnitude * normal_y, axis=1)], axis=1
    )


def block_table(own, ghosts):
    blocks = own.shape[1] // 128
    edge_blocks = ghosts.shape[2] // 128
    mine = own.reshape(5, blocks, 128).transpose(1, 0, 2)
    theirs = (
        ghosts.reshape(8, 5, edge_blocks, 128)
        .transpose(0, 2, 1, 3)
        .reshape(8 * edge_blocks, 5, 128)
    )
    return jnp.concatenate([mine, theirs], axis=0)


def contact_batch(table, lists, valid, blocks, edge_blocks):
    source = lists[1]
    neighbour = source - (source > 4).astype(jnp.int32)
    partner = jnp.where(source == 4, lists[2], blocks + neighbour * edge_blocks + lists[2])
    forces = pair_forces(table[lists[0]], table[partner])
    forces = jnp.where(valid[:, None, None], forces, 0.0)
    onehot = (lists[0][:, None] == jnp.arange(blocks, dtype=jnp.int32)[None, :]).astype(jnp.float32)
    return jnp.einsum("pn,pcf->ncf", onehot, forces, precision=lax.Precision.HIGHEST)


def split_parts(x):
    high = x.astype(jnp.bfloat16).astype(jnp.float32)
    rest = x - high
    middle = rest.astype(jnp.bfloat16).astype(jnp.float32)
    low = (rest - middle).astype(jnp.bfloat16).astype(jnp.float32)
    return high, middle, low


def stacked_select(stack_ref, x, onehot):
    rows = x.shape[0]
    pitch = stack_ref.shape[0] // 3
    for part, value in enumerate(split_parts(x)):
        stack_ref[part * pitch : part * pitch + rows, :] = value
    picked = jnp.dot(
        stack_ref[...].astype(jnp.bfloat16), onehot, preferred_element_type=jnp.float32
    )
    return (picked[0:rows] + picked[pitch : pitch + rows]) + picked[2 * pitch : 2 * pitch + rows]


def sample_kernel(window_ref, rows_ref, cols_ref, out_ref, stack_ref):
    window_rows, window_cols = window_ref.shape[1:]
    floes = rows_ref.shape[1]
    onehot = (
        lax.broadcasted_iota(jnp.int32, (window_rows, floes), 0) == rows_ref[...]
    ).astype(jnp.bfloat16)
    pick = lax.broadcasted_iota(jnp.int32, (window_cols, floes), 0) == cols_ref[...]
    for channel in range(window_ref.shape[0]):
        picked = stacked_select(stack_ref, window_ref[channel].T, onehot)
        out_ref[channel : channel + 1, :] = jnp.sum(
            jnp.where(pick, picked, 0.0), axis=0, keepdims=True
        )


def sample_surface(window, rows, cols):
    return pl.pallas_call(
        sample_kernel,
        out_shape=jax.ShapeDtypeStruct((window.shape[0], rows.shape[1]), jnp.float32),
        scratch_shapes=[pltpu.VMEM((3 * window.shape[2], window.shape[1]), jnp.float32)],
    )(window, rows, cols)


def gather_kernel(state_ref, radius_ref, mass_ref, polygon_ref, index_ref, out_ref, record_ref, stack_ref):
    floes = state_ref.shape[1]
    slots = index_ref.shape[1]
    width = out_ref.shape[1]
    record_ref[...] = jnp.zeros_like(record_ref)
    stack_ref[...] = jnp.zeros_like(stack_ref)
    record_ref[0:4, :] = state_ref[...]
    record_ref[4:5, :] = radius_ref[...]
    record_ref[5:6, :] = mass_ref[...]
    record_ref[6:width, :] = polygon_ref[...]
    record = record_ref[...]
    for way in range(index_ref.shape[0]):
        onehot = (
            lax.broadcasted_iota(jnp.int32, (floes, slots), 0) == index_ref[way : way + 1, :]
        ).astype(jnp.bfloat16)
        out_ref[way] = stacked_select(stack_ref, record, onehot)[0:width]


def gather_records(state, radius, mass, polygon, index):
    width = 6 + polygon.shape[0]
    padded = -(-width // 16) * 16
    return pl.pallas_call(
        gather_kernel,
        out_shape=jax.ShapeDtypeStruct((index.shape[0], width, index.shape[1]), jnp.float32),
        scratch_shapes=[
            pltpu.VMEM((padded, state.shape[1]), jnp.float32),
            pltpu.VMEM((3 * padded, state.shape[1]), jnp.float32),
        ],
    )(state, radius, mass, polygon, index)


def exchange(low, high, axis):
    size = lax.axis_size(axis)
    up = [(i, i + 1) for i in range(size - 1)]
    down = [(i + 1, i) for i in range(size - 1)]
    from_previous = lax.ppermute(high, axis, up)
    from_next = lax.ppermute(low, axis, down)
    return from_previous, from_next


def shards(
    ocean_velocity,
    wind_stress,
    level_counts,
    floe_position,
    floe_velocity,
    floe_radius,
    floe_mass,
    floe_polygon,
    remap_cells,
    contact_count,
    contact_list,
    move_index,
    move_count,
):
    columns = ("sec", "gy")
    comps, levels_here, rows_here, cols_here = ocean_velocity.shape
    halo = OSTEPS
    position = floe_position[0, 0]
    velocity = floe_velocity[0, 0]
    radius = floe_radius[0, 0]
    mass = floe_mass[0, 0]
    cells = remap_cells[0, 0]
    floes = position.shape[1]
    blocks = floes // 128
    record = jnp.concatenate([position, velocity, radius[None]], axis=0)
    edge = record[:, : GHOST * 128]
    edge_size = edge.size

    fields = jnp.concatenate(
        [
            ocean_velocity.reshape(comps * levels_here, rows_here, cols_here),
            wind_stress,
            level_counts.astype(jnp.float32)[None],
        ],
        axis=0,
    )
    channels = fields.shape[0]
    row_strip = channels * halo * cols_here
    low = jnp.concatenate([fields[:, :halo].reshape(-1), edge.reshape(-1)])
    high = jnp.concatenate([fields[:, -halo:].reshape(-1), edge.reshape(-1)])
    above, below = exchange(low, high, "gx")
    extended = jnp.concatenate(
        [
            above[:row_strip].reshape(channels, halo, cols_here),
            fields,
            below[:row_strip].reshape(channels, halo, cols_here),
        ],
        axis=1,
    )
    ghost_column = jnp.stack(
        [above[row_strip:].reshape(edge.shape), edge, below[row_strip:].reshape(edge.shape)]
    )
    ext_rows = rows_here + 2 * halo
    col_strip = channels * ext_rows * halo
    low = jnp.concatenate([extended[:, :, :halo].reshape(-1), ghost_column.reshape(-1)])
    high = jnp.concatenate([extended[:, :, -halo:].reshape(-1), ghost_column.reshape(-1)])
    left, right = exchange(low, high, columns)
    extended = jnp.concatenate(
        [
            left[:col_strip].reshape(channels, ext_rows, halo),
            extended,
            right[:col_strip].reshape(channels, ext_rows, halo),
        ],
        axis=2,
    )
    ghost_left = left[col_strip:].reshape(3, *edge.shape)
    ghost_right = right[col_strip:].reshape(3, *edge.shape)
    beside = [ghost_left, ghost_column, ghost_right]
    ghosts = jnp.stack([beside[p % 3][p // 3] for p in PLACES])

    ext_cols = cols_here + 2 * halo
    counts_ext = extended[-1]
    wet = (jnp.arange(levels_here, dtype=jnp.float32)[:, None, None] < counts_ext[None]).astype(
        jnp.float32
    )
    wind_ext = extended[comps * levels_here : comps * levels_here + 2]
    flow = extended[: comps * levels_here].reshape(comps, levels_here, ext_rows, ext_cols) * wet[None]
    for substep in range(OSTEPS):
        padded = jnp.pad(flow, ((0, 0), (0, 0), (1, 1), (1, 1)))
        flow = ocean_substep(flow, padded, wet, wind_ext)
    flow = flow[:, :, halo : halo + rows_here, halo : halo + cols_here]

    table = block_table(record, ghosts)
    surface = jnp.stack([flow[0, 0], flow[1, 0], wind_stress[0], wind_stress[1]])
    margin = rows_here // 2
    from_above, from_below = exchange(surface[:, :margin], surface[:, -margin:], "gx")
    near = jnp.concatenate([from_above, surface, from_below], axis=1)
    first_row = lax.axis_index("gx") * rows_here - margin
    sampled = sample_surface(
        near,
        (cells // cols_here - first_row)[None],
        (cells % cols_here)[None],
    )
    lists = contact_list[0, 0]
    count = contact_count[0, 0]
    slots = lists.shape[1]
    batch = math.gcd(slots, 32)
    rounds = (count + batch - 1) // batch

    def accumulate(turn, total):
        start = turn * batch
        group = lax.dynamic_slice_in_dim(lists, start, batch, 1)
        valid = start + jnp.arange(batch, dtype=jnp.int32) < count
        return total + contact_batch(table, group, valid, blocks, GHOST)

    contact = lax.fori_loop(0, rounds, accumulate, jnp.zeros((blocks, 2, 128), jnp.float32))
    contact = contact.transpose(1, 0, 2).reshape(2, floes)
    area = math.pi * radius * radius
    relative = sampled[0:2] - velocity
    speed = jnp.sqrt(jnp.sum(relative * relative, axis=0, keepdims=True))
    total = contact + area[None] * (WATER_DRAG * speed * relative + AIR_GAIN * sampled[2:4])
    new_velocity = velocity + ICE_STEP * total / mass[None]
    new_position = position + ICE_STEP * new_velocity
    floe_next = jnp.concatenate([new_position, new_velocity], axis=0)
    leaving = move_index[0, 0]
    capacity = leaving.shape[1]
    valid_slots = jnp.arange(capacity, dtype=jnp.int32)[None, :] < move_count[0, 0][:, None]
    outgoing = gather_records(
        floe_next, radius[None], mass[None], floe_polygon[0, 0], jnp.where(valid_slots, leaving, -1)
    )
    from_above, from_below = exchange(outgoing[0:3], outgoing[5:8], "gx")
    heading_left = jnp.stack([from_below[0], outgoing[3], from_above[0]])
    heading_right = jnp.stack([from_below[2], outgoing[4], from_above[2]])
    from_left, from_right = exchange(heading_left, heading_right, columns)
    arrivals = jnp.stack(
        [
            from_right[0],
            from_below[1],
            from_left[0],
            from_right[1],
            from_left[1],
            from_right[2],
            from_above[1],
            from_left[2],
        ]
    )
    return (flow, floe_next[None, None], arrivals[None, None])


def solution(mesh):
    return jax.shard_map(
        shards,
        mesh=mesh,
        in_specs=(
            P(None, None, "gx", ("sec", "gy")),
            P(None, "gx", ("sec", "gy")),
            P("gx", ("sec", "gy")),
            P("gx", ("sec", "gy"), None, None),
            P("gx", ("sec", "gy"), None, None),
            P("gx", ("sec", "gy"), None),
            P("gx", ("sec", "gy"), None),
            P("gx", ("sec", "gy"), None, None),
            P("gx", ("sec", "gy"), None),
            P("gx", ("sec", "gy")),
            P("gx", ("sec", "gy"), None, None),
            P("gx", ("sec", "gy"), None, None),
            P("gx", ("sec", "gy"), None),
        ),
        out_specs=(
            P(None, None, "gx", ("sec", "gy")),
            P("gx", ("sec", "gy"), None, None),
            P("gx", ("sec", "gy"), None, None, None),
        ),
        check_vma=False,
    )
```

```python
import math

import jax
import jax.numpy as jnp
from jax import lax
from jax.experimental import pallas as pl
from jax.experimental.pallas import tpu as pltpu
from jax.sharding import PartitionSpec as P

OSTEPS = 4
GHOST = 4


SOFTEN = 0.1
STIFFNESS = 0.1
DAMPING = 0.05
VERT_MIX = 0.15
CORIOLIS = 0.1
SURFACE_GAIN = 0.25
WATER_DRAG = 0.1
AIR_GAIN = 0.2
ICE_STEP = 0.5
PLACES = (0, 1, 2, 3, 5, 6, 7, 8)


def with_halo(array, sides, width):
    for axis, dim in sides:
        size, length = (lax.axis_size(axis), array.shape[dim])
        up = [(i, (i + 1) % size) for i in range(size - 1)]
        down = [(j, i) for i, j in up]
        last = lax.slice_in_dim(array, length - width, length, axis=dim)
        leading = lax.slice_in_dim(array, 0, width, axis=dim)
        before = lax.ppermute(last, axis, up)
        after = lax.ppermute(leading, axis, down)
        array = jnp.concatenate([before, array, after], axis=dim)
    return array


def ocean_substep(flow, padded, wet, wind):
    levels_here = flow.shape[1]
    lap = (
        padded[:, :, :-2, 1:-1]
        + padded[:, :, 2:, 1:-1]
        + padded[:, :, 1:-1, :-2]
        + padded[:, :, 1:-1, 2:]
        - 4.0 * flow
    )
    depth = jnp.arange(levels_here, dtype=jnp.float32)
    horizontal = (0.15 - 0.05 * depth / levels_here)[None, :, None, None]
    flux = VERT_MIX * (flow[:, 1:] - flow[:, :-1]) * wet[None, 1:]
    empty = jnp.zeros_like(flow[:, :1])
    vert = jnp.concatenate([flux, empty], axis=1) - jnp.concatenate([empty, flux], axis=1)
    turning = jnp.stack([CORIOLIS * flow[1], -CORIOLIS * flow[0]])
    surface = jnp.concatenate([SURFACE_GAIN * wind[:, None], jnp.zeros_like(flow[:, 1:])], axis=1)
    return (flow + horizontal * lap + vert + turning + surface) * wet[None]


def pair_forces(first, second):
    own = first[:, :, None, :]
    other = second[:, :, :, None]
    delta_x = own[:, 0] - other[:, 0]
    delta_y = own[:, 1] - other[:, 1]
    inverse = lax.rsqrt(delta_x * delta_x + delta_y * delta_y + SOFTEN * SOFTEN)
    distance = (delta_x * delta_x + delta_y * delta_y + SOFTEN * SOFTEN) * inverse
    reach = own[:, 4] + other[:, 4]
    intersection = jnp.maximum(reach - distance, 0.0)
    reduced = own[:, 4] * other[:, 4] / reach
    normal_x = delta_x * inverse
    normal_y = delta_y * inverse
    closing = (own[:, 2] - other[:, 2]) * normal_x + (own[:, 3] - other[:, 3]) * normal_y
    magnitude = intersection * reduced * (STIFFNESS - DAMPING * closing)
    return jnp.stack(
        [jnp.sum(magnitude * normal_x, axis=1), jnp.sum(magnitude * normal_y, axis=1)], axis=1
    )


def block_table(own, ghosts):
    blocks = own.shape[1] // 128
    edge_blocks = ghosts.shape[2] // 128
    mine = own.reshape(5, blocks, 128).transpose(1, 0, 2)
    theirs = (
        ghosts.reshape(8, 5, edge_blocks, 128)
        .transpose(0, 2, 1, 3)
        .reshape(8 * edge_blocks, 5, 128)
    )
    return jnp.concatenate([mine, theirs], axis=0)


def contact_batch(table, lists, valid, blocks, edge_blocks):
    source = lists[1]
    neighbour = source - (source > 4).astype(jnp.int32)
    partner = jnp.where(source == 4, lists[2], blocks + neighbour * edge_blocks + lists[2])
    forces = pair_forces(table[lists[0]], table[partner])
    forces = jnp.where(valid[:, None, None], forces, 0.0)
    onehot = (lists[0][:, None] == jnp.arange(blocks, dtype=jnp.int32)[None, :]).astype(jnp.float32)
    return jnp.einsum("pn,pcf->ncf", onehot, forces, precision=lax.Precision.HIGHEST)


def split_parts(x):
    high = x.astype(jnp.bfloat16).astype(jnp.float32)
    rest = x - high
    middle = rest.astype(jnp.bfloat16).astype(jnp.float32)
    low = (rest - middle).astype(jnp.bfloat16).astype(jnp.float32)
    return high, middle, low


def stacked_select(stack_ref, x, onehot):
    rows = x.shape[0]
    pitch = stack_ref.shape[0] // 3
    for part, value in enumerate(split_parts(x)):
        stack_ref[part * pitch : part * pitch + rows, :] = value
    picked = jnp.dot(
        stack_ref[...].astype(jnp.bfloat16), onehot, preferred_element_type=jnp.float32
    )
    return (picked[0:rows] + picked[pitch : pitch + rows]) + picked[2 * pitch : 2 * pitch + rows]


def sample_kernel(window_ref, rows_ref, cols_ref, out_ref, stack_ref):
    window_rows, window_cols = window_ref.shape[1:]
    floes = rows_ref.shape[1]
    onehot = (
        lax.broadcasted_iota(jnp.int32, (window_rows, floes), 0) == rows_ref[...]
    ).astype(jnp.bfloat16)
    pick = lax.broadcasted_iota(jnp.int32, (window_cols, floes), 0) == cols_ref[...]
    for channel in range(window_ref.shape[0]):
        picked = stacked_select(stack_ref, window_ref[channel].T, onehot)
        out_ref[channel : channel + 1, :] = jnp.sum(
            jnp.where(pick, picked, 0.0), axis=0, keepdims=True
        )


def sample_surface(window, rows, cols):
    return pl.pallas_call(
        sample_kernel,
        out_shape=jax.ShapeDtypeStruct((window.shape[0], rows.shape[1]), jnp.float32),
        scratch_shapes=[pltpu.VMEM((3 * window.shape[2], window.shape[1]), jnp.float32)],
    )(window, rows, cols)


def gather_kernel(state_ref, radius_ref, mass_ref, polygon_ref, index_ref, out_ref, record_ref, stack_ref):
    floes = state_ref.shape[1]
    slots = index_ref.shape[1]
    width = out_ref.shape[1]
    record_ref[...] = jnp.zeros_like(record_ref)
    stack_ref[...] = jnp.zeros_like(stack_ref)
    record_ref[0:4, :] = state_ref[...]
    record_ref[4:5, :] = radius_ref[...]
    record_ref[5:6, :] = mass_ref[...]
    record_ref[6:width, :] = polygon_ref[...]
    record = record_ref[...]
    for way in range(index_ref.shape[0]):
        onehot = (
            lax.broadcasted_iota(jnp.int32, (floes, slots), 0) == index_ref[way : way + 1, :]
        ).astype(jnp.bfloat16)
        out_ref[way] = stacked_select(stack_ref, record, onehot)[0:width]


def gather_records(state, radius, mass, polygon, index):
    width = 6 + polygon.shape[0]
    padded = -(-width // 16) * 16
    return pl.pallas_call(
        gather_kernel,
        out_shape=jax.ShapeDtypeStruct((index.shape[0], width, index.shape[1]), jnp.float32),
        scratch_shapes=[
            pltpu.VMEM((padded, state.shape[1]), jnp.float32),
            pltpu.VMEM((3 * padded, state.shape[1]), jnp.float32),
        ],
    )(state, radius, mass, polygon, index)


def exchange(low, high, axis):
    size = lax.axis_size(axis)
    up = [(i, i + 1) for i in range(size - 1)]
    down = [(i + 1, i) for i in range(size - 1)]
    from_previous = lax.ppermute(high, axis, up)
    from_next = lax.ppermute(low, axis, down)
    return from_previous, from_next


def shards(
    ocean_velocity,
    wind_stress,
    level_counts,
    floe_position,
    floe_velocity,
    floe_radius,
    floe_mass,
    floe_polygon,
    remap_cells,
    contact_count,
    contact_list,
    move_index,
    move_count,
):
    columns = ("sec", "gy")
    comps, levels_here, rows_here, cols_here = ocean_velocity.shape
    halo = OSTEPS
    position = floe_position[0, 0]
    velocity = floe_velocity[0, 0]
    radius = floe_radius[0, 0]
    mass = floe_mass[0, 0]
    cells = remap_cells[0, 0]
    floes = position.shape[1]
    blocks = floes // 128
    record = jnp.concatenate([position, velocity, radius[None]], axis=0)
    edge = record[:, : GHOST * 128]
    edge_size = edge.size

    fields = jnp.concatenate(
        [
            ocean_velocity.reshape(comps * levels_here, rows_here, cols_here),
            wind_stress,
            level_counts.astype(jnp.float32)[None],
        ],
        axis=0,
    )
    channels = fields.shape[0]
    row_strip = channels * halo * cols_here
    low = jnp.concatenate([fields[:, :halo].reshape(-1), edge.reshape(-1)])
    high = jnp.concatenate([fields[:, -halo:].reshape(-1), edge.reshape(-1)])
    above, below = exchange(low, high, "gx")
    extended = jnp.concatenate(
        [
            above[:row_strip].reshape(channels, halo, cols_here),
            fields,
            below[:row_strip].reshape(channels, halo, cols_here),
        ],
        axis=1,
    )
    ghost_column = jnp.stack(
        [above[row_strip:].reshape(edge.shape), edge, below[row_strip:].reshape(edge.shape)]
    )
    ext_rows = rows_here + 2 * halo
    col_strip = channels * ext_rows * halo
    low = jnp.concatenate([extended[:, :, :halo].reshape(-1), ghost_column.reshape(-1)])
    high = jnp.concatenate([extended[:, :, -halo:].reshape(-1), ghost_column.reshape(-1)])
    left, right = exchange(low, high, columns)
    extended = jnp.concatenate(
        [
            left[:col_strip].reshape(channels, ext_rows, halo),
            extended,
            right[:col_strip].reshape(channels, ext_rows, halo),
        ],
        axis=2,
    )
    ghost_left = left[col_strip:].reshape(3, *edge.shape)
    ghost_right = right[col_strip:].reshape(3, *edge.shape)
    beside = [ghost_left, ghost_column, ghost_right]
    ghosts = jnp.stack([beside[p % 3][p // 3] for p in PLACES])

    ext_cols = cols_here + 2 * halo
    counts_ext = extended[-1]
    wet = (jnp.arange(levels_here, dtype=jnp.float32)[:, None, None] < counts_ext[None]).astype(
        jnp.float32
    )
    wind_ext = extended[comps * levels_here : comps * levels_here + 2]
    flow = extended[: comps * levels_here].reshape(comps, levels_here, ext_rows, ext_cols) * wet[None]
    for substep in range(OSTEPS):
        margin = halo - 1 - substep
        rows = slice(substep + 1, substep + 1 + rows_here + 2 * margin)
        cols = slice(substep + 1, substep + 1 + cols_here + 2 * margin)
        flow = ocean_substep(flow[:, :, 1:-1, 1:-1], flow, wet[:, rows, cols], wind_ext[:, rows, cols])

    table = block_table(record, ghosts)
    surface = jnp.stack([flow[0, 0], flow[1, 0], wind_stress[0], wind_stress[1]])
    margin = rows_here // 2
    from_above, from_below = exchange(surface[:, :margin], surface[:, -margin:], "gx")
    near = jnp.concatenate([from_above, surface, from_below], axis=1)
    first_row = lax.axis_index("gx") * rows_here - margin
    sampled = sample_surface(
        near,
        (cells // cols_here - first_row)[None],
        (cells % cols_here)[None],
    )
    lists = contact_list[0, 0]
    count = contact_count[0, 0]
    slots = lists.shape[1]
    batch = math.gcd(slots, 32)
    rounds = (count + batch - 1) // batch

    def accumulate(turn, total):
        start = turn * batch
        group = lax.dynamic_slice_in_dim(lists, start, batch, 1)
        valid = start + jnp.arange(batch, dtype=jnp.int32) < count
        return total + contact_batch(table, group, valid, blocks, GHOST)

    contact = lax.fori_loop(0, rounds, accumulate, jnp.zeros((blocks, 2, 128), jnp.float32))
    contact = contact.transpose(1, 0, 2).reshape(2, floes)
    area = math.pi * radius * radius
    relative = sampled[0:2] - velocity
    speed = jnp.sqrt(jnp.sum(relative * relative, axis=0, keepdims=True))
    total = contact + area[None] * (WATER_DRAG * speed * relative + AIR_GAIN * sampled[2:4])
    new_velocity = velocity + ICE_STEP * total / mass[None]
    new_position = position + ICE_STEP * new_velocity
    floe_next = jnp.concatenate([new_position, new_velocity], axis=0)
    leaving = move_index[0, 0]
    capacity = leaving.shape[1]
    valid_slots = jnp.arange(capacity, dtype=jnp.int32)[None, :] < move_count[0, 0][:, None]
    outgoing = gather_records(
        floe_next, radius[None], mass[None], floe_polygon[0, 0], jnp.where(valid_slots, leaving, -1)
    )
    from_above, from_below = exchange(outgoing[0:3], outgoing[5:8], "gx")
    heading_left = jnp.stack([from_below[0], outgoing[3], from_above[0]])
    heading_right = jnp.stack([from_below[2], outgoing[4], from_above[2]])
    from_left, from_right = exchange(heading_left, heading_right, columns)
    arrivals = jnp.stack(
        [
            from_right[0],
            from_below[1],
            from_left[0],
            from_right[1],
            from_left[1],
            from_right[2],
            from_above[1],
            from_left[2],
        ]
    )
    return (flow, floe_next[None, None], arrivals[None, None])


def solution(mesh):
    return jax.shard_map(
        shards,
        mesh=mesh,
        in_specs=(
            P(None, None, "gx", ("sec", "gy")),
            P(None, "gx", ("sec", "gy")),
            P("gx", ("sec", "gy")),
            P("gx", ("sec", "gy"), None, None),
            P("gx", ("sec", "gy"), None, None),
            P("gx", ("sec", "gy"), None),
            P("gx", ("sec", "gy"), None),
            P("gx", ("sec", "gy"), None, None),
            P("gx", ("sec", "gy"), None),
            P("gx", ("sec", "gy")),
            P("gx", ("sec", "gy"), None, None),
            P("gx", ("sec", "gy"), None, None),
            P("gx", ("sec", "gy"), None),
        ),
        out_specs=(
            P(None, None, "gx", ("sec", "gy")),
            P("gx", ("sec", "gy"), None, None),
            P("gx", ("sec", "gy"), None, None, None),
        ),
        check_vma=False,
    )
```

```python
import math

import jax
import jax.numpy as jnp
from jax import lax
from jax.experimental import pallas as pl
from jax.experimental.pallas import tpu as pltpu
from jax.sharding import PartitionSpec as P

OSTEPS = 4
GHOST = 4


SOFTEN = 0.1
STIFFNESS = 0.1
DAMPING = 0.05
VERT_MIX = 0.15
CORIOLIS = 0.1
SURFACE_GAIN = 0.25
WATER_DRAG = 0.1
AIR_GAIN = 0.2
ICE_STEP = 0.5
PLACES = (0, 1, 2, 3, 5, 6, 7, 8)


def with_halo(array, sides, width):
    for axis, dim in sides:
        size, length = (lax.axis_size(axis), array.shape[dim])
        up = [(i, (i + 1) % size) for i in range(size - 1)]
        down = [(j, i) for i, j in up]
        last = lax.slice_in_dim(array, length - width, length, axis=dim)
        leading = lax.slice_in_dim(array, 0, width, axis=dim)
        before = lax.ppermute(last, axis, up)
        after = lax.ppermute(leading, axis, down)
        array = jnp.concatenate([before, array, after], axis=dim)
    return array


def ocean_substep(flow, padded, wet, wind):
    levels_here = flow.shape[1]
    lap = (
        padded[:, :, :-2, 1:-1]
        + padded[:, :, 2:, 1:-1]
        + padded[:, :, 1:-1, :-2]
        + padded[:, :, 1:-1, 2:]
        - 4.0 * flow
    )
    depth = jnp.arange(levels_here, dtype=jnp.float32)
    horizontal = (0.15 - 0.05 * depth / levels_here)[None, :, None, None]
    flux = VERT_MIX * (flow[:, 1:] - flow[:, :-1]) * wet[None, 1:]
    empty = jnp.zeros_like(flow[:, :1])
    vert = jnp.concatenate([flux, empty], axis=1) - jnp.concatenate([empty, flux], axis=1)
    turning = jnp.stack([CORIOLIS * flow[1], -CORIOLIS * flow[0]])
    surface = jnp.concatenate([SURFACE_GAIN * wind[:, None], jnp.zeros_like(flow[:, 1:])], axis=1)
    return (flow + horizontal * lap + vert + turning + surface) * wet[None]


def pair_forces(first, second):
    own = first[:, :, None, :]
    other = second[:, :, :, None]
    delta_x = own[:, 0] - other[:, 0]
    delta_y = own[:, 1] - other[:, 1]
    inverse = lax.rsqrt(delta_x * delta_x + delta_y * delta_y + SOFTEN * SOFTEN)
    distance = (delta_x * delta_x + delta_y * delta_y + SOFTEN * SOFTEN) * inverse
    reach = own[:, 4] + other[:, 4]
    intersection = jnp.maximum(reach - distance, 0.0)
    reduced = own[:, 4] * other[:, 4] / reach
    normal_x = delta_x * inverse
    normal_y = delta_y * inverse
    closing = (own[:, 2] - other[:, 2]) * normal_x + (own[:, 3] - other[:, 3]) * normal_y
    magnitude = intersection * reduced * (STIFFNESS - DAMPING * closing)
    return jnp.stack(
        [jnp.sum(magnitude * normal_x, axis=1), jnp.sum(magnitude * normal_y, axis=1)], axis=1
    )


def block_table(own, ghosts):
    blocks = own.shape[1] // 128
    edge_blocks = ghosts.shape[2] // 128
    mine = own.reshape(5, blocks, 128).transpose(1, 0, 2)
    theirs = (
        ghosts.reshape(8, 5, edge_blocks, 128)
        .transpose(0, 2, 1, 3)
        .reshape(8 * edge_blocks, 5, 128)
    )
    return jnp.concatenate([mine, theirs], axis=0)


def contact_batch(table, lists, valid, blocks, edge_blocks):
    source = lists[1]
    neighbour = source - (source > 4).astype(jnp.int32)
    partner = jnp.where(source == 4, lists[2], blocks + neighbour * edge_blocks + lists[2])
    forces = pair_forces(table[lists[0]], table[partner])
    forces = jnp.where(valid[:, None, None], forces, 0.0)
    onehot = (lists[0][:, None] == jnp.arange(blocks, dtype=jnp.int32)[None, :]).astype(jnp.float32)
    return jnp.einsum("pn,pcf->ncf", onehot, forces, precision=lax.Precision.HIGHEST)


def split_parts(x):
    high = x.astype(jnp.bfloat16).astype(jnp.float32)
    rest = x - high
    middle = rest.astype(jnp.bfloat16).astype(jnp.float32)
    low = (rest - middle).astype(jnp.bfloat16).astype(jnp.float32)
    return high, middle, low


def stacked_select(stack_ref, x, onehot):
    rows = x.shape[0]
    pitch = stack_ref.shape[0] // 3
    for part, value in enumerate(split_parts(x)):
        stack_ref[part * pitch : part * pitch + rows, :] = value
    picked = jnp.dot(
        stack_ref[...].astype(jnp.bfloat16), onehot, preferred_element_type=jnp.float32
    )
    return (picked[0:rows] + picked[pitch : pitch + rows]) + picked[2 * pitch : 2 * pitch + rows]


def sample_kernel(window_ref, rows_ref, cols_ref, out_ref, stack_ref):
    window_rows, window_cols = window_ref.shape[1:]
    floes = rows_ref.shape[1]
    onehot = (
        lax.broadcasted_iota(jnp.int32, (window_rows, floes), 0) == rows_ref[...]
    ).astype(jnp.bfloat16)
    pick = lax.broadcasted_iota(jnp.int32, (window_cols, floes), 0) == cols_ref[...]
    for channel in range(window_ref.shape[0]):
        picked = stacked_select(stack_ref, window_ref[channel].T, onehot)
        out_ref[channel : channel + 1, :] = jnp.sum(
            jnp.where(pick, picked, 0.0), axis=0, keepdims=True
        )


def sample_surface(window, rows, cols):
    return pl.pallas_call(
        sample_kernel,
        out_shape=jax.ShapeDtypeStruct((window.shape[0], rows.shape[1]), jnp.float32),
        scratch_shapes=[pltpu.VMEM((3 * window.shape[2], window.shape[1]), jnp.float32)],
    )(window, rows, cols)


def gather_kernel(state_ref, radius_ref, mass_ref, polygon_ref, index_ref, out_ref, record_ref, stack_ref):
    floes = state_ref.shape[1]
    slots = index_ref.shape[1]
    width = out_ref.shape[1]
    record_ref[...] = jnp.zeros_like(record_ref)
    stack_ref[...] = jnp.zeros_like(stack_ref)
    record_ref[0:4, :] = state_ref[...]
    record_ref[4:5, :] = radius_ref[...]
    record_ref[5:6, :] = mass_ref[...]
    record_ref[6:width, :] = polygon_ref[...]
    record = record_ref[...]
    for way in range(index_ref.shape[0]):
        onehot = (
            lax.broadcasted_iota(jnp.int32, (floes, slots), 0) == index_ref[way : way + 1, :]
        ).astype(jnp.bfloat16)
        out_ref[way] = stacked_select(stack_ref, record, onehot)[0:width]


def gather_records(state, radius, mass, polygon, index):
    width = 6 + polygon.shape[0]
    padded = -(-width // 16) * 16
    return pl.pallas_call(
        gather_kernel,
        out_shape=jax.ShapeDtypeStruct((index.shape[0], width, index.shape[1]), jnp.float32),
        scratch_shapes=[
            pltpu.VMEM((padded, state.shape[1]), jnp.float32),
            pltpu.VMEM((3 * padded, state.shape[1]), jnp.float32),
        ],
    )(state, radius, mass, polygon, index)


def exchange(low, high, axis):
    size = lax.axis_size(axis)
    up = [(i, i + 1) for i in range(size - 1)]
    down = [(i + 1, i) for i in range(size - 1)]
    from_previous = lax.ppermute(high, axis, up)
    from_next = lax.ppermute(low, axis, down)
    return from_previous, from_next


def shards(
    ocean_velocity,
    wind_stress,
    level_counts,
    floe_position,
    floe_velocity,
    floe_radius,
    floe_mass,
    floe_polygon,
    remap_cells,
    contact_count,
    contact_list,
    move_index,
    move_count,
):
    columns = ("sec", "gy")
    comps, levels_here, rows_here, cols_here = ocean_velocity.shape
    halo = OSTEPS
    position = floe_position[0, 0]
    velocity = floe_velocity[0, 0]
    radius = floe_radius[0, 0]
    mass = floe_mass[0, 0]
    cells = remap_cells[0, 0]
    floes = position.shape[1]
    blocks = floes // 128
    record = jnp.concatenate([position, velocity, radius[None]], axis=0)
    edge = record[:, : GHOST * 128]
    edge_size = edge.size

    fields = jnp.concatenate(
        [
            ocean_velocity.reshape(comps * levels_here, rows_here, cols_here),
            wind_stress,
            level_counts.astype(jnp.float32)[None],
        ],
        axis=0,
    )
    channels = fields.shape[0]
    row_strip = channels * halo * cols_here
    low = jnp.concatenate([fields[:, :halo].reshape(-1), edge.reshape(-1)])
    high = jnp.concatenate([fields[:, -halo:].reshape(-1), edge.reshape(-1)])
    above, below = exchange(low, high, "gx")
    extended = jnp.concatenate(
        [
            above[:row_strip].reshape(channels, halo, cols_here),
            fields,
            below[:row_strip].reshape(channels, halo, cols_here),
        ],
        axis=1,
    )
    ghost_column = jnp.stack(
        [above[row_strip:].reshape(edge.shape), edge, below[row_strip:].reshape(edge.shape)]
    )
    ext_rows = rows_here + 2 * halo
    col_strip = channels * ext_rows * halo
    low = jnp.concatenate([extended[:, :, :halo].reshape(-1), ghost_column.reshape(-1)])
    high = jnp.concatenate([extended[:, :, -halo:].reshape(-1), ghost_column.reshape(-1)])
    left, right = exchange(low, high, columns)
    extended = jnp.concatenate(
        [
            left[:col_strip].reshape(channels, ext_rows, halo),
            extended,
            right[:col_strip].reshape(channels, ext_rows, halo),
        ],
        axis=2,
    )
    ghost_left = left[col_strip:].reshape(3, *edge.shape)
    ghost_right = right[col_strip:].reshape(3, *edge.shape)
    beside = [ghost_left, ghost_column, ghost_right]
    ghosts = jnp.stack([beside[p % 3][p // 3] for p in PLACES])

    ext_cols = cols_here + 2 * halo
    counts_ext = extended[-1]
    wet = (jnp.arange(levels_here, dtype=jnp.float32)[:, None, None] < counts_ext[None]).astype(
        jnp.float32
    )
    wind_ext = extended[comps * levels_here : comps * levels_here + 2]
    flow = extended[: comps * levels_here].reshape(comps, levels_here, ext_rows, ext_cols) * wet[None]
    for substep in range(OSTEPS):
        padded = jnp.pad(flow, ((0, 0), (0, 0), (1, 1), (1, 1)))
        flow = ocean_substep(flow, padded, wet, wind_ext)
    flow = flow[:, :, halo : halo + rows_here, halo : halo + cols_here]

    table = block_table(record, ghosts)
    surface = jnp.stack([flow[0, 0], flow[1, 0], wind_stress[0], wind_stress[1]])
    margin = rows_here // 2
    from_above, from_below = exchange(surface[:, :margin], surface[:, -margin:], "gx")
    near = jnp.concatenate([from_above, surface, from_below], axis=1)
    first_row = lax.axis_index("gx") * rows_here - margin
    sampled = sample_surface(
        near,
        (cells // cols_here - first_row)[None],
        (cells % cols_here)[None],
    )
    lists = contact_list[0, 0]
    count = contact_count[0, 0]
    slots = lists.shape[1]
    sizes = sorted({min(slots, size) for size in (16, 32, slots)})

    def pass_over(size):
        def run(lists, count):
            valid = jnp.arange(size, dtype=jnp.int32) < count
            return contact_batch(table, lists[:, :size], valid, blocks, GHOST)

        return run

    which = sum((count > size).astype(jnp.int32) for size in sizes[:-1])
    contact = lax.switch(which, [pass_over(size) for size in sizes], lists, count)
    contact = contact.transpose(1, 0, 2).reshape(2, floes)
    area = math.pi * radius * radius
    relative = sampled[0:2] - velocity
    speed = jnp.sqrt(jnp.sum(relative * relative, axis=0, keepdims=True))
    total = contact + area[None] * (WATER_DRAG * speed * relative + AIR_GAIN * sampled[2:4])
    new_velocity = velocity + ICE_STEP * total / mass[None]
    new_position = position + ICE_STEP * new_velocity
    floe_next = jnp.concatenate([new_position, new_velocity], axis=0)
    leaving = move_index[0, 0]
    capacity = leaving.shape[1]
    valid_slots = jnp.arange(capacity, dtype=jnp.int32)[None, :] < move_count[0, 0][:, None]
    outgoing = gather_records(
        floe_next, radius[None], mass[None], floe_polygon[0, 0], jnp.where(valid_slots, leaving, -1)
    )
    from_above, from_below = exchange(outgoing[0:3], outgoing[5:8], "gx")
    heading_left = jnp.stack([from_below[0], outgoing[3], from_above[0]])
    heading_right = jnp.stack([from_below[2], outgoing[4], from_above[2]])
    from_left, from_right = exchange(heading_left, heading_right, columns)
    arrivals = jnp.stack(
        [
            from_right[0],
            from_below[1],
            from_left[0],
            from_right[1],
            from_left[1],
            from_right[2],
            from_above[1],
            from_left[2],
        ]
    )
    return (flow, floe_next[None, None], arrivals[None, None])


def solution(mesh):
    return jax.shard_map(
        shards,
        mesh=mesh,
        in_specs=(
            P(None, None, "gx", ("sec", "gy")),
            P(None, "gx", ("sec", "gy")),
            P("gx", ("sec", "gy")),
            P("gx", ("sec", "gy"), None, None),
            P("gx", ("sec", "gy"), None, None),
            P("gx", ("sec", "gy"), None),
            P("gx", ("sec", "gy"), None),
            P("gx", ("sec", "gy"), None, None),
            P("gx", ("sec", "gy"), None),
            P("gx", ("sec", "gy")),
            P("gx", ("sec", "gy"), None, None),
            P("gx", ("sec", "gy"), None, None),
            P("gx", ("sec", "gy"), None),
        ),
        out_specs=(
            P(None, None, "gx", ("sec", "gy")),
            P("gx", ("sec", "gy"), None, None),
            P("gx", ("sec", "gy"), None, None, None),
        ),
        check_vma=False,
    )
```

```python
import math

import jax
import jax.numpy as jnp
from jax import lax
from jax.experimental import pallas as pl
from jax.experimental.pallas import tpu as pltpu
from jax.sharding import PartitionSpec as P

OSTEPS = 4
GHOST = 4


SOFTEN = 0.1
STIFFNESS = 0.1
DAMPING = 0.05
VERT_MIX = 0.15
CORIOLIS = 0.1
SURFACE_GAIN = 0.25
WATER_DRAG = 0.1
AIR_GAIN = 0.2
ICE_STEP = 0.5
PLACES = (0, 1, 2, 3, 5, 6, 7, 8)


def with_halo(array, sides, width):
    for axis, dim in sides:
        size, length = (lax.axis_size(axis), array.shape[dim])
        up = [(i, (i + 1) % size) for i in range(size - 1)]
        down = [(j, i) for i, j in up]
        last = lax.slice_in_dim(array, length - width, length, axis=dim)
        leading = lax.slice_in_dim(array, 0, width, axis=dim)
        before = lax.ppermute(last, axis, up)
        after = lax.ppermute(leading, axis, down)
        array = jnp.concatenate([before, array, after], axis=dim)
    return array


def ocean_substep(flow, padded, wet, wind):
    levels_here = flow.shape[1]
    lap = (
        padded[:, :, :-2, 1:-1]
        + padded[:, :, 2:, 1:-1]
        + padded[:, :, 1:-1, :-2]
        + padded[:, :, 1:-1, 2:]
        - 4.0 * flow
    )
    depth = jnp.arange(levels_here, dtype=jnp.float32)
    horizontal = (0.15 - 0.05 * depth / levels_here)[None, :, None, None]
    flux = VERT_MIX * (flow[:, 1:] - flow[:, :-1]) * wet[None, 1:]
    empty = jnp.zeros_like(flow[:, :1])
    vert = jnp.concatenate([flux, empty], axis=1) - jnp.concatenate([empty, flux], axis=1)
    turning = jnp.stack([CORIOLIS * flow[1], -CORIOLIS * flow[0]])
    surface = jnp.concatenate([SURFACE_GAIN * wind[:, None], jnp.zeros_like(flow[:, 1:])], axis=1)
    return (flow + horizontal * lap + vert + turning + surface) * wet[None]


def pair_forces(first, second):
    own = first[:, :, None, :]
    other = second[:, :, :, None]
    delta_x = own[:, 0] - other[:, 0]
    delta_y = own[:, 1] - other[:, 1]
    inverse = lax.rsqrt(delta_x * delta_x + delta_y * delta_y + SOFTEN * SOFTEN)
    distance = (delta_x * delta_x + delta_y * delta_y + SOFTEN * SOFTEN) * inverse
    reach = own[:, 4] + other[:, 4]
    intersection = jnp.maximum(reach - distance, 0.0)
    reduced = own[:, 4] * other[:, 4] / reach
    normal_x = delta_x * inverse
    normal_y = delta_y * inverse
    closing = (own[:, 2] - other[:, 2]) * normal_x + (own[:, 3] - other[:, 3]) * normal_y
    magnitude = intersection * reduced * (STIFFNESS - DAMPING * closing)
    return jnp.stack(
        [jnp.sum(magnitude * normal_x, axis=1), jnp.sum(magnitude * normal_y, axis=1)], axis=1
    )


def block_table(own, ghosts):
    blocks = own.shape[1] // 128
    edge_blocks = ghosts.shape[2] // 128
    mine = own.reshape(5, blocks, 128).transpose(1, 0, 2)
    theirs = (
        ghosts.reshape(8, 5, edge_blocks, 128)
        .transpose(0, 2, 1, 3)
        .reshape(8 * edge_blocks, 5, 128)
    )
    return jnp.concatenate([mine, theirs], axis=0)


def contact_batch(table, lists, valid, blocks, edge_blocks):
    source = lists[1]
    neighbour = source - (source > 4).astype(jnp.int32)
    partner = jnp.where(source == 4, lists[2], blocks + neighbour * edge_blocks + lists[2])
    forces = pair_forces(table[lists[0]], table[partner])
    forces = jnp.where(valid[:, None, None], forces, 0.0)
    onehot = (lists[0][:, None] == jnp.arange(blocks, dtype=jnp.int32)[None, :]).astype(jnp.float32)
    return jnp.einsum("pn,pcf->ncf", onehot, forces, precision=lax.Precision.HIGHEST)


def split_parts(x):
    high = x.astype(jnp.bfloat16).astype(jnp.float32)
    rest = x - high
    middle = rest.astype(jnp.bfloat16).astype(jnp.float32)
    low = (rest - middle).astype(jnp.bfloat16).astype(jnp.float32)
    return high, middle, low


def stacked_select(stack_ref, x, onehot):
    rows = x.shape[0]
    pitch = stack_ref.shape[0] // 3
    for part, value in enumerate(split_parts(x)):
        stack_ref[part * pitch : part * pitch + rows, :] = value
    picked = jnp.dot(
        stack_ref[...].astype(jnp.bfloat16), onehot, preferred_element_type=jnp.float32
    )
    return (picked[0:rows] + picked[pitch : pitch + rows]) + picked[2 * pitch : 2 * pitch + rows]


def sample_kernel(window_ref, rows_ref, cols_ref, out_ref, stack_ref):
    window_rows, window_cols = window_ref.shape[1:]
    floes = rows_ref.shape[1]
    onehot = (
        lax.broadcasted_iota(jnp.int32, (window_rows, floes), 0) == rows_ref[...]
    ).astype(jnp.bfloat16)
    pick = lax.broadcasted_iota(jnp.int32, (window_cols, floes), 0) == cols_ref[...]
    for channel in range(window_ref.shape[0]):
        picked = stacked_select(stack_ref, window_ref[channel].T, onehot)
        out_ref[channel : channel + 1, :] = jnp.sum(
            jnp.where(pick, picked, 0.0), axis=0, keepdims=True
        )


def sample_surface(window, rows, cols):
    return pl.pallas_call(
        sample_kernel,
        out_shape=jax.ShapeDtypeStruct((window.shape[0], rows.shape[1]), jnp.float32),
        scratch_shapes=[pltpu.VMEM((3 * window.shape[2], window.shape[1]), jnp.float32)],
    )(window, rows, cols)


def gather_kernel(state_ref, radius_ref, mass_ref, polygon_ref, index_ref, out_ref, record_ref, stack_ref):
    floes = state_ref.shape[1]
    slots = index_ref.shape[1]
    width = out_ref.shape[1]
    record_ref[...] = jnp.zeros_like(record_ref)
    stack_ref[...] = jnp.zeros_like(stack_ref)
    record_ref[0:4, :] = state_ref[...]
    record_ref[4:5, :] = radius_ref[...]
    record_ref[5:6, :] = mass_ref[...]
    record_ref[6:width, :] = polygon_ref[...]
    record = record_ref[...]
    for way in range(index_ref.shape[0]):
        onehot = (
            lax.broadcasted_iota(jnp.int32, (floes, slots), 0) == index_ref[way : way + 1, :]
        ).astype(jnp.bfloat16)
        out_ref[way] = stacked_select(stack_ref, record, onehot)[0:width]


def gather_records(state, radius, mass, polygon, index):
    width = 6 + polygon.shape[0]
    padded = -(-width // 16) * 16
    return pl.pallas_call(
        gather_kernel,
        out_shape=jax.ShapeDtypeStruct((index.shape[0], width, index.shape[1]), jnp.float32),
        scratch_shapes=[
            pltpu.VMEM((padded, state.shape[1]), jnp.float32),
            pltpu.VMEM((3 * padded, state.shape[1]), jnp.float32),
        ],
    )(state, radius, mass, polygon, index)


def exchange(low, high, axis):
    size = lax.axis_size(axis)
    up = [(i, i + 1) for i in range(size - 1)]
    down = [(i + 1, i) for i in range(size - 1)]
    from_previous = lax.ppermute(high, axis, up)
    from_next = lax.ppermute(low, axis, down)
    return from_previous, from_next


def shards(
    ocean_velocity,
    wind_stress,
    level_counts,
    floe_position,
    floe_velocity,
    floe_radius,
    floe_mass,
    floe_polygon,
    remap_cells,
    contact_count,
    contact_list,
    move_index,
    move_count,
):
    columns = ("sec", "gy")
    comps, levels_here, rows_here, cols_here = ocean_velocity.shape
    halo = OSTEPS
    position = floe_position[0, 0]
    velocity = floe_velocity[0, 0]
    radius = floe_radius[0, 0]
    mass = floe_mass[0, 0]
    cells = remap_cells[0, 0]
    floes = position.shape[1]
    blocks = floes // 128
    record = jnp.concatenate([position, velocity, radius[None]], axis=0)
    edge = record[:, : GHOST * 128]
    edge_size = edge.size

    fields = jnp.concatenate(
        [
            ocean_velocity.reshape(comps * levels_here, rows_here, cols_here),
            wind_stress,
            level_counts.astype(jnp.float32)[None],
        ],
        axis=0,
    )
    channels = fields.shape[0]
    row_strip = channels * halo * cols_here
    low = jnp.concatenate([fields[:, :halo].reshape(-1), edge.reshape(-1)])
    high = jnp.concatenate([fields[:, -halo:].reshape(-1), edge.reshape(-1)])
    above, below = exchange(low, high, "gx")
    extended = jnp.concatenate(
        [
            above[:row_strip].reshape(channels, halo, cols_here),
            fields,
            below[:row_strip].reshape(channels, halo, cols_here),
        ],
        axis=1,
    )
    ghost_column = jnp.stack(
        [above[row_strip:].reshape(edge.shape), edge, below[row_strip:].reshape(edge.shape)]
    )
    ext_rows = rows_here + 2 * halo
    col_strip = channels * ext_rows * halo
    low = jnp.concatenate([extended[:, :, :halo].reshape(-1), ghost_column.reshape(-1)])
    high = jnp.concatenate([extended[:, :, -halo:].reshape(-1), ghost_column.reshape(-1)])
    left, right = exchange(low, high, columns)
    extended = jnp.concatenate(
        [
            left[:col_strip].reshape(channels, ext_rows, halo),
            extended,
            right[:col_strip].reshape(channels, ext_rows, halo),
        ],
        axis=2,
    )
    ghost_left = left[col_strip:].reshape(3, *edge.shape)
    ghost_right = right[col_strip:].reshape(3, *edge.shape)
    beside = [ghost_left, ghost_column, ghost_right]
    ghosts = jnp.stack([beside[p % 3][p // 3] for p in PLACES])

    ext_cols = cols_here + 2 * halo
    counts_ext = extended[-1]
    wet = (jnp.arange(levels_here, dtype=jnp.float32)[:, None, None] < counts_ext[None]).astype(
        jnp.float32
    )
    wind_ext = extended[comps * levels_here : comps * levels_here + 2]
    flow = extended[: comps * levels_here].reshape(comps, levels_here, ext_rows, ext_cols) * wet[None]
    for substep in range(OSTEPS - 1):
        padded = jnp.pad(flow, ((0, 0), (0, 0), (1, 1), (1, 1)))
        flow = ocean_substep(flow, padded, wet, wind_ext)
    wet_tile = (jnp.arange(levels_here, dtype=jnp.int32)[:, None, None] < level_counts[None]).astype(
        jnp.float32
    )
    flow = ocean_substep(
        flow[:, :, halo : halo + rows_here, halo : halo + cols_here],
        flow[:, :, halo - 1 : halo + rows_here + 1, halo - 1 : halo + cols_here + 1],
        wet_tile,
        wind_stress,
    )

    table = block_table(record, ghosts)
    surface = jnp.stack([flow[0, 0], flow[1, 0], wind_stress[0], wind_stress[1]])
    margin = rows_here // 2
    from_above, from_below = exchange(surface[:, :margin], surface[:, -margin:], "gx")
    near = jnp.concatenate([from_above, surface, from_below], axis=1)
    first_row = lax.axis_index("gx") * rows_here - margin
    sampled = sample_surface(
        near,
        (cells // cols_here - first_row)[None],
        (cells % cols_here)[None],
    )
    lists = contact_list[0, 0]
    count = contact_count[0, 0]
    slots = lists.shape[1]
    sizes = sorted({min(slots, size) for size in (16, 32, slots)})

    def pass_over(size):
        def run(lists, count):
            valid = jnp.arange(size, dtype=jnp.int32) < count
            return contact_batch(table, lists[:, :size], valid, blocks, GHOST)

        return run

    which = sum((count > size).astype(jnp.int32) for size in sizes[:-1])
    contact = lax.switch(which, [pass_over(size) for size in sizes], lists, count)
    contact = contact.transpose(1, 0, 2).reshape(2, floes)
    area = math.pi * radius * radius
    relative = sampled[0:2] - velocity
    speed = jnp.sqrt(jnp.sum(relative * relative, axis=0, keepdims=True))
    total = contact + area[None] * (WATER_DRAG * speed * relative + AIR_GAIN * sampled[2:4])
    new_velocity = velocity + ICE_STEP * total / mass[None]
    new_position = position + ICE_STEP * new_velocity
    floe_next = jnp.concatenate([new_position, new_velocity], axis=0)
    leaving = move_index[0, 0]
    capacity = leaving.shape[1]
    valid_slots = jnp.arange(capacity, dtype=jnp.int32)[None, :] < move_count[0, 0][:, None]
    outgoing = gather_records(
        floe_next, radius[None], mass[None], floe_polygon[0, 0], jnp.where(valid_slots, leaving, -1)
    )
    from_above, from_below = exchange(outgoing[0:3], outgoing[5:8], "gx")
    heading_left = jnp.stack([from_below[0], outgoing[3], from_above[0]])
    heading_right = jnp.stack([from_below[2], outgoing[4], from_above[2]])
    from_left, from_right = exchange(heading_left, heading_right, columns)
    arrivals = jnp.stack(
        [
            from_right[0],
            from_below[1],
            from_left[0],
            from_right[1],
            from_left[1],
            from_right[2],
            from_above[1],
            from_left[2],
        ]
    )
    return (flow, floe_next[None, None], arrivals[None, None])


def solution(mesh):
    return jax.shard_map(
        shards,
        mesh=mesh,
        in_specs=(
            P(None, None, "gx", ("sec", "gy")),
            P(None, "gx", ("sec", "gy")),
            P("gx", ("sec", "gy")),
            P("gx", ("sec", "gy"), None, None),
            P("gx", ("sec", "gy"), None, None),
            P("gx", ("sec", "gy"), None),
            P("gx", ("sec", "gy"), None),
            P("gx", ("sec", "gy"), None, None),
            P("gx", ("sec", "gy"), None),
            P("gx", ("sec", "gy")),
            P("gx", ("sec", "gy"), None, None),
            P("gx", ("sec", "gy"), None, None),
            P("gx", ("sec", "gy"), None),
        ),
        out_specs=(
            P(None, None, "gx", ("sec", "gy")),
            P("gx", ("sec", "gy"), None, None),
            P("gx", ("sec", "gy"), None, None, None),
        ),
        check_vma=False,
    )
```

```python
import math

import jax
import jax.numpy as jnp
from jax import lax
from jax.experimental import pallas as pl
from jax.experimental.pallas import tpu as pltpu
from jax.sharding import PartitionSpec as P

OSTEPS = 4
GHOST = 4


SOFTEN = 0.1
STIFFNESS = 0.1
DAMPING = 0.05
VERT_MIX = 0.15
CORIOLIS = 0.1
SURFACE_GAIN = 0.25
WATER_DRAG = 0.1
AIR_GAIN = 0.2
ICE_STEP = 0.5
PLACES = (0, 1, 2, 3, 5, 6, 7, 8)


def with_halo(array, sides, width):
    for axis, dim in sides:
        size, length = (lax.axis_size(axis), array.shape[dim])
        up = [(i, (i + 1) % size) for i in range(size - 1)]
        down = [(j, i) for i, j in up]
        last = lax.slice_in_dim(array, length - width, length, axis=dim)
        leading = lax.slice_in_dim(array, 0, width, axis=dim)
        before = lax.ppermute(last, axis, up)
        after = lax.ppermute(leading, axis, down)
        array = jnp.concatenate([before, array, after], axis=dim)
    return array


def ocean_substep(flow, padded, wet, wind):
    levels_here = flow.shape[1]
    lap = (
        padded[:, :, :-2, 1:-1]
        + padded[:, :, 2:, 1:-1]
        + padded[:, :, 1:-1, :-2]
        + padded[:, :, 1:-1, 2:]
        - 4.0 * flow
    )
    depth = jnp.arange(levels_here, dtype=jnp.float32)
    horizontal = (0.15 - 0.05 * depth / levels_here)[None, :, None, None]
    flux = VERT_MIX * (flow[:, 1:] - flow[:, :-1]) * wet[None, 1:]
    empty = jnp.zeros_like(flow[:, :1])
    vert = jnp.concatenate([flux, empty], axis=1) - jnp.concatenate([empty, flux], axis=1)
    turning = jnp.stack([CORIOLIS * flow[1], -CORIOLIS * flow[0]])
    surface = jnp.concatenate([SURFACE_GAIN * wind[:, None], jnp.zeros_like(flow[:, 1:])], axis=1)
    return (flow + horizontal * lap + vert + turning + surface) * wet[None]


def pair_forces(first, second):
    own = first[:, :, None, :]
    other = second[:, :, :, None]
    delta_x = own[:, 0] - other[:, 0]
    delta_y = own[:, 1] - other[:, 1]
    inverse = lax.rsqrt(delta_x * delta_x + delta_y * delta_y + SOFTEN * SOFTEN)
    distance = (delta_x * delta_x + delta_y * delta_y + SOFTEN * SOFTEN) * inverse
    reach = own[:, 4] + other[:, 4]
    intersection = jnp.maximum(reach - distance, 0.0)
    reduced = own[:, 4] * other[:, 4] / reach
    normal_x = delta_x * inverse
    normal_y = delta_y * inverse
    closing = (own[:, 2] - other[:, 2]) * normal_x + (own[:, 3] - other[:, 3]) * normal_y
    magnitude = intersection * reduced * (STIFFNESS - DAMPING * closing)
    return jnp.stack(
        [jnp.sum(magnitude * normal_x, axis=1), jnp.sum(magnitude * normal_y, axis=1)], axis=1
    )


def block_table(own, ghosts):
    blocks = own.shape[1] // 128
    edge_blocks = ghosts.shape[2] // 128
    mine = own.reshape(5, blocks, 128).transpose(1, 0, 2)
    theirs = (
        ghosts.reshape(8, 5, edge_blocks, 128)
        .transpose(0, 2, 1, 3)
        .reshape(8 * edge_blocks, 5, 128)
    )
    return jnp.concatenate([mine, theirs], axis=0)


def contact_batch(table, lists, valid, blocks, edge_blocks):
    source = lists[1]
    neighbour = source - (source > 4).astype(jnp.int32)
    partner = jnp.where(source == 4, lists[2], blocks + neighbour * edge_blocks + lists[2])
    forces = pair_forces(table[lists[0]], table[partner])
    forces = jnp.where(valid[:, None, None], forces, 0.0)
    onehot = (lists[0][:, None] == jnp.arange(blocks, dtype=jnp.int32)[None, :]).astype(jnp.float32)
    return jnp.einsum("pn,pcf->ncf", onehot, forces, precision=lax.Precision.HIGHEST)


def split_parts(x):
    high = x.astype(jnp.bfloat16).astype(jnp.float32)
    rest = x - high
    middle = rest.astype(jnp.bfloat16).astype(jnp.float32)
    low = (rest - middle).astype(jnp.bfloat16).astype(jnp.float32)
    return high, middle, low


def stacked_select(stack_ref, x, onehot):
    rows = x.shape[0]
    pitch = stack_ref.shape[0] // 3
    for part, value in enumerate(split_parts(x)):
        stack_ref[part * pitch : part * pitch + rows, :] = value
    picked = jnp.dot(
        stack_ref[...].astype(jnp.bfloat16), onehot, preferred_element_type=jnp.float32
    )
    return (picked[0:rows] + picked[pitch : pitch + rows]) + picked[2 * pitch : 2 * pitch + rows]


def sample_kernel(window_ref, rows_ref, cols_ref, out_ref, stack_ref):
    window_rows, window_cols = window_ref.shape[1:]
    floes = rows_ref.shape[1]
    onehot = (
        lax.broadcasted_iota(jnp.int32, (window_rows, floes), 0) == rows_ref[...]
    ).astype(jnp.bfloat16)
    pick = lax.broadcasted_iota(jnp.int32, (window_cols, floes), 0) == cols_ref[...]
    for channel in range(window_ref.shape[0]):
        picked = stacked_select(stack_ref, window_ref[channel].T, onehot)
        out_ref[channel : channel + 1, :] = jnp.sum(
            jnp.where(pick, picked, 0.0), axis=0, keepdims=True
        )


def sample_surface(window, rows, cols):
    return pl.pallas_call(
        sample_kernel,
        out_shape=jax.ShapeDtypeStruct((window.shape[0], rows.shape[1]), jnp.float32),
        scratch_shapes=[pltpu.VMEM((3 * window.shape[2], window.shape[1]), jnp.float32)],
    )(window, rows, cols)


def gather_kernel(state_ref, radius_ref, mass_ref, polygon_ref, index_ref, out_ref, record_ref, stack_ref):
    floes = state_ref.shape[1]
    slots = index_ref.shape[1]
    width = out_ref.shape[1]
    record_ref[...] = jnp.zeros_like(record_ref)
    stack_ref[...] = jnp.zeros_like(stack_ref)
    record_ref[0:4, :] = state_ref[...]
    record_ref[4:5, :] = radius_ref[...]
    record_ref[5:6, :] = mass_ref[...]
    record_ref[6:width, :] = polygon_ref[...]
    record = record_ref[...]
    for way in range(index_ref.shape[0]):
        onehot = (
            lax.broadcasted_iota(jnp.int32, (floes, slots), 0) == index_ref[way : way + 1, :]
        ).astype(jnp.bfloat16)
        out_ref[way] = stacked_select(stack_ref, record, onehot)[0:width]


def gather_records(state, radius, mass, polygon, index):
    width = 6 + polygon.shape[0]
    padded = -(-width // 16) * 16
    return pl.pallas_call(
        gather_kernel,
        out_shape=jax.ShapeDtypeStruct((index.shape[0], width, index.shape[1]), jnp.float32),
        scratch_shapes=[
            pltpu.VMEM((padded, state.shape[1]), jnp.float32),
            pltpu.VMEM((3 * padded, state.shape[1]), jnp.float32),
        ],
    )(state, radius, mass, polygon, index)


def state_kernel(state_ref, index_ref, static_ref, out_ref, record_ref, stack_ref):
    floes = state_ref.shape[1]
    slots = index_ref.shape[1]
    rows = state_ref.shape[0]
    record_ref[...] = jnp.zeros_like(record_ref)
    stack_ref[...] = jnp.zeros_like(stack_ref)
    record_ref[0:rows, :] = state_ref[...]
    record = record_ref[...]
    out_ref[...] = static_ref[...]
    for way in range(index_ref.shape[0]):
        onehot = (
            lax.broadcasted_iota(jnp.int32, (floes, slots), 0) == index_ref[way : way + 1, :]
        ).astype(jnp.bfloat16)
        out_ref[way, 0:rows, :] = stacked_select(stack_ref, record, onehot)[0:rows]


def gather_state(state, index, static):
    padded = -(-state.shape[0] // 8) * 8
    return pl.pallas_call(
        state_kernel,
        out_shape=jax.ShapeDtypeStruct(static.shape, jnp.float32),
        scratch_shapes=[
            pltpu.VMEM((padded, state.shape[1]), jnp.float32),
            pltpu.VMEM((3 * padded, state.shape[1]), jnp.float32),
        ],
    )(state, index, static)


def exchange(low, high, axis):
    size = lax.axis_size(axis)
    up = [(i, i + 1) for i in range(size - 1)]
    down = [(i + 1, i) for i in range(size - 1)]
    from_previous = lax.ppermute(high, axis, up)
    from_next = lax.ppermute(low, axis, down)
    return from_previous, from_next


def shards(
    ocean_velocity,
    wind_stress,
    level_counts,
    floe_position,
    floe_velocity,
    floe_radius,
    floe_mass,
    floe_polygon,
    remap_cells,
    contact_count,
    contact_list,
    move_index,
    move_count,
):
    columns = ("sec", "gy")
    comps, levels_here, rows_here, cols_here = ocean_velocity.shape
    halo = OSTEPS
    position = floe_position[0, 0]
    velocity = floe_velocity[0, 0]
    radius = floe_radius[0, 0]
    mass = floe_mass[0, 0]
    cells = remap_cells[0, 0]
    floes = position.shape[1]
    blocks = floes // 128
    record = jnp.concatenate([position, velocity, radius[None]], axis=0)
    edge = record[:, : GHOST * 128]
    edge_size = edge.size

    fields = jnp.concatenate(
        [
            ocean_velocity.reshape(comps * levels_here, rows_here, cols_here),
            wind_stress,
            level_counts.astype(jnp.float32)[None],
        ],
        axis=0,
    )
    channels = fields.shape[0]
    row_strip = channels * halo * cols_here
    margin = rows_here // 2
    low = jnp.concatenate(
        [fields[:, :halo].reshape(-1), edge.reshape(-1), wind_stress[:, :margin].reshape(-1)]
    )
    high = jnp.concatenate(
        [fields[:, -halo:].reshape(-1), edge.reshape(-1), wind_stress[:, -margin:].reshape(-1)]
    )
    above, below = exchange(low, high, "gx")
    wind_strip = (2, margin, cols_here)
    wind_window = jnp.concatenate(
        [
            above[row_strip + edge_size :].reshape(wind_strip),
            wind_stress,
            below[row_strip + edge_size :].reshape(wind_strip),
        ],
        axis=1,
    )
    extended = jnp.concatenate(
        [
            above[:row_strip].reshape(channels, halo, cols_here),
            fields,
            below[:row_strip].reshape(channels, halo, cols_here),
        ],
        axis=1,
    )
    ghost_column = jnp.stack(
        [
            above[row_strip : row_strip + edge_size].reshape(edge.shape),
            edge,
            below[row_strip : row_strip + edge_size].reshape(edge.shape),
        ]
    )
    ext_rows = rows_here + 2 * halo
    col_strip = channels * ext_rows * halo
    low = jnp.concatenate([extended[:, :, :halo].reshape(-1), ghost_column.reshape(-1)])
    high = jnp.concatenate([extended[:, :, -halo:].reshape(-1), ghost_column.reshape(-1)])
    left, right = exchange(low, high, columns)
    extended = jnp.concatenate(
        [
            left[:col_strip].reshape(channels, ext_rows, halo),
            extended,
            right[:col_strip].reshape(channels, ext_rows, halo),
        ],
        axis=2,
    )
    ghost_left = left[col_strip:].reshape(3, *edge.shape)
    ghost_right = right[col_strip:].reshape(3, *edge.shape)
    beside = [ghost_left, ghost_column, ghost_right]
    ghosts = jnp.stack([beside[p % 3][p // 3] for p in PLACES])

    ext_cols = cols_here + 2 * halo
    counts_ext = extended[-1]
    wet = (jnp.arange(levels_here, dtype=jnp.float32)[:, None, None] < counts_ext[None]).astype(
        jnp.float32
    )
    wind_ext = extended[comps * levels_here : comps * levels_here + 2]
    flow = extended[: comps * levels_here].reshape(comps, levels_here, ext_rows, ext_cols) * wet[None]
    first_row = lax.axis_index("gx") * rows_here - margin
    floe_rows = (cells // cols_here - first_row)[None]
    floe_cols = (cells % cols_here)[None]
    sampled_wind = sample_surface(wind_window, floe_rows, floe_cols)
    leaving = move_index[0, 0]
    capacity = leaving.shape[1]
    valid_slots = jnp.arange(capacity, dtype=jnp.int32)[None, :] < move_count[0, 0][:, None]
    chosen = jnp.where(valid_slots, leaving, -1)
    fixed_records = gather_records(
        jnp.zeros((4, floes), jnp.float32), radius[None], mass[None], floe_polygon[0, 0], chosen
    )
    flow, sampled_wind, fixed_records = lax.optimization_barrier((flow, sampled_wind, fixed_records))
    for substep in range(OSTEPS - 1):
        padded = jnp.pad(flow, ((0, 0), (0, 0), (1, 1), (1, 1)))
        flow = ocean_substep(flow, padded, wet, wind_ext)
    wet_tile = (jnp.arange(levels_here, dtype=jnp.int32)[:, None, None] < level_counts[None]).astype(
        jnp.float32
    )
    flow = ocean_substep(
        flow[:, :, halo : halo + rows_here, halo : halo + cols_here],
        flow[:, :, halo - 1 : halo + rows_here + 1, halo - 1 : halo + cols_here + 1],
        wet_tile,
        wind_stress,
    )

    table = block_table(record, ghosts)
    surface = jnp.stack([flow[0, 0], flow[1, 0]])
    from_above, from_below = exchange(surface[:, :margin], surface[:, -margin:], "gx")
    near = jnp.concatenate([from_above, surface, from_below], axis=1)
    sampled_flow = sample_surface(near, floe_rows, floe_cols)
    lists = contact_list[0, 0]
    count = contact_count[0, 0]
    slots = lists.shape[1]
    sizes = sorted({min(slots, size) for size in (16, 32, slots)})

    def pass_over(size):
        def run(lists, count):
            valid = jnp.arange(size, dtype=jnp.int32) < count
            return contact_batch(table, lists[:, :size], valid, blocks, GHOST)

        return run

    which = sum((count > size).astype(jnp.int32) for size in sizes[:-1])
    contact = lax.switch(which, [pass_over(size) for size in sizes], lists, count)
    contact = contact.transpose(1, 0, 2).reshape(2, floes)
    area = math.pi * radius * radius
    relative = sampled_flow - velocity
    speed = jnp.sqrt(jnp.sum(relative * relative, axis=0, keepdims=True))
    total = contact + area[None] * (WATER_DRAG * speed * relative + AIR_GAIN * sampled_wind)
    new_velocity = velocity + ICE_STEP * total / mass[None]
    new_position = position + ICE_STEP * new_velocity
    floe_next = jnp.concatenate([new_position, new_velocity], axis=0)
    outgoing = gather_state(floe_next, chosen, fixed_records)
    from_above, from_below = exchange(outgoing[0:3], outgoing[5:8], "gx")
    heading_left = jnp.stack([from_below[0], outgoing[3], from_above[0]])
    heading_right = jnp.stack([from_below[2], outgoing[4], from_above[2]])
    from_left, from_right = exchange(heading_left, heading_right, columns)
    arrivals = jnp.stack(
        [
            from_right[0],
            from_below[1],
            from_left[0],
            from_right[1],
            from_left[1],
            from_right[2],
            from_above[1],
            from_left[2],
        ]
    )
    return (flow, floe_next[None, None], arrivals[None, None])


def solution(mesh):
    return jax.shard_map(
        shards,
        mesh=mesh,
        in_specs=(
            P(None, None, "gx", ("sec", "gy")),
            P(None, "gx", ("sec", "gy")),
            P("gx", ("sec", "gy")),
            P("gx", ("sec", "gy"), None, None),
            P("gx", ("sec", "gy"), None, None),
            P("gx", ("sec", "gy"), None),
            P("gx", ("sec", "gy"), None),
            P("gx", ("sec", "gy"), None, None),
            P("gx", ("sec", "gy"), None),
            P("gx", ("sec", "gy")),
            P("gx", ("sec", "gy"), None, None),
            P("gx", ("sec", "gy"), None, None),
            P("gx", ("sec", "gy"), None),
        ),
        out_specs=(
            P(None, None, "gx", ("sec", "gy")),
            P("gx", ("sec", "gy"), None, None),
            P("gx", ("sec", "gy"), None, None, None),
        ),
        check_vma=False,
    )
```

```python
import math

import jax
import jax.numpy as jnp
from jax import lax
from jax.experimental import pallas as pl
from jax.experimental.pallas import tpu as pltpu
from jax.sharding import PartitionSpec as P

OSTEPS = 4
GHOST = 4


SOFTEN = 0.1
STIFFNESS = 0.1
DAMPING = 0.05
VERT_MIX = 0.15
CORIOLIS = 0.1
SURFACE_GAIN = 0.25
WATER_DRAG = 0.1
AIR_GAIN = 0.2
ICE_STEP = 0.5
PLACES = (0, 1, 2, 3, 5, 6, 7, 8)


def with_halo(array, sides, width):
    for axis, dim in sides:
        size, length = (lax.axis_size(axis), array.shape[dim])
        up = [(i, (i + 1) % size) for i in range(size - 1)]
        down = [(j, i) for i, j in up]
        last = lax.slice_in_dim(array, length - width, length, axis=dim)
        leading = lax.slice_in_dim(array, 0, width, axis=dim)
        before = lax.ppermute(last, axis, up)
        after = lax.ppermute(leading, axis, down)
        array = jnp.concatenate([before, array, after], axis=dim)
    return array


def ocean_substep(flow, padded, wet, wind):
    levels_here = flow.shape[1]
    lap = (
        padded[:, :, :-2, 1:-1]
        + padded[:, :, 2:, 1:-1]
        + padded[:, :, 1:-1, :-2]
        + padded[:, :, 1:-1, 2:]
        - 4.0 * flow
    )
    depth = jnp.arange(levels_here, dtype=jnp.float32)
    horizontal = (0.15 - 0.05 * depth / levels_here)[None, :, None, None]
    flux = VERT_MIX * (flow[:, 1:] - flow[:, :-1]) * wet[None, 1:]
    empty = jnp.zeros_like(flow[:, :1])
    vert = jnp.concatenate([flux, empty], axis=1) - jnp.concatenate([empty, flux], axis=1)
    turning = jnp.stack([CORIOLIS * flow[1], -CORIOLIS * flow[0]])
    surface = jnp.concatenate([SURFACE_GAIN * wind[:, None], jnp.zeros_like(flow[:, 1:])], axis=1)
    return (flow + horizontal * lap + vert + turning + surface) * wet[None]


def pair_forces(first, second):
    own = first[:, :, None, :]
    other = second[:, :, :, None]
    delta_x = own[:, 0] - other[:, 0]
    delta_y = own[:, 1] - other[:, 1]
    inverse = lax.rsqrt(delta_x * delta_x + delta_y * delta_y + SOFTEN * SOFTEN)
    distance = (delta_x * delta_x + delta_y * delta_y + SOFTEN * SOFTEN) * inverse
    reach = own[:, 4] + other[:, 4]
    intersection = jnp.maximum(reach - distance, 0.0)
    reduced = own[:, 4] * other[:, 4] / reach
    normal_x = delta_x * inverse
    normal_y = delta_y * inverse
    closing = (own[:, 2] - other[:, 2]) * normal_x + (own[:, 3] - other[:, 3]) * normal_y
    magnitude = intersection * reduced * (STIFFNESS - DAMPING * closing)
    return jnp.stack(
        [jnp.sum(magnitude * normal_x, axis=1), jnp.sum(magnitude * normal_y, axis=1)], axis=1
    )


def block_table(own, ghosts):
    blocks = own.shape[1] // 128
    edge_blocks = ghosts.shape[2] // 128
    mine = own.reshape(5, blocks, 128).transpose(1, 0, 2)
    theirs = (
        ghosts.reshape(8, 5, edge_blocks, 128)
        .transpose(0, 2, 1, 3)
        .reshape(8 * edge_blocks, 5, 128)
    )
    return jnp.concatenate([mine, theirs], axis=0)


def contact_batch(table, lists, valid, blocks, edge_blocks):
    source = lists[1]
    neighbour = source - (source > 4).astype(jnp.int32)
    partner = jnp.where(source == 4, lists[2], blocks + neighbour * edge_blocks + lists[2])
    forces = pair_forces(table[lists[0]], table[partner])
    forces = jnp.where(valid[:, None, None], forces, 0.0)
    onehot = (lists[0][:, None] == jnp.arange(blocks, dtype=jnp.int32)[None, :]).astype(jnp.float32)
    return jnp.einsum("pn,pcf->ncf", onehot, forces, precision=lax.Precision.HIGHEST)


def split_parts(x):
    high = x.astype(jnp.bfloat16).astype(jnp.float32)
    rest = x - high
    middle = rest.astype(jnp.bfloat16).astype(jnp.float32)
    low = (rest - middle).astype(jnp.bfloat16).astype(jnp.float32)
    return high, middle, low


def stacked_select(stack_ref, x, onehot):
    rows = x.shape[0]
    pitch = stack_ref.shape[0] // 3
    for part, value in enumerate(split_parts(x)):
        stack_ref[part * pitch : part * pitch + rows, :] = value
    picked = jnp.dot(
        stack_ref[...].astype(jnp.bfloat16), onehot, preferred_element_type=jnp.float32
    )
    return (picked[0:rows] + picked[pitch : pitch + rows]) + picked[2 * pitch : 2 * pitch + rows]


def sample_kernel(window_ref, rows_ref, cols_ref, out_ref, stack_ref):
    window_rows, window_cols = window_ref.shape[1:]
    floes = rows_ref.shape[1]
    onehot = (
        lax.broadcasted_iota(jnp.int32, (window_rows, floes), 0) == rows_ref[...]
    ).astype(jnp.bfloat16)
    pick = lax.broadcasted_iota(jnp.int32, (window_cols, floes), 0) == cols_ref[...]
    for channel in range(window_ref.shape[0]):
        picked = stacked_select(stack_ref, window_ref[channel].T, onehot)
        out_ref[channel : channel + 1, :] = jnp.sum(
            jnp.where(pick, picked, 0.0), axis=0, keepdims=True
        )


def sample_surface(window, rows, cols):
    return pl.pallas_call(
        sample_kernel,
        out_shape=jax.ShapeDtypeStruct((window.shape[0], rows.shape[1]), jnp.float32),
        scratch_shapes=[pltpu.VMEM((3 * window.shape[2], window.shape[1]), jnp.float32)],
    )(window, rows, cols)


def gather_kernel(state_ref, radius_ref, mass_ref, polygon_ref, index_ref, out_ref, record_ref, stack_ref):
    floes = state_ref.shape[1]
    slots = index_ref.shape[1]
    width = out_ref.shape[1]
    record_ref[...] = jnp.zeros_like(record_ref)
    stack_ref[...] = jnp.zeros_like(stack_ref)
    record_ref[0:4, :] = state_ref[...]
    record_ref[4:5, :] = radius_ref[...]
    record_ref[5:6, :] = mass_ref[...]
    record_ref[6:width, :] = polygon_ref[...]
    record = record_ref[...]
    for way in range(index_ref.shape[0]):
        onehot = (
            lax.broadcasted_iota(jnp.int32, (floes, slots), 0) == index_ref[way : way + 1, :]
        ).astype(jnp.bfloat16)
        out_ref[way] = stacked_select(stack_ref, record, onehot)[0:width]


def gather_records(state, radius, mass, polygon, index):
    width = 6 + polygon.shape[0]
    padded = -(-width // 16) * 16
    return pl.pallas_call(
        gather_kernel,
        out_shape=jax.ShapeDtypeStruct((index.shape[0], width, index.shape[1]), jnp.float32),
        scratch_shapes=[
            pltpu.VMEM((padded, state.shape[1]), jnp.float32),
            pltpu.VMEM((3 * padded, state.shape[1]), jnp.float32),
        ],
    )(state, radius, mass, polygon, index)


def state_kernel(state_ref, index_ref, static_ref, out_ref, record_ref, stack_ref):
    floes = state_ref.shape[1]
    slots = index_ref.shape[1]
    rows = state_ref.shape[0]
    record_ref[...] = jnp.zeros_like(record_ref)
    stack_ref[...] = jnp.zeros_like(stack_ref)
    record_ref[0:rows, :] = state_ref[...]
    record = record_ref[...]
    out_ref[...] = static_ref[...]
    for way in range(index_ref.shape[0]):
        onehot = (
            lax.broadcasted_iota(jnp.int32, (floes, slots), 0) == index_ref[way : way + 1, :]
        ).astype(jnp.bfloat16)
        out_ref[way, 0:rows, :] = stacked_select(stack_ref, record, onehot)[0:rows]


def gather_state(state, index, static):
    padded = -(-state.shape[0] // 8) * 8
    return pl.pallas_call(
        state_kernel,
        out_shape=jax.ShapeDtypeStruct(static.shape, jnp.float32),
        scratch_shapes=[
            pltpu.VMEM((padded, state.shape[1]), jnp.float32),
            pltpu.VMEM((3 * padded, state.shape[1]), jnp.float32),
        ],
    )(state, index, static)


def tail_kernel(
    window_ref, rows_ref, cols_ref, position_ref, velocity_ref, radius_ref, mass_ref, contact_ref,
    wind_ref, index_ref, fixed_ref, next_ref, out_ref, sample_ref, record_ref, stack_ref,
):
    window_rows, window_cols = window_ref.shape[1:]
    floes = rows_ref.shape[1]
    slots = index_ref.shape[1]
    onehot = (
        lax.broadcasted_iota(jnp.int32, (window_rows, floes), 0) == rows_ref[...]
    ).astype(jnp.bfloat16)
    pick = lax.broadcasted_iota(jnp.int32, (window_cols, floes), 0) == cols_ref[...]
    sampled = [
        jnp.sum(
            jnp.where(pick, stacked_select(sample_ref, window_ref[channel].T, onehot), 0.0),
            axis=0,
            keepdims=True,
        )
        for channel in range(2)
    ]
    velocity = velocity_ref[...]
    position = position_ref[...]
    contact = contact_ref[...]
    wind = wind_ref[...]
    radius = radius_ref[...]
    mass = mass_ref[...]
    relative = [sampled[axis] - velocity[axis : axis + 1] for axis in range(2)]
    speed = jnp.sqrt(relative[0] * relative[0] + relative[1] * relative[1])
    area = math.pi * radius * radius
    for axis in range(2):
        total = contact[axis : axis + 1] + area * (
            WATER_DRAG * speed * relative[axis] + AIR_GAIN * wind[axis : axis + 1]
        )
        new_velocity = velocity[axis : axis + 1] + ICE_STEP * total / mass
        next_ref[2 + axis : 3 + axis, :] = new_velocity
        next_ref[axis : axis + 1, :] = position[axis : axis + 1] + ICE_STEP * new_velocity
    rows = next_ref.shape[0]
    record_ref[...] = jnp.zeros_like(record_ref)
    stack_ref[...] = jnp.zeros_like(stack_ref)
    record_ref[0:rows, :] = next_ref[...]
    record = record_ref[...]
    out_ref[...] = fixed_ref[...]
    for way in range(index_ref.shape[0]):
        chosen = (
            lax.broadcasted_iota(jnp.int32, (floes, slots), 0) == index_ref[way : way + 1, :]
        ).astype(jnp.bfloat16)
        out_ref[way, 0:rows, :] = stacked_select(stack_ref, record, chosen)[0:rows]


def sample_update_gather(window, rows, cols, position, velocity, radius, mass, contact, wind, index, fixed):
    floes = rows.shape[1]
    return pl.pallas_call(
        tail_kernel,
        out_shape=(
            jax.ShapeDtypeStruct((4, floes), jnp.float32),
            jax.ShapeDtypeStruct(fixed.shape, jnp.float32),
        ),
        scratch_shapes=[
            pltpu.VMEM((3 * window.shape[2], window.shape[1]), jnp.float32),
            pltpu.VMEM((8, floes), jnp.float32),
            pltpu.VMEM((24, floes), jnp.float32),
        ],
    )(window, rows, cols, position, velocity, radius, mass, contact, wind, index, fixed)


def exchange(low, high, axis):
    size = lax.axis_size(axis)
    up = [(i, i + 1) for i in range(size - 1)]
    down = [(i + 1, i) for i in range(size - 1)]
    from_previous = lax.ppermute(high, axis, up)
    from_next = lax.ppermute(low, axis, down)
    return from_previous, from_next


def shards(
    ocean_velocity,
    wind_stress,
    level_counts,
    floe_position,
    floe_velocity,
    floe_radius,
    floe_mass,
    floe_polygon,
    remap_cells,
    contact_count,
    contact_list,
    move_index,
    move_count,
):
    columns = ("sec", "gy")
    comps, levels_here, rows_here, cols_here = ocean_velocity.shape
    halo = OSTEPS
    position = floe_position[0, 0]
    velocity = floe_velocity[0, 0]
    radius = floe_radius[0, 0]
    mass = floe_mass[0, 0]
    cells = remap_cells[0, 0]
    floes = position.shape[1]
    blocks = floes // 128
    record = jnp.concatenate([position, velocity, radius[None]], axis=0)
    edge = record[:, : GHOST * 128]
    edge_size = edge.size

    fields = jnp.concatenate(
        [
            ocean_velocity.reshape(comps * levels_here, rows_here, cols_here),
            wind_stress,
            level_counts.astype(jnp.float32)[None],
        ],
        axis=0,
    )
    channels = fields.shape[0]
    row_strip = channels * halo * cols_here
    margin = rows_here // 2
    low = jnp.concatenate(
        [fields[:, :halo].reshape(-1), edge.reshape(-1), wind_stress[:, :margin].reshape(-1)]
    )
    high = jnp.concatenate(
        [fields[:, -halo:].reshape(-1), edge.reshape(-1), wind_stress[:, -margin:].reshape(-1)]
    )
    above, below = exchange(low, high, "gx")
    wind_strip = (2, margin, cols_here)
    wind_window = jnp.concatenate(
        [
            above[row_strip + edge_size :].reshape(wind_strip),
            wind_stress,
            below[row_strip + edge_size :].reshape(wind_strip),
        ],
        axis=1,
    )
    extended = jnp.concatenate(
        [
            above[:row_strip].reshape(channels, halo, cols_here),
            fields,
            below[:row_strip].reshape(channels, halo, cols_here),
        ],
        axis=1,
    )
    ghost_column = jnp.stack(
        [
            above[row_strip : row_strip + edge_size].reshape(edge.shape),
            edge,
            below[row_strip : row_strip + edge_size].reshape(edge.shape),
        ]
    )
    ext_rows = rows_here + 2 * halo
    col_strip = channels * ext_rows * halo
    low = jnp.concatenate([extended[:, :, :halo].reshape(-1), ghost_column.reshape(-1)])
    high = jnp.concatenate([extended[:, :, -halo:].reshape(-1), ghost_column.reshape(-1)])
    left, right = exchange(low, high, columns)
    extended = jnp.concatenate(
        [
            left[:col_strip].reshape(channels, ext_rows, halo),
            extended,
            right[:col_strip].reshape(channels, ext_rows, halo),
        ],
        axis=2,
    )
    ghost_left = left[col_strip:].reshape(3, *edge.shape)
    ghost_right = right[col_strip:].reshape(3, *edge.shape)
    beside = [ghost_left, ghost_column, ghost_right]
    ghosts = jnp.stack([beside[p % 3][p // 3] for p in PLACES])

    ext_cols = cols_here + 2 * halo
    counts_ext = extended[-1]
    wet = (jnp.arange(levels_here, dtype=jnp.float32)[:, None, None] < counts_ext[None]).astype(
        jnp.float32
    )
    wind_ext = extended[comps * levels_here : comps * levels_here + 2]
    flow = extended[: comps * levels_here].reshape(comps, levels_here, ext_rows, ext_cols) * wet[None]
    first_row = lax.axis_index("gx") * rows_here - margin
    floe_rows = (cells // cols_here - first_row)[None]
    floe_cols = (cells % cols_here)[None]
    sampled_wind = sample_surface(wind_window, floe_rows, floe_cols)
    leaving = move_index[0, 0]
    capacity = leaving.shape[1]
    valid_slots = jnp.arange(capacity, dtype=jnp.int32)[None, :] < move_count[0, 0][:, None]
    chosen = jnp.where(valid_slots, leaving, -1)
    fixed_records = gather_records(
        jnp.zeros((4, floes), jnp.float32), radius[None], mass[None], floe_polygon[0, 0], chosen
    )
    flow, sampled_wind, fixed_records = lax.optimization_barrier((flow, sampled_wind, fixed_records))
    for substep in range(OSTEPS - 1):
        padded = jnp.pad(flow, ((0, 0), (0, 0), (1, 1), (1, 1)))
        flow = ocean_substep(flow, padded, wet, wind_ext)
    wet_tile = (jnp.arange(levels_here, dtype=jnp.int32)[:, None, None] < level_counts[None]).astype(
        jnp.float32
    )
    flow = ocean_substep(
        flow[:, :, halo : halo + rows_here, halo : halo + cols_here],
        flow[:, :, halo - 1 : halo + rows_here + 1, halo - 1 : halo + cols_here + 1],
        wet_tile,
        wind_stress,
    )

    table = block_table(record, ghosts)
    surface = jnp.stack([flow[0, 0], flow[1, 0]])
    from_above, from_below = exchange(surface[:, :margin], surface[:, -margin:], "gx")
    near = jnp.concatenate([from_above, surface, from_below], axis=1)
    lists = contact_list[0, 0]
    count = contact_count[0, 0]
    slots = lists.shape[1]
    sizes = sorted({min(slots, size) for size in (16, 32, slots)})

    def pass_over(size):
        def run(lists, count):
            valid = jnp.arange(size, dtype=jnp.int32) < count
            return contact_batch(table, lists[:, :size], valid, blocks, GHOST)

        return run

    which = sum((count > size).astype(jnp.int32) for size in sizes[:-1])
    contact = lax.switch(which, [pass_over(size) for size in sizes], lists, count)
    contact = contact.transpose(1, 0, 2).reshape(2, floes)
    floe_next, outgoing = sample_update_gather(
        near, floe_rows, floe_cols, position, velocity, radius[None], mass[None], contact,
        sampled_wind, chosen, fixed_records,
    )
    from_above, from_below = exchange(outgoing[0:3], outgoing[5:8], "gx")
    heading_left = jnp.stack([from_below[0], outgoing[3], from_above[0]])
    heading_right = jnp.stack([from_below[2], outgoing[4], from_above[2]])
    from_left, from_right = exchange(heading_left, heading_right, columns)
    arrivals = jnp.stack(
        [
            from_right[0],
            from_below[1],
            from_left[0],
            from_right[1],
            from_left[1],
            from_right[2],
            from_above[1],
            from_left[2],
        ]
    )
    return (flow, floe_next[None, None], arrivals[None, None])


def solution(mesh):
    return jax.shard_map(
        shards,
        mesh=mesh,
        in_specs=(
            P(None, None, "gx", ("sec", "gy")),
            P(None, "gx", ("sec", "gy")),
            P("gx", ("sec", "gy")),
            P("gx", ("sec", "gy"), None, None),
            P("gx", ("sec", "gy"), None, None),
            P("gx", ("sec", "gy"), None),
            P("gx", ("sec", "gy"), None),
            P("gx", ("sec", "gy"), None, None),
            P("gx", ("sec", "gy"), None),
            P("gx", ("sec", "gy")),
            P("gx", ("sec", "gy"), None, None),
            P("gx", ("sec", "gy"), None, None),
            P("gx", ("sec", "gy"), None),
        ),
        out_specs=(
            P(None, None, "gx", ("sec", "gy")),
            P("gx", ("sec", "gy"), None, None),
            P("gx", ("sec", "gy"), None, None, None),
        ),
        check_vma=False,
    )
```

```python
import math

import jax
import jax.numpy as jnp
from jax import lax
from jax.experimental import pallas as pl
from jax.experimental.pallas import tpu as pltpu
from jax.sharding import PartitionSpec as P

OSTEPS = 4
GHOST = 4


SOFTEN = 0.1
STIFFNESS = 0.1
DAMPING = 0.05
VERT_MIX = 0.15
CORIOLIS = 0.1
SURFACE_GAIN = 0.25
WATER_DRAG = 0.1
AIR_GAIN = 0.2
ICE_STEP = 0.5
PLACES = (0, 1, 2, 3, 5, 6, 7, 8)


def with_halo(array, sides, width):
    for axis, dim in sides:
        size, length = (lax.axis_size(axis), array.shape[dim])
        up = [(i, (i + 1) % size) for i in range(size - 1)]
        down = [(j, i) for i, j in up]
        last = lax.slice_in_dim(array, length - width, length, axis=dim)
        leading = lax.slice_in_dim(array, 0, width, axis=dim)
        before = lax.ppermute(last, axis, up)
        after = lax.ppermute(leading, axis, down)
        array = jnp.concatenate([before, array, after], axis=dim)
    return array


def ocean_substep(flow, padded, wet, wind):
    levels_here = flow.shape[1]
    lap = (
        padded[:, :, :-2, 1:-1]
        + padded[:, :, 2:, 1:-1]
        + padded[:, :, 1:-1, :-2]
        + padded[:, :, 1:-1, 2:]
        - 4.0 * flow
    )
    depth = jnp.arange(levels_here, dtype=jnp.float32)
    horizontal = (0.15 - 0.05 * depth / levels_here)[None, :, None, None]
    flux = VERT_MIX * (flow[:, 1:] - flow[:, :-1]) * wet[None, 1:]
    empty = jnp.zeros_like(flow[:, :1])
    vert = jnp.concatenate([flux, empty], axis=1) - jnp.concatenate([empty, flux], axis=1)
    turning = jnp.stack([CORIOLIS * flow[1], -CORIOLIS * flow[0]])
    surface = jnp.concatenate([SURFACE_GAIN * wind[:, None], jnp.zeros_like(flow[:, 1:])], axis=1)
    return (flow + horizontal * lap + vert + turning + surface) * wet[None]


def pair_forces(first, second):
    own = first[:, :, None, :]
    other = second[:, :, :, None]
    delta_x = own[:, 0] - other[:, 0]
    delta_y = own[:, 1] - other[:, 1]
    inverse = lax.rsqrt(delta_x * delta_x + delta_y * delta_y + SOFTEN * SOFTEN)
    distance = (delta_x * delta_x + delta_y * delta_y + SOFTEN * SOFTEN) * inverse
    reach = own[:, 4] + other[:, 4]
    intersection = jnp.maximum(reach - distance, 0.0)
    reduced = own[:, 4] * other[:, 4] / reach
    normal_x = delta_x * inverse
    normal_y = delta_y * inverse
    closing = (own[:, 2] - other[:, 2]) * normal_x + (own[:, 3] - other[:, 3]) * normal_y
    magnitude = intersection * reduced * (STIFFNESS - DAMPING * closing)
    return jnp.stack(
        [jnp.sum(magnitude * normal_x, axis=1), jnp.sum(magnitude * normal_y, axis=1)], axis=1
    )


def block_table(own, ghosts):
    blocks = own.shape[1] // 128
    edge_blocks = ghosts.shape[2] // 128
    mine = own.reshape(5, blocks, 128).transpose(1, 0, 2)
    theirs = (
        ghosts.reshape(8, 5, edge_blocks, 128)
        .transpose(0, 2, 1, 3)
        .reshape(8 * edge_blocks, 5, 128)
    )
    return jnp.concatenate([mine, theirs], axis=0)


def contact_batch(table, lists, valid, blocks, edge_blocks):
    source = lists[1]
    neighbour = source - (source > 4).astype(jnp.int32)
    partner = jnp.where(source == 4, lists[2], blocks + neighbour * edge_blocks + lists[2])
    forces = pair_forces(table[lists[0]], table[partner])
    forces = jnp.where(valid[:, None, None], forces, 0.0)
    onehot = (lists[0][:, None] == jnp.arange(blocks, dtype=jnp.int32)[None, :]).astype(jnp.float32)
    return jnp.einsum("pn,pcf->ncf", onehot, forces, precision=lax.Precision.HIGHEST)


def split_parts(x):
    high = x.astype(jnp.bfloat16).astype(jnp.float32)
    rest = x - high
    middle = rest.astype(jnp.bfloat16).astype(jnp.float32)
    low = (rest - middle).astype(jnp.bfloat16).astype(jnp.float32)
    return high, middle, low


def stacked_select(stack_ref, x, onehot):
    rows = x.shape[0]
    pitch = stack_ref.shape[0] // 3
    for part, value in enumerate(split_parts(x)):
        stack_ref[part * pitch : part * pitch + rows, :] = value
    picked = jnp.dot(
        stack_ref[...].astype(jnp.bfloat16), onehot, preferred_element_type=jnp.float32
    )
    return (picked[0:rows] + picked[pitch : pitch + rows]) + picked[2 * pitch : 2 * pitch + rows]


def sample_kernel(window_ref, rows_ref, cols_ref, out_ref, stack_ref):
    window_rows, window_cols = window_ref.shape[1:]
    floes = rows_ref.shape[1]
    onehot = (
        lax.broadcasted_iota(jnp.int32, (window_rows, floes), 0) == rows_ref[...]
    ).astype(jnp.bfloat16)
    pick = lax.broadcasted_iota(jnp.int32, (window_cols, floes), 0) == cols_ref[...]
    for channel in range(window_ref.shape[0]):
        picked = stacked_select(stack_ref, window_ref[channel].T, onehot)
        out_ref[channel : channel + 1, :] = jnp.sum(
            jnp.where(pick, picked, 0.0), axis=0, keepdims=True
        )


def sample_surface(window, rows, cols):
    return pl.pallas_call(
        sample_kernel,
        out_shape=jax.ShapeDtypeStruct((window.shape[0], rows.shape[1]), jnp.float32),
        scratch_shapes=[pltpu.VMEM((3 * window.shape[2], window.shape[1]), jnp.float32)],
    )(window, rows, cols)


def gather_kernel(state_ref, radius_ref, mass_ref, polygon_ref, index_ref, out_ref, record_ref, stack_ref):
    floes = state_ref.shape[1]
    slots = index_ref.shape[1]
    width = out_ref.shape[1]
    record_ref[...] = jnp.zeros_like(record_ref)
    stack_ref[...] = jnp.zeros_like(stack_ref)
    record_ref[0:4, :] = state_ref[...]
    record_ref[4:5, :] = radius_ref[...]
    record_ref[5:6, :] = mass_ref[...]
    record_ref[6:width, :] = polygon_ref[...]
    record = record_ref[...]
    for way in range(index_ref.shape[0]):
        onehot = (
            lax.broadcasted_iota(jnp.int32, (floes, slots), 0) == index_ref[way : way + 1, :]
        ).astype(jnp.bfloat16)
        out_ref[way] = stacked_select(stack_ref, record, onehot)[0:width]


def gather_records(state, radius, mass, polygon, index):
    width = 6 + polygon.shape[0]
    padded = -(-width // 16) * 16
    return pl.pallas_call(
        gather_kernel,
        out_shape=jax.ShapeDtypeStruct((index.shape[0], width, index.shape[1]), jnp.float32),
        scratch_shapes=[
            pltpu.VMEM((padded, state.shape[1]), jnp.float32),
            pltpu.VMEM((3 * padded, state.shape[1]), jnp.float32),
        ],
    )(state, radius, mass, polygon, index)


def state_kernel(state_ref, index_ref, static_ref, out_ref, record_ref, stack_ref):
    floes = state_ref.shape[1]
    slots = index_ref.shape[1]
    rows = state_ref.shape[0]
    record_ref[...] = jnp.zeros_like(record_ref)
    stack_ref[...] = jnp.zeros_like(stack_ref)
    record_ref[0:rows, :] = state_ref[...]
    record = record_ref[...]
    out_ref[...] = static_ref[...]
    for way in range(index_ref.shape[0]):
        onehot = (
            lax.broadcasted_iota(jnp.int32, (floes, slots), 0) == index_ref[way : way + 1, :]
        ).astype(jnp.bfloat16)
        out_ref[way, 0:rows, :] = stacked_select(stack_ref, record, onehot)[0:rows]


def gather_state(state, index, static):
    padded = -(-state.shape[0] // 8) * 8
    return pl.pallas_call(
        state_kernel,
        out_shape=jax.ShapeDtypeStruct(static.shape, jnp.float32),
        scratch_shapes=[
            pltpu.VMEM((padded, state.shape[1]), jnp.float32),
            pltpu.VMEM((3 * padded, state.shape[1]), jnp.float32),
        ],
    )(state, index, static)


def tail_kernel(
    window_ref, rows_ref, cols_ref, position_ref, velocity_ref, radius_ref, mass_ref, contact_ref,
    wind_ref, polygon_ref, index_ref, next_ref, out_ref, sample_ref, record_ref, stack_ref,
):
    window_rows, window_cols = window_ref.shape[1:]
    floes = rows_ref.shape[1]
    slots = index_ref.shape[1]
    onehot = (
        lax.broadcasted_iota(jnp.int32, (window_rows, floes), 0) == rows_ref[...]
    ).astype(jnp.bfloat16)
    pick = lax.broadcasted_iota(jnp.int32, (window_cols, floes), 0) == cols_ref[...]
    sampled = [
        jnp.sum(
            jnp.where(pick, stacked_select(sample_ref, window_ref[channel].T, onehot), 0.0),
            axis=0,
            keepdims=True,
        )
        for channel in range(2)
    ]
    velocity = velocity_ref[...]
    position = position_ref[...]
    contact = contact_ref[...]
    wind = wind_ref[...]
    radius = radius_ref[...]
    mass = mass_ref[...]
    relative = [sampled[axis] - velocity[axis : axis + 1] for axis in range(2)]
    speed = jnp.sqrt(relative[0] * relative[0] + relative[1] * relative[1])
    area = math.pi * radius * radius
    for axis in range(2):
        total = contact[axis : axis + 1] + area * (
            WATER_DRAG * speed * relative[axis] + AIR_GAIN * wind[axis : axis + 1]
        )
        new_velocity = velocity[axis : axis + 1] + ICE_STEP * total / mass
        next_ref[2 + axis : 3 + axis, :] = new_velocity
        next_ref[axis : axis + 1, :] = position[axis : axis + 1] + ICE_STEP * new_velocity
    width = out_ref.shape[1]
    record_ref[...] = jnp.zeros_like(record_ref)
    stack_ref[...] = jnp.zeros_like(stack_ref)
    record_ref[0:4, :] = next_ref[...]
    record_ref[4:5, :] = radius
    record_ref[5:6, :] = mass
    record_ref[6:width, :] = polygon_ref[...]
    record = record_ref[...]
    for way in range(index_ref.shape[0]):
        chosen = (
            lax.broadcasted_iota(jnp.int32, (floes, slots), 0) == index_ref[way : way + 1, :]
        ).astype(jnp.bfloat16)
        out_ref[way] = stacked_select(stack_ref, record, chosen)[0:width]


def sample_update_gather(window, rows, cols, position, velocity, radius, mass, contact, wind, polygon, index):
    floes = rows.shape[1]
    width = 6 + polygon.shape[0]
    padded = -(-width // 16) * 16
    return pl.pallas_call(
        tail_kernel,
        out_shape=(
            jax.ShapeDtypeStruct((4, floes), jnp.float32),
            jax.ShapeDtypeStruct((index.shape[0], width, index.shape[1]), jnp.float32),
        ),
        scratch_shapes=[
            pltpu.VMEM((3 * window.shape[2], window.shape[1]), jnp.float32),
            pltpu.VMEM((padded, floes), jnp.float32),
            pltpu.VMEM((3 * padded, floes), jnp.float32),
        ],
    )(window, rows, cols, position, velocity, radius, mass, contact, wind, polygon, index)


def exchange(low, high, axis):
    size = lax.axis_size(axis)
    up = [(i, i + 1) for i in range(size - 1)]
    down = [(i + 1, i) for i in range(size - 1)]
    from_previous = lax.ppermute(high, axis, up)
    from_next = lax.ppermute(low, axis, down)
    return from_previous, from_next


def shards(
    ocean_velocity,
    wind_stress,
    level_counts,
    floe_position,
    floe_velocity,
    floe_radius,
    floe_mass,
    floe_polygon,
    remap_cells,
    contact_count,
    contact_list,
    move_index,
    move_count,
):
    columns = ("sec", "gy")
    comps, levels_here, rows_here, cols_here = ocean_velocity.shape
    halo = OSTEPS
    position = floe_position[0, 0]
    velocity = floe_velocity[0, 0]
    radius = floe_radius[0, 0]
    mass = floe_mass[0, 0]
    cells = remap_cells[0, 0]
    floes = position.shape[1]
    blocks = floes // 128
    record = jnp.concatenate([position, velocity, radius[None]], axis=0)
    edge = record[:, : GHOST * 128]
    edge_size = edge.size

    fields = jnp.concatenate(
        [
            ocean_velocity.reshape(comps * levels_here, rows_here, cols_here),
            wind_stress,
            level_counts.astype(jnp.float32)[None],
        ],
        axis=0,
    )
    channels = fields.shape[0]
    row_strip = channels * halo * cols_here
    margin = rows_here // 2
    low = jnp.concatenate(
        [fields[:, :halo].reshape(-1), edge.reshape(-1), wind_stress[:, :margin].reshape(-1)]
    )
    high = jnp.concatenate(
        [fields[:, -halo:].reshape(-1), edge.reshape(-1), wind_stress[:, -margin:].reshape(-1)]
    )
    above, below = exchange(low, high, "gx")
    wind_strip = (2, margin, cols_here)
    wind_window = jnp.concatenate(
        [
            above[row_strip + edge_size :].reshape(wind_strip),
            wind_stress,
            below[row_strip + edge_size :].reshape(wind_strip),
        ],
        axis=1,
    )
    extended = jnp.concatenate(
        [
            above[:row_strip].reshape(channels, halo, cols_here),
            fields,
            below[:row_strip].reshape(channels, halo, cols_here),
        ],
        axis=1,
    )
    ghost_column = jnp.stack(
        [
            above[row_strip : row_strip + edge_size].reshape(edge.shape),
            edge,
            below[row_strip : row_strip + edge_size].reshape(edge.shape),
        ]
    )
    ext_rows = rows_here + 2 * halo
    col_strip = channels * ext_rows * halo
    low = jnp.concatenate([extended[:, :, :halo].reshape(-1), ghost_column.reshape(-1)])
    high = jnp.concatenate([extended[:, :, -halo:].reshape(-1), ghost_column.reshape(-1)])
    left, right = exchange(low, high, columns)
    extended = jnp.concatenate(
        [
            left[:col_strip].reshape(channels, ext_rows, halo),
            extended,
            right[:col_strip].reshape(channels, ext_rows, halo),
        ],
        axis=2,
    )
    ghost_left = left[col_strip:].reshape(3, *edge.shape)
    ghost_right = right[col_strip:].reshape(3, *edge.shape)
    beside = [ghost_left, ghost_column, ghost_right]
    ghosts = jnp.stack([beside[p % 3][p // 3] for p in PLACES])

    ext_cols = cols_here + 2 * halo
    counts_ext = extended[-1]
    wet = (jnp.arange(levels_here, dtype=jnp.float32)[:, None, None] < counts_ext[None]).astype(
        jnp.float32
    )
    wind_ext = extended[comps * levels_here : comps * levels_here + 2]
    flow = extended[: comps * levels_here].reshape(comps, levels_here, ext_rows, ext_cols) * wet[None]
    first_row = lax.axis_index("gx") * rows_here - margin
    floe_rows = (cells // cols_here - first_row)[None]
    floe_cols = (cells % cols_here)[None]
    sampled_wind = sample_surface(wind_window, floe_rows, floe_cols)
    leaving = move_index[0, 0]
    capacity = leaving.shape[1]
    valid_slots = jnp.arange(capacity, dtype=jnp.int32)[None, :] < move_count[0, 0][:, None]
    chosen = jnp.where(valid_slots, leaving, -1)
    flow, sampled_wind = lax.optimization_barrier((flow, sampled_wind))
    for substep in range(OSTEPS - 1):
        padded = jnp.pad(flow, ((0, 0), (0, 0), (1, 1), (1, 1)))
        flow = ocean_substep(flow, padded, wet, wind_ext)
    wet_tile = (jnp.arange(levels_here, dtype=jnp.int32)[:, None, None] < level_counts[None]).astype(
        jnp.float32
    )
    flow = ocean_substep(
        flow[:, :, halo : halo + rows_here, halo : halo + cols_here],
        flow[:, :, halo - 1 : halo + rows_here + 1, halo - 1 : halo + cols_here + 1],
        wet_tile,
        wind_stress,
    )

    table = block_table(record, ghosts)
    surface = jnp.stack([flow[0, 0], flow[1, 0]])
    from_above, from_below = exchange(surface[:, :margin], surface[:, -margin:], "gx")
    near = jnp.concatenate([from_above, surface, from_below], axis=1)
    lists = contact_list[0, 0]
    count = contact_count[0, 0]
    slots = lists.shape[1]
    sizes = sorted({min(slots, size) for size in (16, 32, slots)})

    def pass_over(size):
        def run(lists, count):
            valid = jnp.arange(size, dtype=jnp.int32) < count
            return contact_batch(table, lists[:, :size], valid, blocks, GHOST)

        return run

    which = sum((count > size).astype(jnp.int32) for size in sizes[:-1])
    contact = lax.switch(which, [pass_over(size) for size in sizes], lists, count)
    contact = contact.transpose(1, 0, 2).reshape(2, floes)
    floe_next, outgoing = sample_update_gather(
        near, floe_rows, floe_cols, position, velocity, radius[None], mass[None], contact,
        sampled_wind, floe_polygon[0, 0], chosen,
    )
    from_above, from_below = exchange(outgoing[0:3], outgoing[5:8], "gx")
    heading_left = jnp.stack([from_below[0], outgoing[3], from_above[0]])
    heading_right = jnp.stack([from_below[2], outgoing[4], from_above[2]])
    from_left, from_right = exchange(heading_left, heading_right, columns)
    arrivals = jnp.stack(
        [
            from_right[0],
            from_below[1],
            from_left[0],
            from_right[1],
            from_left[1],
            from_right[2],
            from_above[1],
            from_left[2],
        ]
    )
    return (flow, floe_next[None, None], arrivals[None, None])


def solution(mesh):
    return jax.shard_map(
        shards,
        mesh=mesh,
        in_specs=(
            P(None, None, "gx", ("sec", "gy")),
            P(None, "gx", ("sec", "gy")),
            P("gx", ("sec", "gy")),
            P("gx", ("sec", "gy"), None, None),
            P("gx", ("sec", "gy"), None, None),
            P("gx", ("sec", "gy"), None),
            P("gx", ("sec", "gy"), None),
            P("gx", ("sec", "gy"), None, None),
            P("gx", ("sec", "gy"), None),
            P("gx", ("sec", "gy")),
            P("gx", ("sec", "gy"), None, None),
            P("gx", ("sec", "gy"), None, None),
            P("gx", ("sec", "gy"), None),
        ),
        out_specs=(
            P(None, None, "gx", ("sec", "gy")),
            P("gx", ("sec", "gy"), None, None),
            P("gx", ("sec", "gy"), None, None, None),
        ),
        check_vma=False,
    )
```

```python
import math

import jax
import jax.numpy as jnp
from jax import lax
from jax.experimental import pallas as pl
from jax.experimental.pallas import tpu as pltpu
from jax.sharding import PartitionSpec as P

OSTEPS = 4
GHOST = 4


SOFTEN = 0.1
STIFFNESS = 0.1
DAMPING = 0.05
VERT_MIX = 0.15
CORIOLIS = 0.1
SURFACE_GAIN = 0.25
WATER_DRAG = 0.1
AIR_GAIN = 0.2
ICE_STEP = 0.5
PLACES = (0, 1, 2, 3, 5, 6, 7, 8)


def with_halo(array, sides, width):
    for axis, dim in sides:
        size, length = (lax.axis_size(axis), array.shape[dim])
        up = [(i, (i + 1) % size) for i in range(size - 1)]
        down = [(j, i) for i, j in up]
        last = lax.slice_in_dim(array, length - width, length, axis=dim)
        leading = lax.slice_in_dim(array, 0, width, axis=dim)
        before = lax.ppermute(last, axis, up)
        after = lax.ppermute(leading, axis, down)
        array = jnp.concatenate([before, array, after], axis=dim)
    return array


def ocean_substep(flow, padded, wet, wind):
    levels_here = flow.shape[1]
    lap = (
        padded[:, :, :-2, 1:-1]
        + padded[:, :, 2:, 1:-1]
        + padded[:, :, 1:-1, :-2]
        + padded[:, :, 1:-1, 2:]
        - 4.0 * flow
    )
    depth = jnp.arange(levels_here, dtype=jnp.float32)
    horizontal = (0.15 - 0.05 * depth / levels_here)[None, :, None, None]
    flux = VERT_MIX * (flow[:, 1:] - flow[:, :-1]) * wet[None, 1:]
    empty = jnp.zeros_like(flow[:, :1])
    vert = jnp.concatenate([flux, empty], axis=1) - jnp.concatenate([empty, flux], axis=1)
    turning = jnp.stack([CORIOLIS * flow[1], -CORIOLIS * flow[0]])
    surface = jnp.concatenate([SURFACE_GAIN * wind[:, None], jnp.zeros_like(flow[:, 1:])], axis=1)
    return (flow + horizontal * lap + vert + turning + surface) * wet[None]


def pair_forces(first, second):
    own = first[:, :, None, :]
    other = second[:, :, :, None]
    delta_x = own[:, 0] - other[:, 0]
    delta_y = own[:, 1] - other[:, 1]
    inverse = lax.rsqrt(delta_x * delta_x + delta_y * delta_y + SOFTEN * SOFTEN)
    distance = (delta_x * delta_x + delta_y * delta_y + SOFTEN * SOFTEN) * inverse
    reach = own[:, 4] + other[:, 4]
    intersection = jnp.maximum(reach - distance, 0.0)
    reduced = own[:, 4] * other[:, 4] / reach
    normal_x = delta_x * inverse
    normal_y = delta_y * inverse
    closing = (own[:, 2] - other[:, 2]) * normal_x + (own[:, 3] - other[:, 3]) * normal_y
    magnitude = intersection * reduced * (STIFFNESS - DAMPING * closing)
    return jnp.stack(
        [jnp.sum(magnitude * normal_x, axis=1), jnp.sum(magnitude * normal_y, axis=1)], axis=1
    )


def block_table(own, ghosts):
    blocks = own.shape[1] // 128
    edge_blocks = ghosts.shape[2] // 128
    mine = own.reshape(5, blocks, 128).transpose(1, 0, 2)
    theirs = (
        ghosts.reshape(8, 5, edge_blocks, 128)
        .transpose(0, 2, 1, 3)
        .reshape(8 * edge_blocks, 5, 128)
    )
    return jnp.concatenate([mine, theirs], axis=0)


def contact_batch(table, lists, valid, blocks, edge_blocks):
    source = lists[1]
    neighbour = source - (source > 4).astype(jnp.int32)
    partner = jnp.where(source == 4, lists[2], blocks + neighbour * edge_blocks + lists[2])
    forces = pair_forces(table[lists[0]], table[partner])
    forces = jnp.where(valid[:, None, None], forces, 0.0)
    onehot = (lists[0][:, None] == jnp.arange(blocks, dtype=jnp.int32)[None, :]).astype(jnp.float32)
    return jnp.einsum("pn,pcf->ncf", onehot, forces, precision=lax.Precision.HIGHEST)


def split_parts(x):
    high = x.astype(jnp.bfloat16).astype(jnp.float32)
    rest = x - high
    middle = rest.astype(jnp.bfloat16).astype(jnp.float32)
    low = (rest - middle).astype(jnp.bfloat16).astype(jnp.float32)
    return high, middle, low


def stacked_select(stack_ref, x, onehot):
    rows = x.shape[0]
    pitch = stack_ref.shape[0] // 3
    for part, value in enumerate(split_parts(x)):
        stack_ref[part * pitch : part * pitch + rows, :] = value
    picked = jnp.dot(
        stack_ref[...].astype(jnp.bfloat16), onehot, preferred_element_type=jnp.float32
    )
    return (picked[0:rows] + picked[pitch : pitch + rows]) + picked[2 * pitch : 2 * pitch + rows]


def sample_kernel(window_ref, rows_ref, cols_ref, out_ref, stack_ref):
    window_rows, window_cols = window_ref.shape[1:]
    floes = rows_ref.shape[1]
    onehot = (
        lax.broadcasted_iota(jnp.int32, (window_rows, floes), 0) == rows_ref[...]
    ).astype(jnp.bfloat16)
    pick = lax.broadcasted_iota(jnp.int32, (window_cols, floes), 0) == cols_ref[...]
    for channel in range(window_ref.shape[0]):
        picked = stacked_select(stack_ref, window_ref[channel].T, onehot)
        out_ref[channel : channel + 1, :] = jnp.sum(
            jnp.where(pick, picked, 0.0), axis=0, keepdims=True
        )


def sample_surface(window, rows, cols):
    return pl.pallas_call(
        sample_kernel,
        out_shape=jax.ShapeDtypeStruct((window.shape[0], rows.shape[1]), jnp.float32),
        scratch_shapes=[pltpu.VMEM((3 * window.shape[2], window.shape[1]), jnp.float32)],
    )(window, rows, cols)


def gather_kernel(state_ref, radius_ref, mass_ref, polygon_ref, index_ref, out_ref, record_ref, stack_ref):
    floes = state_ref.shape[1]
    slots = index_ref.shape[1]
    width = out_ref.shape[1]
    record_ref[...] = jnp.zeros_like(record_ref)
    stack_ref[...] = jnp.zeros_like(stack_ref)
    record_ref[0:4, :] = state_ref[...]
    record_ref[4:5, :] = radius_ref[...]
    record_ref[5:6, :] = mass_ref[...]
    record_ref[6:width, :] = polygon_ref[...]
    record = record_ref[...]
    for way in range(index_ref.shape[0]):
        onehot = (
            lax.broadcasted_iota(jnp.int32, (floes, slots), 0) == index_ref[way : way + 1, :]
        ).astype(jnp.bfloat16)
        out_ref[way] = stacked_select(stack_ref, record, onehot)[0:width]


def gather_records(state, radius, mass, polygon, index):
    width = 6 + polygon.shape[0]
    padded = -(-width // 16) * 16
    return pl.pallas_call(
        gather_kernel,
        out_shape=jax.ShapeDtypeStruct((index.shape[0], width, index.shape[1]), jnp.float32),
        scratch_shapes=[
            pltpu.VMEM((padded, state.shape[1]), jnp.float32),
            pltpu.VMEM((3 * padded, state.shape[1]), jnp.float32),
        ],
    )(state, radius, mass, polygon, index)


def state_kernel(state_ref, index_ref, static_ref, out_ref, record_ref, stack_ref):
    floes = state_ref.shape[1]
    slots = index_ref.shape[1]
    rows = state_ref.shape[0]
    record_ref[...] = jnp.zeros_like(record_ref)
    stack_ref[...] = jnp.zeros_like(stack_ref)
    record_ref[0:rows, :] = state_ref[...]
    record = record_ref[...]
    out_ref[...] = static_ref[...]
    for way in range(index_ref.shape[0]):
        onehot = (
            lax.broadcasted_iota(jnp.int32, (floes, slots), 0) == index_ref[way : way + 1, :]
        ).astype(jnp.bfloat16)
        out_ref[way, 0:rows, :] = stacked_select(stack_ref, record, onehot)[0:rows]


def gather_state(state, index, static):
    padded = -(-state.shape[0] // 8) * 8
    return pl.pallas_call(
        state_kernel,
        out_shape=jax.ShapeDtypeStruct(static.shape, jnp.float32),
        scratch_shapes=[
            pltpu.VMEM((padded, state.shape[1]), jnp.float32),
            pltpu.VMEM((3 * padded, state.shape[1]), jnp.float32),
        ],
    )(state, index, static)


def tail_kernel(
    window_ref, rows_ref, cols_ref, position_ref, velocity_ref, radius_ref, mass_ref, contact_ref,
    wind_ref, polygon_ref, index_ref, next_ref, out_ref, sample_ref, record_ref, stack_ref,
):
    window_rows, window_cols = window_ref.shape[1:]
    floes = rows_ref.shape[1]
    slots = index_ref.shape[1]
    onehot = (
        lax.broadcasted_iota(jnp.int32, (window_rows, floes), 0) == rows_ref[...]
    ).astype(jnp.bfloat16)
    pick = lax.broadcasted_iota(jnp.int32, (window_cols, floes), 0) == cols_ref[...]
    sampled = [
        jnp.sum(
            jnp.where(pick, stacked_select(sample_ref, window_ref[channel].T, onehot), 0.0),
            axis=0,
            keepdims=True,
        )
        for channel in range(2)
    ]
    velocity = velocity_ref[...]
    position = position_ref[...]
    contact = contact_ref[...]
    wind = wind_ref[...]
    radius = radius_ref[...]
    mass = mass_ref[...]
    relative = [sampled[axis] - velocity[axis : axis + 1] for axis in range(2)]
    speed = jnp.sqrt(relative[0] * relative[0] + relative[1] * relative[1])
    area = math.pi * radius * radius
    for axis in range(2):
        total = contact[axis : axis + 1] + area * (
            WATER_DRAG * speed * relative[axis] + AIR_GAIN * wind[axis : axis + 1]
        )
        new_velocity = velocity[axis : axis + 1] + ICE_STEP * total / mass
        next_ref[2 + axis : 3 + axis, :] = new_velocity
        next_ref[axis : axis + 1, :] = position[axis : axis + 1] + ICE_STEP * new_velocity
    width = out_ref.shape[1]
    record_ref[...] = jnp.zeros_like(record_ref)
    stack_ref[...] = jnp.zeros_like(stack_ref)
    record_ref[0:4, :] = next_ref[...]
    record_ref[4:5, :] = radius
    record_ref[5:6, :] = mass
    record_ref[6:width, :] = polygon_ref[...]
    record = record_ref[...]
    for way in range(index_ref.shape[0]):
        chosen = (
            lax.broadcasted_iota(jnp.int32, (floes, slots), 0) == index_ref[way : way + 1, :]
        ).astype(jnp.bfloat16)
        out_ref[way] = stacked_select(stack_ref, record, chosen)[0:width]


def sample_update_gather(window, rows, cols, position, velocity, radius, mass, contact, wind, polygon, index):
    floes = rows.shape[1]
    width = 6 + polygon.shape[0]
    padded = -(-width // 16) * 16
    return pl.pallas_call(
        tail_kernel,
        out_shape=(
            jax.ShapeDtypeStruct((4, floes), jnp.float32),
            jax.ShapeDtypeStruct((index.shape[0], width, index.shape[1]), jnp.float32),
        ),
        scratch_shapes=[
            pltpu.VMEM((3 * window.shape[2], window.shape[1]), jnp.float32),
            pltpu.VMEM((padded, floes), jnp.float32),
            pltpu.VMEM((3 * padded, floes), jnp.float32),
        ],
    )(window, rows, cols, position, velocity, radius, mass, contact, wind, polygon, index)


def exchange(low, high, axis):
    size = lax.axis_size(axis)
    up = [(i, i + 1) for i in range(size - 1)]
    down = [(i + 1, i) for i in range(size - 1)]
    from_previous = lax.ppermute(high, axis, up)
    from_next = lax.ppermute(low, axis, down)
    return from_previous, from_next


def shards(
    ocean_velocity,
    wind_stress,
    level_counts,
    floe_position,
    floe_velocity,
    floe_radius,
    floe_mass,
    floe_polygon,
    remap_cells,
    contact_count,
    contact_list,
    move_index,
    move_count,
):
    columns = ("sec", "gy")
    comps, levels_here, rows_here, cols_here = ocean_velocity.shape
    halo = OSTEPS
    position = floe_position[0, 0]
    velocity = floe_velocity[0, 0]
    radius = floe_radius[0, 0]
    mass = floe_mass[0, 0]
    cells = remap_cells[0, 0]
    floes = position.shape[1]
    blocks = floes // 128
    record = jnp.concatenate([position, velocity, radius[None]], axis=0)
    edge = record[:, : GHOST * 128]
    edge_size = edge.size

    fields = jnp.concatenate(
        [
            ocean_velocity.reshape(comps * levels_here, rows_here, cols_here),
            wind_stress,
            level_counts.astype(jnp.float32)[None],
        ],
        axis=0,
    )
    channels = fields.shape[0]
    row_strip = channels * halo * cols_here
    margin = rows_here // 2
    def strip(rows):
        return jnp.concatenate(
            [
                ocean_velocity[:, :, rows].reshape(-1),
                wind_stress[:, rows].reshape(-1),
                level_counts[rows].astype(jnp.float32).reshape(-1),
            ]
        )

    low = jnp.concatenate(
        [strip(slice(0, halo)), edge.reshape(-1), wind_stress[:, :margin].reshape(-1)]
    )
    high = jnp.concatenate(
        [
            strip(slice(rows_here - halo, rows_here)),
            edge.reshape(-1),
            wind_stress[:, -margin:].reshape(-1),
        ]
    )
    above, below = exchange(low, high, "gx")
    wind_strip = (2, margin, cols_here)
    wind_window = jnp.concatenate(
        [
            above[row_strip + edge_size :].reshape(wind_strip),
            wind_stress,
            below[row_strip + edge_size :].reshape(wind_strip),
        ],
        axis=1,
    )
    extended = jnp.concatenate(
        [
            above[:row_strip].reshape(channels, halo, cols_here),
            fields,
            below[:row_strip].reshape(channels, halo, cols_here),
        ],
        axis=1,
    )
    ghost_column = jnp.stack(
        [
            above[row_strip : row_strip + edge_size].reshape(edge.shape),
            edge,
            below[row_strip : row_strip + edge_size].reshape(edge.shape),
        ]
    )
    ext_rows = rows_here + 2 * halo
    col_strip = channels * ext_rows * halo
    low = jnp.concatenate([extended[:, :, :halo].reshape(-1), ghost_column.reshape(-1)])
    high = jnp.concatenate([extended[:, :, -halo:].reshape(-1), ghost_column.reshape(-1)])
    left, right = exchange(low, high, columns)
    extended = jnp.concatenate(
        [
            left[:col_strip].reshape(channels, ext_rows, halo),
            extended,
            right[:col_strip].reshape(channels, ext_rows, halo),
        ],
        axis=2,
    )
    ghost_left = left[col_strip:].reshape(3, *edge.shape)
    ghost_right = right[col_strip:].reshape(3, *edge.shape)
    beside = [ghost_left, ghost_column, ghost_right]
    ghosts = jnp.stack([beside[p % 3][p // 3] for p in PLACES])

    ext_cols = cols_here + 2 * halo
    counts_ext = extended[-1]
    wet = (jnp.arange(levels_here, dtype=jnp.float32)[:, None, None] < counts_ext[None]).astype(
        jnp.float32
    )
    wind_ext = extended[comps * levels_here : comps * levels_here + 2]
    flow = extended[: comps * levels_here].reshape(comps, levels_here, ext_rows, ext_cols) * wet[None]
    first_row = lax.axis_index("gx") * rows_here - margin
    floe_rows = (cells // cols_here - first_row)[None]
    floe_cols = (cells % cols_here)[None]
    sampled_wind = sample_surface(wind_window, floe_rows, floe_cols)
    leaving = move_index[0, 0]
    capacity = leaving.shape[1]
    valid_slots = jnp.arange(capacity, dtype=jnp.int32)[None, :] < move_count[0, 0][:, None]
    chosen = jnp.where(valid_slots, leaving, -1)
    flow, sampled_wind = lax.optimization_barrier((flow, sampled_wind))
    for substep in range(OSTEPS - 1):
        padded = jnp.pad(flow, ((0, 0), (0, 0), (1, 1), (1, 1)))
        flow = ocean_substep(flow, padded, wet, wind_ext)
    wet_tile = (jnp.arange(levels_here, dtype=jnp.int32)[:, None, None] < level_counts[None]).astype(
        jnp.float32
    )
    flow = ocean_substep(
        flow[:, :, halo : halo + rows_here, halo : halo + cols_here],
        flow[:, :, halo - 1 : halo + rows_here + 1, halo - 1 : halo + cols_here + 1],
        wet_tile,
        wind_stress,
    )

    table = block_table(record, ghosts)
    surface = jnp.stack([flow[0, 0], flow[1, 0]])
    from_above, from_below = exchange(surface[:, :margin], surface[:, -margin:], "gx")
    near = jnp.concatenate([from_above, surface, from_below], axis=1)
    lists = contact_list[0, 0]
    count = contact_count[0, 0]
    slots = lists.shape[1]
    sizes = sorted({min(slots, size) for size in (16, 32, slots)})

    def pass_over(size):
        def run(lists, count):
            valid = jnp.arange(size, dtype=jnp.int32) < count
            return contact_batch(table, lists[:, :size], valid, blocks, GHOST)

        return run

    which = sum((count > size).astype(jnp.int32) for size in sizes[:-1])
    contact = lax.switch(which, [pass_over(size) for size in sizes], lists, count)
    contact = contact.transpose(1, 0, 2).reshape(2, floes)
    floe_next, outgoing = sample_update_gather(
        near, floe_rows, floe_cols, position, velocity, radius[None], mass[None], contact,
        sampled_wind, floe_polygon[0, 0], chosen,
    )
    from_above, from_below = exchange(outgoing[0:3], outgoing[5:8], "gx")
    heading_left = jnp.stack([from_below[0], outgoing[3], from_above[0]])
    heading_right = jnp.stack([from_below[2], outgoing[4], from_above[2]])
    from_left, from_right = exchange(heading_left, heading_right, columns)
    arrivals = jnp.stack(
        [
            from_right[0],
            from_below[1],
            from_left[0],
            from_right[1],
            from_left[1],
            from_right[2],
            from_above[1],
            from_left[2],
        ]
    )
    return (flow, floe_next[None, None], arrivals[None, None])


def solution(mesh):
    return jax.shard_map(
        shards,
        mesh=mesh,
        in_specs=(
            P(None, None, "gx", ("sec", "gy")),
            P(None, "gx", ("sec", "gy")),
            P("gx", ("sec", "gy")),
            P("gx", ("sec", "gy"), None, None),
            P("gx", ("sec", "gy"), None, None),
            P("gx", ("sec", "gy"), None),
            P("gx", ("sec", "gy"), None),
            P("gx", ("sec", "gy"), None, None),
            P("gx", ("sec", "gy"), None),
            P("gx", ("sec", "gy")),
            P("gx", ("sec", "gy"), None, None),
            P("gx", ("sec", "gy"), None, None),
            P("gx", ("sec", "gy"), None),
        ),
        out_specs=(
            P(None, None, "gx", ("sec", "gy")),
            P("gx", ("sec", "gy"), None, None),
            P("gx", ("sec", "gy"), None, None, None),
        ),
        check_vma=False,
    )
```

```python
import math

import jax
import jax.numpy as jnp
from jax import lax
from jax.experimental import pallas as pl
from jax.experimental.pallas import tpu as pltpu
from jax.sharding import PartitionSpec as P

OSTEPS = 4
GHOST = 4


SOFTEN = 0.1
STIFFNESS = 0.1
DAMPING = 0.05
VERT_MIX = 0.15
CORIOLIS = 0.1
SURFACE_GAIN = 0.25
WATER_DRAG = 0.1
AIR_GAIN = 0.2
ICE_STEP = 0.5
PLACES = (0, 1, 2, 3, 5, 6, 7, 8)


def with_halo(array, sides, width):
    for axis, dim in sides:
        size, length = (lax.axis_size(axis), array.shape[dim])
        up = [(i, (i + 1) % size) for i in range(size - 1)]
        down = [(j, i) for i, j in up]
        last = lax.slice_in_dim(array, length - width, length, axis=dim)
        leading = lax.slice_in_dim(array, 0, width, axis=dim)
        before = lax.ppermute(last, axis, up)
        after = lax.ppermute(leading, axis, down)
        array = jnp.concatenate([before, array, after], axis=dim)
    return array


def ocean_substep(flow, padded, wet, wind):
    levels_here = flow.shape[1]
    lap = (
        padded[:, :, :-2, 1:-1]
        + padded[:, :, 2:, 1:-1]
        + padded[:, :, 1:-1, :-2]
        + padded[:, :, 1:-1, 2:]
        - 4.0 * flow
    )
    depth = jnp.arange(levels_here, dtype=jnp.float32)
    horizontal = (0.15 - 0.05 * depth / levels_here)[None, :, None, None]
    flux = VERT_MIX * (flow[:, 1:] - flow[:, :-1]) * wet[None, 1:]
    empty = jnp.zeros_like(flow[:, :1])
    vert = jnp.concatenate([flux, empty], axis=1) - jnp.concatenate([empty, flux], axis=1)
    turning = jnp.stack([CORIOLIS * flow[1], -CORIOLIS * flow[0]])
    surface = jnp.concatenate([SURFACE_GAIN * wind[:, None], jnp.zeros_like(flow[:, 1:])], axis=1)
    return (flow + horizontal * lap + vert + turning + surface) * wet[None]


def pair_forces(first, second):
    own = first[:, :, None, :]
    other = second[:, :, :, None]
    delta_x = own[:, 0] - other[:, 0]
    delta_y = own[:, 1] - other[:, 1]
    inverse = lax.rsqrt(delta_x * delta_x + delta_y * delta_y + SOFTEN * SOFTEN)
    distance = (delta_x * delta_x + delta_y * delta_y + SOFTEN * SOFTEN) * inverse
    reach = own[:, 4] + other[:, 4]
    intersection = jnp.maximum(reach - distance, 0.0)
    reduced = own[:, 4] * other[:, 4] / reach
    normal_x = delta_x * inverse
    normal_y = delta_y * inverse
    closing = (own[:, 2] - other[:, 2]) * normal_x + (own[:, 3] - other[:, 3]) * normal_y
    magnitude = intersection * reduced * (STIFFNESS - DAMPING * closing)
    return jnp.stack(
        [jnp.sum(magnitude * normal_x, axis=1), jnp.sum(magnitude * normal_y, axis=1)], axis=1
    )


def block_table(own, ghosts):
    blocks = own.shape[1] // 128
    edge_blocks = ghosts.shape[2] // 128
    mine = own.reshape(5, blocks, 128).transpose(1, 0, 2)
    theirs = (
        ghosts.reshape(8, 5, edge_blocks, 128)
        .transpose(0, 2, 1, 3)
        .reshape(8 * edge_blocks, 5, 128)
    )
    return jnp.concatenate([mine, theirs], axis=0)


def contact_batch(table, lists, valid, blocks, edge_blocks):
    source = lists[1]
    neighbour = source - (source > 4).astype(jnp.int32)
    partner = jnp.where(source == 4, lists[2], blocks + neighbour * edge_blocks + lists[2])
    forces = pair_forces(table[lists[0]], table[partner])
    forces = jnp.where(valid[:, None, None], forces, 0.0)
    onehot = (lists[0][:, None] == jnp.arange(blocks, dtype=jnp.int32)[None, :]).astype(jnp.float32)
    return jnp.einsum("pn,pcf->ncf", onehot, forces, precision=lax.Precision.HIGHEST)


def split_parts(x):
    high = x.astype(jnp.bfloat16).astype(jnp.float32)
    rest = x - high
    middle = rest.astype(jnp.bfloat16).astype(jnp.float32)
    low = (rest - middle).astype(jnp.bfloat16).astype(jnp.float32)
    return high, middle, low


def stacked_select(stack_ref, x, onehot):
    rows = x.shape[0]
    pitch = stack_ref.shape[0] // 3
    for part, value in enumerate(split_parts(x)):
        stack_ref[part * pitch : part * pitch + rows, :] = value
    picked = jnp.dot(
        stack_ref[...].astype(jnp.bfloat16), onehot, preferred_element_type=jnp.float32
    )
    return (picked[0:rows] + picked[pitch : pitch + rows]) + picked[2 * pitch : 2 * pitch + rows]


def sample_kernel(window_ref, rows_ref, cols_ref, out_ref, stack_ref):
    window_rows, window_cols = window_ref.shape[1:]
    floes = rows_ref.shape[1]
    onehot = (
        lax.broadcasted_iota(jnp.int32, (window_rows, floes), 0) == rows_ref[...]
    ).astype(jnp.bfloat16)
    pick = lax.broadcasted_iota(jnp.int32, (window_cols, floes), 0) == cols_ref[...]
    for channel in range(window_ref.shape[0]):
        picked = stacked_select(stack_ref, window_ref[channel].T, onehot)
        out_ref[channel : channel + 1, :] = jnp.sum(
            jnp.where(pick, picked, 0.0), axis=0, keepdims=True
        )


def sample_surface(window, rows, cols):
    return pl.pallas_call(
        sample_kernel,
        out_shape=jax.ShapeDtypeStruct((window.shape[0], rows.shape[1]), jnp.float32),
        scratch_shapes=[pltpu.VMEM((3 * window.shape[2], window.shape[1]), jnp.float32)],
    )(window, rows, cols)


def gather_kernel(state_ref, radius_ref, mass_ref, polygon_ref, index_ref, out_ref, record_ref, stack_ref):
    floes = state_ref.shape[1]
    slots = index_ref.shape[1]
    width = out_ref.shape[1]
    record_ref[...] = jnp.zeros_like(record_ref)
    stack_ref[...] = jnp.zeros_like(stack_ref)
    record_ref[0:4, :] = state_ref[...]
    record_ref[4:5, :] = radius_ref[...]
    record_ref[5:6, :] = mass_ref[...]
    record_ref[6:width, :] = polygon_ref[...]
    record = record_ref[...]
    for way in range(index_ref.shape[0]):
        onehot = (
            lax.broadcasted_iota(jnp.int32, (floes, slots), 0) == index_ref[way : way + 1, :]
        ).astype(jnp.bfloat16)
        out_ref[way] = stacked_select(stack_ref, record, onehot)[0:width]


def gather_records(state, radius, mass, polygon, index):
    width = 6 + polygon.shape[0]
    padded = -(-width // 16) * 16
    return pl.pallas_call(
        gather_kernel,
        out_shape=jax.ShapeDtypeStruct((index.shape[0], width, index.shape[1]), jnp.float32),
        scratch_shapes=[
            pltpu.VMEM((padded, state.shape[1]), jnp.float32),
            pltpu.VMEM((3 * padded, state.shape[1]), jnp.float32),
        ],
    )(state, radius, mass, polygon, index)


def state_kernel(state_ref, index_ref, static_ref, out_ref, record_ref, stack_ref):
    floes = state_ref.shape[1]
    slots = index_ref.shape[1]
    rows = state_ref.shape[0]
    record_ref[...] = jnp.zeros_like(record_ref)
    stack_ref[...] = jnp.zeros_like(stack_ref)
    record_ref[0:rows, :] = state_ref[...]
    record = record_ref[...]
    out_ref[...] = static_ref[...]
    for way in range(index_ref.shape[0]):
        onehot = (
            lax.broadcasted_iota(jnp.int32, (floes, slots), 0) == index_ref[way : way + 1, :]
        ).astype(jnp.bfloat16)
        out_ref[way, 0:rows, :] = stacked_select(stack_ref, record, onehot)[0:rows]


def gather_state(state, index, static):
    padded = -(-state.shape[0] // 8) * 8
    return pl.pallas_call(
        state_kernel,
        out_shape=jax.ShapeDtypeStruct(static.shape, jnp.float32),
        scratch_shapes=[
            pltpu.VMEM((padded, state.shape[1]), jnp.float32),
            pltpu.VMEM((3 * padded, state.shape[1]), jnp.float32),
        ],
    )(state, index, static)


def tail_kernel(
    window_ref, rows_ref, cols_ref, position_ref, velocity_ref, radius_ref, mass_ref, contact_ref,
    wind_ref, polygon_ref, index_ref, next_ref, out_ref, sample_ref, record_ref, stack_ref,
):
    window_rows, window_cols = window_ref.shape[1:]
    floes = rows_ref.shape[1]
    slots = index_ref.shape[1]
    onehot = (
        lax.broadcasted_iota(jnp.int32, (window_rows, floes), 0) == rows_ref[...]
    ).astype(jnp.bfloat16)
    pick = lax.broadcasted_iota(jnp.int32, (window_cols, floes), 0) == cols_ref[...]
    sampled = [
        jnp.sum(
            jnp.where(pick, stacked_select(sample_ref, window_ref[channel].T, onehot), 0.0),
            axis=0,
            keepdims=True,
        )
        for channel in range(2)
    ]
    velocity = velocity_ref[...]
    position = position_ref[...]
    contact = jnp.concatenate([contact_ref[block] for block in range(contact_ref.shape[0])], axis=1)
    wind = wind_ref[...]
    radius = radius_ref[...]
    mass = mass_ref[...]
    relative = [sampled[axis] - velocity[axis : axis + 1] for axis in range(2)]
    speed = jnp.sqrt(relative[0] * relative[0] + relative[1] * relative[1])
    area = math.pi * radius * radius
    for axis in range(2):
        total = contact[axis : axis + 1] + area * (
            WATER_DRAG * speed * relative[axis] + AIR_GAIN * wind[axis : axis + 1]
        )
        new_velocity = velocity[axis : axis + 1] + ICE_STEP * total / mass
        next_ref[2 + axis : 3 + axis, :] = new_velocity
        next_ref[axis : axis + 1, :] = position[axis : axis + 1] + ICE_STEP * new_velocity
    width = out_ref.shape[1]
    record_ref[...] = jnp.zeros_like(record_ref)
    stack_ref[...] = jnp.zeros_like(stack_ref)
    record_ref[0:4, :] = next_ref[...]
    record_ref[4:5, :] = radius
    record_ref[5:6, :] = mass
    record_ref[6:width, :] = polygon_ref[...]
    record = record_ref[...]
    for way in range(index_ref.shape[0]):
        chosen = (
            lax.broadcasted_iota(jnp.int32, (floes, slots), 0) == index_ref[way : way + 1, :]
        ).astype(jnp.bfloat16)
        out_ref[way] = stacked_select(stack_ref, record, chosen)[0:width]


def sample_update_gather(window, rows, cols, position, velocity, radius, mass, contact, wind, polygon, index):
    floes = rows.shape[1]
    width = 6 + polygon.shape[0]
    padded = -(-width // 16) * 16
    return pl.pallas_call(
        tail_kernel,
        out_shape=(
            jax.ShapeDtypeStruct((4, floes), jnp.float32),
            jax.ShapeDtypeStruct((index.shape[0], width, index.shape[1]), jnp.float32),
        ),
        scratch_shapes=[
            pltpu.VMEM((3 * window.shape[2], window.shape[1]), jnp.float32),
            pltpu.VMEM((padded, floes), jnp.float32),
            pltpu.VMEM((3 * padded, floes), jnp.float32),
        ],
    )(window, rows, cols, position, velocity, radius, mass, contact, wind, polygon, index)


def exchange(low, high, axis):
    size = lax.axis_size(axis)
    up = [(i, i + 1) for i in range(size - 1)]
    down = [(i + 1, i) for i in range(size - 1)]
    from_previous = lax.ppermute(high, axis, up)
    from_next = lax.ppermute(low, axis, down)
    return from_previous, from_next


def shards(
    ocean_velocity,
    wind_stress,
    level_counts,
    floe_position,
    floe_velocity,
    floe_radius,
    floe_mass,
    floe_polygon,
    remap_cells,
    contact_count,
    contact_list,
    move_index,
    move_count,
):
    columns = ("sec", "gy")
    comps, levels_here, rows_here, cols_here = ocean_velocity.shape
    halo = OSTEPS
    position = floe_position[0, 0]
    velocity = floe_velocity[0, 0]
    radius = floe_radius[0, 0]
    mass = floe_mass[0, 0]
    cells = remap_cells[0, 0]
    floes = position.shape[1]
    blocks = floes // 128
    record = jnp.concatenate([position, velocity, radius[None]], axis=0)
    edge = record[:, : GHOST * 128]
    edge_size = edge.size

    fields = jnp.concatenate(
        [
            ocean_velocity.reshape(comps * levels_here, rows_here, cols_here),
            wind_stress,
            level_counts.astype(jnp.float32)[None],
        ],
        axis=0,
    )
    channels = fields.shape[0]
    row_strip = channels * halo * cols_here
    margin = rows_here // 2
    def strip(rows):
        return jnp.concatenate(
            [
                ocean_velocity[:, :, rows].reshape(-1),
                wind_stress[:, rows].reshape(-1),
                level_counts[rows].astype(jnp.float32).reshape(-1),
            ]
        )

    low = jnp.concatenate(
        [strip(slice(0, halo)), edge.reshape(-1), wind_stress[:, :margin].reshape(-1)]
    )
    high = jnp.concatenate(
        [
            strip(slice(rows_here - halo, rows_here)),
            edge.reshape(-1),
            wind_stress[:, -margin:].reshape(-1),
        ]
    )
    above, below = exchange(low, high, "gx")
    wind_strip = (2, margin, cols_here)
    wind_window = jnp.concatenate(
        [
            above[row_strip + edge_size :].reshape(wind_strip),
            wind_stress,
            below[row_strip + edge_size :].reshape(wind_strip),
        ],
        axis=1,
    )
    extended = jnp.concatenate(
        [
            above[:row_strip].reshape(channels, halo, cols_here),
            fields,
            below[:row_strip].reshape(channels, halo, cols_here),
        ],
        axis=1,
    )
    ghost_column = jnp.stack(
        [
            above[row_strip : row_strip + edge_size].reshape(edge.shape),
            edge,
            below[row_strip : row_strip + edge_size].reshape(edge.shape),
        ]
    )
    ext_rows = rows_here + 2 * halo
    col_strip = channels * ext_rows * halo
    low = jnp.concatenate([extended[:, :, :halo].reshape(-1), ghost_column.reshape(-1)])
    high = jnp.concatenate([extended[:, :, -halo:].reshape(-1), ghost_column.reshape(-1)])
    left, right = exchange(low, high, columns)
    extended = jnp.concatenate(
        [
            left[:col_strip].reshape(channels, ext_rows, halo),
            extended,
            right[:col_strip].reshape(channels, ext_rows, halo),
        ],
        axis=2,
    )
    ghost_left = left[col_strip:].reshape(3, *edge.shape)
    ghost_right = right[col_strip:].reshape(3, *edge.shape)
    beside = [ghost_left, ghost_column, ghost_right]
    ghosts = jnp.stack([beside[p % 3][p // 3] for p in PLACES])

    ext_cols = cols_here + 2 * halo
    counts_ext = extended[-1]
    wet = (jnp.arange(levels_here, dtype=jnp.float32)[:, None, None] < counts_ext[None]).astype(
        jnp.float32
    )
    wind_ext = extended[comps * levels_here : comps * levels_here + 2]
    flow = extended[: comps * levels_here].reshape(comps, levels_here, ext_rows, ext_cols) * wet[None]
    first_row = lax.axis_index("gx") * rows_here - margin
    floe_rows = (cells // cols_here - first_row)[None]
    floe_cols = (cells % cols_here)[None]
    sampled_wind = sample_surface(wind_window, floe_rows, floe_cols)
    leaving = move_index[0, 0]
    capacity = leaving.shape[1]
    valid_slots = jnp.arange(capacity, dtype=jnp.int32)[None, :] < move_count[0, 0][:, None]
    chosen = jnp.where(valid_slots, leaving, -1)
    flow, sampled_wind = lax.optimization_barrier((flow, sampled_wind))
    for substep in range(OSTEPS - 1):
        padded = jnp.pad(flow, ((0, 0), (0, 0), (1, 1), (1, 1)))
        flow = ocean_substep(flow, padded, wet, wind_ext)
    wet_tile = (jnp.arange(levels_here, dtype=jnp.int32)[:, None, None] < level_counts[None]).astype(
        jnp.float32
    )
    flow = ocean_substep(
        flow[:, :, halo : halo + rows_here, halo : halo + cols_here],
        flow[:, :, halo - 1 : halo + rows_here + 1, halo - 1 : halo + cols_here + 1],
        wet_tile,
        wind_stress,
    )

    table = block_table(record, ghosts)
    surface = jnp.stack([flow[0, 0], flow[1, 0]])
    from_above, from_below = exchange(surface[:, :margin], surface[:, -margin:], "gx")
    near = jnp.concatenate([from_above, surface, from_below], axis=1)
    lists = contact_list[0, 0]
    count = contact_count[0, 0]
    slots = lists.shape[1]
    sizes = sorted({min(slots, size) for size in (16, 32, slots)})

    def pass_over(size):
        def run(lists, count):
            valid = jnp.arange(size, dtype=jnp.int32) < count
            return contact_batch(table, lists[:, :size], valid, blocks, GHOST)

        return run

    which = sum((count > size).astype(jnp.int32) for size in sizes[:-1])
    contact = lax.switch(which, [pass_over(size) for size in sizes], lists, count)
    floe_next, outgoing = sample_update_gather(
        near, floe_rows, floe_cols, position, velocity, radius[None], mass[None], contact,
        sampled_wind, floe_polygon[0, 0], chosen,
    )
    from_above, from_below = exchange(outgoing[0:3], outgoing[5:8], "gx")
    heading_left = jnp.stack([from_below[0], outgoing[3], from_above[0]])
    heading_right = jnp.stack([from_below[2], outgoing[4], from_above[2]])
    from_left, from_right = exchange(heading_left, heading_right, columns)
    arrivals = jnp.stack(
        [
            from_right[0],
            from_below[1],
            from_left[0],
            from_right[1],
            from_left[1],
            from_right[2],
            from_above[1],
            from_left[2],
        ]
    )
    return (flow, floe_next[None, None], arrivals[None, None])


def solution(mesh):
    return jax.shard_map(
        shards,
        mesh=mesh,
        in_specs=(
            P(None, None, "gx", ("sec", "gy")),
            P(None, "gx", ("sec", "gy")),
            P("gx", ("sec", "gy")),
            P("gx", ("sec", "gy"), None, None),
            P("gx", ("sec", "gy"), None, None),
            P("gx", ("sec", "gy"), None),
            P("gx", ("sec", "gy"), None),
            P("gx", ("sec", "gy"), None, None),
            P("gx", ("sec", "gy"), None),
            P("gx", ("sec", "gy")),
            P("gx", ("sec", "gy"), None, None),
            P("gx", ("sec", "gy"), None, None),
            P("gx", ("sec", "gy"), None),
        ),
        out_specs=(
            P(None, None, "gx", ("sec", "gy")),
            P("gx", ("sec", "gy"), None, None),
            P("gx", ("sec", "gy"), None, None, None),
        ),
        check_vma=False,
    )
```

```python
import math

import jax
import jax.numpy as jnp
from jax import lax
from jax.experimental import pallas as pl
from jax.experimental.pallas import tpu as pltpu
from jax.sharding import PartitionSpec as P

OSTEPS = 4
GHOST = 4


SOFTEN = 0.1
STIFFNESS = 0.1
DAMPING = 0.05
VERT_MIX = 0.15
CORIOLIS = 0.1
SURFACE_GAIN = 0.25
WATER_DRAG = 0.1
AIR_GAIN = 0.2
ICE_STEP = 0.5
PLACES = (0, 1, 2, 3, 5, 6, 7, 8)


def with_halo(array, sides, width):
    for axis, dim in sides:
        size, length = (lax.axis_size(axis), array.shape[dim])
        up = [(i, (i + 1) % size) for i in range(size - 1)]
        down = [(j, i) for i, j in up]
        last = lax.slice_in_dim(array, length - width, length, axis=dim)
        leading = lax.slice_in_dim(array, 0, width, axis=dim)
        before = lax.ppermute(last, axis, up)
        after = lax.ppermute(leading, axis, down)
        array = jnp.concatenate([before, array, after], axis=dim)
    return array


def ocean_substep(flow, padded, wet, wind):
    levels_here = flow.shape[1]
    lap = (
        padded[:, :, :-2, 1:-1]
        + padded[:, :, 2:, 1:-1]
        + padded[:, :, 1:-1, :-2]
        + padded[:, :, 1:-1, 2:]
        - 4.0 * flow
    )
    depth = jnp.arange(levels_here, dtype=jnp.float32)
    horizontal = (0.15 - 0.05 * depth / levels_here)[None, :, None, None]
    flux = VERT_MIX * (flow[:, 1:] - flow[:, :-1]) * wet[None, 1:]
    empty = jnp.zeros_like(flow[:, :1])
    vert = jnp.concatenate([flux, empty], axis=1) - jnp.concatenate([empty, flux], axis=1)
    turning = jnp.stack([CORIOLIS * flow[1], -CORIOLIS * flow[0]])
    surface = jnp.concatenate([SURFACE_GAIN * wind[:, None], jnp.zeros_like(flow[:, 1:])], axis=1)
    return (flow + horizontal * lap + vert + turning + surface) * wet[None]


def pair_forces(first, second):
    own = first[:, :, None, :]
    other = second[:, :, :, None]
    delta_x = own[:, 0] - other[:, 0]
    delta_y = own[:, 1] - other[:, 1]
    inverse = lax.rsqrt(delta_x * delta_x + delta_y * delta_y + SOFTEN * SOFTEN)
    distance = (delta_x * delta_x + delta_y * delta_y + SOFTEN * SOFTEN) * inverse
    reach = own[:, 4] + other[:, 4]
    intersection = jnp.maximum(reach - distance, 0.0)
    reduced = own[:, 4] * other[:, 4] / reach
    normal_x = delta_x * inverse
    normal_y = delta_y * inverse
    closing = (own[:, 2] - other[:, 2]) * normal_x + (own[:, 3] - other[:, 3]) * normal_y
    magnitude = intersection * reduced * (STIFFNESS - DAMPING * closing)
    return jnp.stack(
        [jnp.sum(magnitude * normal_x, axis=1), jnp.sum(magnitude * normal_y, axis=1)], axis=1
    )


def block_table(own, ghosts):
    blocks = own.shape[1] // 128
    edge_blocks = ghosts.shape[2] // 128
    mine = own.reshape(5, blocks, 128).transpose(1, 0, 2)
    theirs = (
        ghosts.reshape(8, 5, edge_blocks, 128)
        .transpose(0, 2, 1, 3)
        .reshape(8 * edge_blocks, 5, 128)
    )
    return jnp.concatenate([mine, theirs], axis=0)


def contact_batch(table, lists, valid, blocks, edge_blocks):
    source = lists[1]
    neighbour = source - (source > 4).astype(jnp.int32)
    partner = jnp.where(source == 4, lists[2], blocks + neighbour * edge_blocks + lists[2])
    forces = pair_forces(table[lists[0]], table[partner])
    forces = jnp.where(valid[:, None, None], forces, 0.0)
    onehot = (lists[0][:, None] == jnp.arange(blocks, dtype=jnp.int32)[None, :]).astype(jnp.float32)
    return jnp.einsum("pn,pcf->ncf", onehot, forces, precision=lax.Precision.HIGHEST)


def split_parts(x):
    high = x.astype(jnp.bfloat16).astype(jnp.float32)
    rest = x - high
    middle = rest.astype(jnp.bfloat16).astype(jnp.float32)
    low = (rest - middle).astype(jnp.bfloat16).astype(jnp.float32)
    return high, middle, low


def stacked_select(stack_ref, x, onehot):
    rows = x.shape[0]
    pitch = stack_ref.shape[0] // 3
    for part, value in enumerate(split_parts(x)):
        stack_ref[part * pitch : part * pitch + rows, :] = value
    picked = jnp.dot(
        stack_ref[...].astype(jnp.bfloat16), onehot, preferred_element_type=jnp.float32
    )
    return (picked[0:rows] + picked[pitch : pitch + rows]) + picked[2 * pitch : 2 * pitch + rows]


def sample_kernel(window_ref, rows_ref, cols_ref, out_ref, stack_ref):
    window_rows, window_cols = window_ref.shape[1:]
    floes = rows_ref.shape[1]
    onehot = (
        lax.broadcasted_iota(jnp.int32, (window_rows, floes), 0) == rows_ref[...]
    ).astype(jnp.bfloat16)
    pick = lax.broadcasted_iota(jnp.int32, (window_cols, floes), 0) == cols_ref[...]
    for channel in range(window_ref.shape[0]):
        picked = stacked_select(stack_ref, window_ref[channel].T, onehot)
        out_ref[channel : channel + 1, :] = jnp.sum(
            jnp.where(pick, picked, 0.0), axis=0, keepdims=True
        )


def sample_surface(window, rows, cols):
    return pl.pallas_call(
        sample_kernel,
        out_shape=jax.ShapeDtypeStruct((window.shape[0], rows.shape[1]), jnp.float32),
        scratch_shapes=[pltpu.VMEM((3 * window.shape[2], window.shape[1]), jnp.float32)],
    )(window, rows, cols)


def gather_kernel(state_ref, radius_ref, mass_ref, polygon_ref, index_ref, out_ref, record_ref, stack_ref):
    floes = state_ref.shape[1]
    slots = index_ref.shape[1]
    width = out_ref.shape[1]
    record_ref[...] = jnp.zeros_like(record_ref)
    stack_ref[...] = jnp.zeros_like(stack_ref)
    record_ref[0:4, :] = state_ref[...]
    record_ref[4:5, :] = radius_ref[...]
    record_ref[5:6, :] = mass_ref[...]
    record_ref[6:width, :] = polygon_ref[...]
    record = record_ref[...]
    for way in range(index_ref.shape[0]):
        onehot = (
            lax.broadcasted_iota(jnp.int32, (floes, slots), 0) == index_ref[way : way + 1, :]
        ).astype(jnp.bfloat16)
        out_ref[way] = stacked_select(stack_ref, record, onehot)[0:width]


def gather_records(state, radius, mass, polygon, index):
    width = 6 + polygon.shape[0]
    padded = -(-width // 16) * 16
    return pl.pallas_call(
        gather_kernel,
        out_shape=jax.ShapeDtypeStruct((index.shape[0], width, index.shape[1]), jnp.float32),
        scratch_shapes=[
            pltpu.VMEM((padded, state.shape[1]), jnp.float32),
            pltpu.VMEM((3 * padded, state.shape[1]), jnp.float32),
        ],
    )(state, radius, mass, polygon, index)


def state_kernel(state_ref, index_ref, static_ref, out_ref, record_ref, stack_ref):
    floes = state_ref.shape[1]
    slots = index_ref.shape[1]
    rows = state_ref.shape[0]
    record_ref[...] = jnp.zeros_like(record_ref)
    stack_ref[...] = jnp.zeros_like(stack_ref)
    record_ref[0:rows, :] = state_ref[...]
    record = record_ref[...]
    out_ref[...] = static_ref[...]
    for way in range(index_ref.shape[0]):
        onehot = (
            lax.broadcasted_iota(jnp.int32, (floes, slots), 0) == index_ref[way : way + 1, :]
        ).astype(jnp.bfloat16)
        out_ref[way, 0:rows, :] = stacked_select(stack_ref, record, onehot)[0:rows]


def gather_state(state, index, static):
    padded = -(-state.shape[0] // 8) * 8
    return pl.pallas_call(
        state_kernel,
        out_shape=jax.ShapeDtypeStruct(static.shape, jnp.float32),
        scratch_shapes=[
            pltpu.VMEM((padded, state.shape[1]), jnp.float32),
            pltpu.VMEM((3 * padded, state.shape[1]), jnp.float32),
        ],
    )(state, index, static)


def tail_kernel(
    window_ref, rows_ref, cols_ref, position_ref, velocity_ref, radius_ref, mass_ref, contact_ref,
    wind_ref, polygon_ref, index_ref, next_ref, out_ref, sample_ref, record_ref, stack_ref,
):
    window_rows, window_cols = window_ref.shape[1:]
    floes = rows_ref.shape[1]
    slots = index_ref.shape[1]
    onehot = (
        lax.broadcasted_iota(jnp.int32, (window_rows, floes), 0) == rows_ref[...]
    ).astype(jnp.bfloat16)
    pick = lax.broadcasted_iota(jnp.int32, (window_cols, floes), 0) == cols_ref[...]
    sampled = [
        jnp.sum(
            jnp.where(pick, stacked_select(sample_ref, window_ref[channel].T, onehot), 0.0),
            axis=0,
            keepdims=True,
        )
        for channel in range(2)
    ]
    velocity = velocity_ref[...]
    position = position_ref[...]
    contact = contact_ref[...]
    wind = wind_ref[...]
    radius = radius_ref[...]
    mass = mass_ref[...]
    relative = [sampled[axis] - velocity[axis : axis + 1] for axis in range(2)]
    speed = jnp.sqrt(relative[0] * relative[0] + relative[1] * relative[1])
    area = math.pi * radius * radius
    for axis in range(2):
        total = contact[axis : axis + 1] + area * (
            WATER_DRAG * speed * relative[axis] + AIR_GAIN * wind[axis : axis + 1]
        )
        new_velocity = velocity[axis : axis + 1] + ICE_STEP * total / mass
        next_ref[2 + axis : 3 + axis, :] = new_velocity
        next_ref[axis : axis + 1, :] = position[axis : axis + 1] + ICE_STEP * new_velocity
    width = out_ref.shape[1]
    record_ref[width:, :] = jnp.zeros((record_ref.shape[0] - width, floes), jnp.float32)
    record_ref[0:4, :] = next_ref[...]
    record_ref[4:5, :] = radius
    record_ref[5:6, :] = mass
    record_ref[6:width, :] = polygon_ref[...]
    record = record_ref[...]
    for way in range(index_ref.shape[0]):
        chosen = (
            lax.broadcasted_iota(jnp.int32, (floes, slots), 0) == index_ref[way : way + 1, :]
        ).astype(jnp.bfloat16)
        out_ref[way] = stacked_select(stack_ref, record, chosen)[0:width]


def sample_update_gather(window, rows, cols, position, velocity, radius, mass, contact, wind, polygon, index):
    floes = rows.shape[1]
    width = 6 + polygon.shape[0]
    padded = -(-width // 16) * 16
    return pl.pallas_call(
        tail_kernel,
        out_shape=(
            jax.ShapeDtypeStruct((4, floes), jnp.float32),
            jax.ShapeDtypeStruct((index.shape[0], width, index.shape[1]), jnp.float32),
        ),
        scratch_shapes=[
            pltpu.VMEM((3 * window.shape[2], window.shape[1]), jnp.float32),
            pltpu.VMEM((padded, floes), jnp.float32),
            pltpu.VMEM((3 * padded, floes), jnp.float32),
        ],
    )(window, rows, cols, position, velocity, radius, mass, contact, wind, polygon, index)


def exchange(low, high, axis):
    size = lax.axis_size(axis)
    up = [(i, i + 1) for i in range(size - 1)]
    down = [(i + 1, i) for i in range(size - 1)]
    from_previous = lax.ppermute(high, axis, up)
    from_next = lax.ppermute(low, axis, down)
    return from_previous, from_next


def shards(
    ocean_velocity,
    wind_stress,
    level_counts,
    floe_position,
    floe_velocity,
    floe_radius,
    floe_mass,
    floe_polygon,
    remap_cells,
    contact_count,
    contact_list,
    move_index,
    move_count,
):
    columns = ("sec", "gy")
    comps, levels_here, rows_here, cols_here = ocean_velocity.shape
    halo = OSTEPS
    position = floe_position[0, 0]
    velocity = floe_velocity[0, 0]
    radius = floe_radius[0, 0]
    mass = floe_mass[0, 0]
    cells = remap_cells[0, 0]
    floes = position.shape[1]
    blocks = floes // 128
    record = jnp.concatenate([position, velocity, radius[None]], axis=0)
    edge = record[:, : GHOST * 128]
    edge_size = edge.size

    fields = jnp.concatenate(
        [
            ocean_velocity.reshape(comps * levels_here, rows_here, cols_here),
            wind_stress,
            level_counts.astype(jnp.float32)[None],
        ],
        axis=0,
    )
    channels = fields.shape[0]
    row_strip = channels * halo * cols_here
    margin = rows_here // 2
    def strip(rows):
        return jnp.concatenate(
            [
                ocean_velocity[:, :, rows].reshape(-1),
                wind_stress[:, rows].reshape(-1),
                level_counts[rows].astype(jnp.float32).reshape(-1),
            ]
        )

    low = jnp.concatenate(
        [strip(slice(0, halo)), edge.reshape(-1), wind_stress[:, :margin].reshape(-1)]
    )
    high = jnp.concatenate(
        [
            strip(slice(rows_here - halo, rows_here)),
            edge.reshape(-1),
            wind_stress[:, -margin:].reshape(-1),
        ]
    )
    above, below = exchange(low, high, "gx")
    wind_strip = (2, margin, cols_here)
    wind_window = jnp.concatenate(
        [
            above[row_strip + edge_size :].reshape(wind_strip),
            wind_stress,
            below[row_strip + edge_size :].reshape(wind_strip),
        ],
        axis=1,
    )
    extended = jnp.concatenate(
        [
            above[:row_strip].reshape(channels, halo, cols_here),
            fields,
            below[:row_strip].reshape(channels, halo, cols_here),
        ],
        axis=1,
    )
    ghost_column = jnp.stack(
        [
            above[row_strip : row_strip + edge_size].reshape(edge.shape),
            edge,
            below[row_strip : row_strip + edge_size].reshape(edge.shape),
        ]
    )
    ext_rows = rows_here + 2 * halo
    col_strip = channels * ext_rows * halo
    low = jnp.concatenate([extended[:, :, :halo].reshape(-1), ghost_column.reshape(-1)])
    high = jnp.concatenate([extended[:, :, -halo:].reshape(-1), ghost_column.reshape(-1)])
    left, right = exchange(low, high, columns)
    extended = jnp.concatenate(
        [
            left[:col_strip].reshape(channels, ext_rows, halo),
            extended,
            right[:col_strip].reshape(channels, ext_rows, halo),
        ],
        axis=2,
    )
    ghost_left = left[col_strip:].reshape(3, *edge.shape)
    ghost_right = right[col_strip:].reshape(3, *edge.shape)
    beside = [ghost_left, ghost_column, ghost_right]
    ghosts = jnp.stack([beside[p % 3][p // 3] for p in PLACES])

    ext_cols = cols_here + 2 * halo
    counts_ext = extended[-1]
    wet = (jnp.arange(levels_here, dtype=jnp.float32)[:, None, None] < counts_ext[None]).astype(
        jnp.float32
    )
    wind_ext = extended[comps * levels_here : comps * levels_here + 2]
    flow = extended[: comps * levels_here].reshape(comps, levels_here, ext_rows, ext_cols) * wet[None]
    first_row = lax.axis_index("gx") * rows_here - margin
    floe_rows = (cells // cols_here - first_row)[None]
    floe_cols = (cells % cols_here)[None]
    sampled_wind = sample_surface(wind_window, floe_rows, floe_cols)
    leaving = move_index[0, 0]
    capacity = leaving.shape[1]
    valid_slots = jnp.arange(capacity, dtype=jnp.int32)[None, :] < move_count[0, 0][:, None]
    chosen = jnp.where(valid_slots, leaving, -1)
    flow, sampled_wind = lax.optimization_barrier((flow, sampled_wind))
    for substep in range(OSTEPS - 1):
        padded = jnp.pad(flow, ((0, 0), (0, 0), (1, 1), (1, 1)))
        flow = ocean_substep(flow, padded, wet, wind_ext)
    wet_tile = (jnp.arange(levels_here, dtype=jnp.int32)[:, None, None] < level_counts[None]).astype(
        jnp.float32
    )
    flow = ocean_substep(
        flow[:, :, halo : halo + rows_here, halo : halo + cols_here],
        flow[:, :, halo - 1 : halo + rows_here + 1, halo - 1 : halo + cols_here + 1],
        wet_tile,
        wind_stress,
    )

    table = block_table(record, ghosts)
    surface = jnp.stack([flow[0, 0], flow[1, 0]])
    from_above, from_below = exchange(surface[:, :margin], surface[:, -margin:], "gx")
    near = jnp.concatenate([from_above, surface, from_below], axis=1)
    lists = contact_list[0, 0]
    count = contact_count[0, 0]
    slots = lists.shape[1]
    sizes = sorted({min(slots, size) for size in (16, 32, slots)})

    def pass_over(size):
        def run(lists, count):
            valid = jnp.arange(size, dtype=jnp.int32) < count
            return contact_batch(table, lists[:, :size], valid, blocks, GHOST)

        return run

    which = sum((count > size).astype(jnp.int32) for size in sizes[:-1])
    contact = lax.switch(which, [pass_over(size) for size in sizes], lists, count)
    contact = contact.transpose(1, 0, 2).reshape(2, floes)
    floe_next, outgoing = sample_update_gather(
        near, floe_rows, floe_cols, position, velocity, radius[None], mass[None], contact,
        sampled_wind, floe_polygon[0, 0], chosen,
    )
    from_above, from_below = exchange(outgoing[0:3], outgoing[5:8], "gx")
    heading_left = jnp.stack([from_below[0], outgoing[3], from_above[0]])
    heading_right = jnp.stack([from_below[2], outgoing[4], from_above[2]])
    from_left, from_right = exchange(heading_left, heading_right, columns)
    arrivals = jnp.stack(
        [
            from_right[0],
            from_below[1],
            from_left[0],
            from_right[1],
            from_left[1],
            from_right[2],
            from_above[1],
            from_left[2],
        ]
    )
    return (flow, floe_next[None, None], arrivals[None, None])


def solution(mesh):
    return jax.shard_map(
        shards,
        mesh=mesh,
        in_specs=(
            P(None, None, "gx", ("sec", "gy")),
            P(None, "gx", ("sec", "gy")),
            P("gx", ("sec", "gy")),
            P("gx", ("sec", "gy"), None, None),
            P("gx", ("sec", "gy"), None, None),
            P("gx", ("sec", "gy"), None),
            P("gx", ("sec", "gy"), None),
            P("gx", ("sec", "gy"), None, None),
            P("gx", ("sec", "gy"), None),
            P("gx", ("sec", "gy")),
            P("gx", ("sec", "gy"), None, None),
            P("gx", ("sec", "gy"), None, None),
            P("gx", ("sec", "gy"), None),
        ),
        out_specs=(
            P(None, None, "gx", ("sec", "gy")),
            P("gx", ("sec", "gy"), None, None),
            P("gx", ("sec", "gy"), None, None, None),
        ),
        check_vma=False,
    )
```
